32 devices in a mesh: lon: 8 (over y, x, core), lat: 4 (over z).
Axes of the slice: x: 2, y: 2, z: 4, core: 2. Of those that a mesh axis runs over, the one named last changes fastest.
Arguments:
- obs_rows: bfloat16 [131072, 128], P(('lon', 'lat')), may hold values from -6 to 6
- cell_ids: int32 [131072], P(('lon', 'lat')), may hold values from 0 to 511
- counts: int32 [32, 32], P(('lon', 'lat')), may hold values from 16 to 128, as said below
- w_embed: bfloat16 [128, 256], replicated, may hold values from -0.5 to 0.5
- w_density: bfloat16 [256], replicated, may hold values from -3 to 3
- kernels: bfloat16 [3, 3, 3, 256, 256], replicated, may hold values from -0.125 to 0.125
- cotangent: bfloat16 [64, 256, 256], P('lat', 'lon'), may hold values from -6 to 6
Outputs:
- encoded: bfloat16 [64, 256, 256], P('lat', 'lon')
- grad_kernels: bfloat16 [3, 3, 3, 256, 256], replicated
- grad_embed: bfloat16 [128, 256], replicated
- grad_obs: bfloat16 [131072, 128], P(('lon', 'lat'))
The draws below stay inside these ranges and needn't reach their ends.
Inputs may be any that keep to these rules, and one draw needn't show every extreme that they name: `counts`: the live rows of each slot are its first ones; in every draw some tile owner receives 128 live rows from every device.
All inputs are finite; a program needn't handle non-finite values.
Results may differ from the reference program's by a relative error of at most 0.011.
Values may be sent and summed in bfloat16 or wider, within the bound.
No kernel may reach another device: no remote copies, remote signals or barrier semaphores. Data moves between devices by JAX's collectives and lax.ppermute only.
A program may use at most 128 MiB of HBM per device.

```python
import math
import jax
import jax.numpy as jnp
from jax import lax

FIN = 128
D = 256
LAYERS = 3
H = 16
W = 32
SLOT = 128
NLAT = 64
NLON = 256
OBS_ALL = 131072
N_LON = 8
N_LAT = 4
DEVICES = 32


def draw_counts(key, part):
    key_hot = jax.random.fold_in(key, 11)
    key_pick = jax.random.fold_in(key, 12)
    key_cold = jax.random.fold_in(key, 13)
    hot_mask = jax.random.randint(key_hot, (DEVICES,), 0, 8) == 0
    forced = jax.random.randint(key_pick, (), 0, DEVICES)
    hot_mask = hot_mask | (jnp.arange(DEVICES) == forced)
    cold_counts = jax.random.randint(key_cold, (DEVICES, DEVICES), SLOT // 8, 3 * SLOT // 4 + 1)
    return jnp.where(hot_mask[None, :], SLOT, cold_counts).astype(jnp.int32)


def plant(entries, own_key, low, largest):
    longest = entries.shape.index(max(entries.shape))
    spots = []
    for shift in (0, 1):
        where = [jax.random.randint(jax.random.fold_in(own_key, axis), (), 0, length) for axis, length in enumerate(entries.shape)]
        where[longest] = (where[longest] + shift) % entries.shape[longest]
        spots.append(tuple(where))
    return entries.at[spots[0]].set(low).at[spots[1]].set(largest)


def shard_levels(key, dims, cuts, low, largest):
    factor_of = 1.0
    for dim, shards_of in cuts:
        heights = jax.random.uniform(jax.random.fold_in(jax.random.fold_in(key, 6), dim), (shards_of,), jnp.float32, low / len(cuts), largest / len(cuts))
        factor_of = factor_of * jnp.repeat(jnp.exp(heights), dims[dim] // shards_of).reshape((-1,) + (1,) * (len(dims) - 1 - dim))
    return factor_of


def centred(rng, dims, width, most, pieces=(), kind=jnp.bfloat16):
    result = jax.random.normal(rng, dims, jnp.float32) * width
    if len(pieces) > 0:
        result = shard_levels(rng, dims, pieces, -0.22, 0.18) * result
    return jnp.clip(result, min=-most, max=most).astype(kind)


def setup_inputs(seed: int = 0) -> dict:
    keys = jax.random.split(jax.random.key(seed), 8)
    obs_rows = centred(keys[0], (OBS_ALL, FIN), 1.0, 6.0, ((0, 32),))
    cell_ids = plant(jax.random.randint(keys[1], (OBS_ALL,), 0, H * W), jax.random.fold_in(keys[1], 1), 0, (H * W) - 1).astype(jnp.int32)
    counts = draw_counts(jax.random.fold_in(keys[7], 71), 0)
    w_embed = centred(keys[3], (FIN, D), FIN ** -0.5, 0.5)
    w_density = centred(keys[4], (D,), 0.5, 3.0)
    kernels = centred(keys[5], (LAYERS, 3, 3, D, D), (9 * D) ** -0.5, 0.125)
    cotangent = centred(keys[6], (NLAT, NLON, D), 1.0, 6.0, ((0, 4), (1, 8)))
    return dict(obs_rows=obs_rows, cell_ids=cell_ids, counts=counts, w_embed=w_embed, w_density=w_density, kernels=kernels, cotangent=cotangent)


def periodic_pad(field):
    field = jnp.concatenate([field[:, -1:], field, field[:, :1]], axis=1)
    return jnp.pad(field, ((1, 1), (0, 0), (0, 0)))

def conv_grid(field, kernel):
    padded = periodic_pad(field)
    rows_n = field.shape[0]
    cols_n = field.shape[1]
    chan_in = field.shape[2]
    total = jnp.zeros((rows_n * cols_n, kernel.shape[3]), jnp.float32)
    for row_off in range(3):
        for col_off in range(3):
            window = padded[row_off:row_off + rows_n, col_off:col_off + cols_n].reshape(rows_n * cols_n, chan_in)
            total = total + jnp.dot(window, kernel[row_off, col_off], precision=lax.Precision.HIGHEST)
    return total.reshape(rows_n, cols_n, kernel.shape[3])

def kernel_grad(field, slope):
    padded = periodic_pad(field)
    rows_n = field.shape[0]
    cols_n = field.shape[1]
    slope_flat = slope.reshape(rows_n * cols_n, slope.shape[2])
    tap_rows = []
    for row_off in range(3):
        tap_cols = []
        for col_off in range(3):
            window = padded[row_off:row_off + rows_n, col_off:col_off + cols_n].reshape(rows_n * cols_n, field.shape[2])
            tap_cols.append(jnp.dot(window.T, slope_flat, precision=lax.Precision.HIGHEST))
        tap_rows.append(jnp.stack(tap_cols))
    return jnp.stack(tap_rows)

def reference(obs_rows, cell_ids, counts, w_embed, w_density, kernels, cotangent):
    devices = N_LON * N_LAT
    grid_cells = NLAT * NLON
    row_index = jnp.arange(devices * devices * SLOT, dtype=jnp.int32)
    source = row_index // (devices * SLOT)
    target_dev = row_index // SLOT % devices
    live_mask = row_index % SLOT < counts[source, target_dev]
    lon_tile = target_dev // N_LAT
    lat_tile = target_dev % N_LAT
    target = (lat_tile * H + cell_ids // W) * NLON + lon_tile * W + cell_ids % W
    segment = jnp.where(live_mask, target, grid_cells).astype(jnp.int32)

    def add_source(running, piece):
        feats_piece, seg_piece = piece
        return (running + jax.ops.segment_sum(feats_piece.astype(jnp.float32), seg_piece, num_segments=grid_cells + 1), None)
    cell_sums, _unused = lax.scan(add_source, jnp.zeros((grid_cells + 1, FIN), jnp.float32), (obs_rows.reshape(devices, devices * SLOT, FIN), segment.reshape(devices, devices * SLOT)))
    cell_sums = cell_sums[:grid_cells]
    density = jax.ops.segment_sum(live_mask.astype(jnp.float32), segment, num_segments=grid_cells + 1)[:grid_cells]
    inv_root = lax.rsqrt(density + 1.0)
    features = (cell_sums * inv_root[:, None]).astype(jnp.bfloat16)
    start_act = jnp.dot(features, w_embed, preferred_element_type=jnp.float32) + jnp.log1p(density)[:, None] * w_density.astype(jnp.float32)[None, :]
    activation = start_act.astype(jnp.bfloat16).reshape(NLAT, NLON, D)
    stored_acts = []
    stored_pre = []
    for layer_index in range(LAYERS):
        preact = conv_grid(activation.astype(jnp.float32), kernels[layer_index].astype(jnp.float32))
        stored_acts.append(activation)
        stored_pre.append(preact)
        activation = (activation.astype(jnp.float32) + jax.nn.silu(preact)).astype(jnp.bfloat16)
    encoded = activation
    grad_scale = 1.0 / math.sqrt(grid_cells)
    back_low = cotangent
    kernel_grads = [None] * LAYERS
    for layer_index in reversed(range(LAYERS)):
        preact = stored_pre[layer_index]
        sigmoid_v = jax.nn.sigmoid(preact)
        slope_bf = (back_low.astype(jnp.float32) * (sigmoid_v * (1.0 + preact * (1.0 - sigmoid_v)))).astype(jnp.bfloat16)
        slope_f = slope_bf.astype(jnp.float32)
        kernel_grads[layer_index] = kernel_grad(stored_acts[layer_index].astype(jnp.float32), slope_f) * grad_scale
        flipped = jnp.transpose(kernels[layer_index][::-1, ::-1], (0, 1, 3, 2)).astype(jnp.float32)
        spread = conv_grid(slope_f, flipped)
        back_low = lax.optimization_barrier((back_low.astype(jnp.float32) + spread).astype(jnp.bfloat16))
    back_flat = back_low.reshape(grid_cells, D)
    embed_grad = jnp.dot(features.astype(jnp.float32).T, back_flat.astype(jnp.float32), precision=lax.Precision.HIGHEST) * grad_scale
    cell_grad = (jnp.dot(back_flat, w_embed.T, preferred_element_type=jnp.float32) * inv_root[:, None]).astype(jnp.bfloat16)
    picked = jnp.take(cell_grad, jnp.minimum(segment, grid_cells - 1), axis=0)
    grad_obs = jnp.where(live_mask[:, None], picked, jnp.zeros_like(picked))
    return (encoded, jnp.stack(kernel_grads).astype(jnp.bfloat16), embed_grad.astype(jnp.bfloat16), grad_obs)
```

```python
import math

import jax
import jax.numpy as jnp
from jax import lax
from jax.sharding import PartitionSpec as P

ID_BASE = 128


def shift_pairs(count, step, periodic):
    pairs = []
    for source in range(count):
        target = source + step
        if 0 <= target < count:
            pairs.append((source, target))
        elif periodic:
            pairs.append((source, target % count))
    return pairs


def widen(block, depth):
    lon_count = lax.axis_size("lon")
    lat_count = lax.axis_size("lat")
    west = lax.ppermute(block[:, -depth:], "lon", shift_pairs(lon_count, 1, True))
    east = lax.ppermute(block[:, :depth], "lon", shift_pairs(lon_count, -1, True))
    block = jnp.concatenate([west, block, east], axis=1)
    north = lax.ppermute(block[-depth:], "lat", shift_pairs(lat_count, 1, False))
    south = lax.ppermute(block[:depth], "lat", shift_pairs(lat_count, -1, False))
    return jnp.concatenate([north, block, south], axis=0)


def lat_mask(rows, margin, height):
    lat_index = lax.axis_index("lat")
    lat_count = lax.axis_size("lat")
    global_row = lat_index * height - margin + jnp.arange(rows, dtype=jnp.int32)
    return ((global_row >= 0) & (global_row < lat_count * height))[:, None, None]


def crop(field, margin):
    if margin == 0:
        return field
    return field[margin:-margin, margin:-margin]


def conv_valid(padded, kernel):
    return lax.conv_general_dilated(
        padded[None],
        kernel,
        (1, 1),
        "VALID",
        dimension_numbers=("NHWC", "HWIO", "NHWC"),
        preferred_element_type=jnp.float32,
    )[0]


def reduce_replicated(parts):
    flat = jnp.concatenate([part.reshape(-1) for part in parts])
    summed = lax.psum_scatter(flat, ("lon", "lat"), scatter_dimension=0, tiled=True)
    return summed


def on_device(obs_rows, cell_ids, counts, w_embed, w_density, kernels, cotangent):
    lon_count = lax.axis_size("lon")
    lat_count = lax.axis_size("lat")
    devices = lon_count * lat_count
    height, tile_width, channels = cotangent.shape
    cell_count = height * tile_width
    slot_rows = obs_rows.shape[0] // devices
    feat_count = obs_rows.shape[1]
    layer_count = kernels.shape[0]
    margin = 2 * layer_count

    cot_wide = widen(cotangent, layer_count)

    live_mask = jnp.arange(slot_rows, dtype=jnp.int32)[None, :] < counts[0][:, None]
    slot_ids = cell_ids.reshape(devices, slot_rows)
    id_high = jnp.where(live_mask, slot_ids // ID_BASE, -1)
    id_low = jnp.where(live_mask, slot_ids % ID_BASE, -1)
    code = jnp.concatenate([id_high, id_low], axis=1).astype(jnp.bfloat16)
    code_rows = -(-2 * slot_rows // feat_count)
    code_pad = -(-code_rows // 16) * 16
    code = jnp.pad(code, ((0, 0), (0, code_rows * feat_count - 2 * slot_rows)))
    code = code.reshape(devices, code_rows, feat_count)
    code = jnp.pad(code, ((0, 0), (0, code_pad - code_rows), (0, 0)))
    packed = jnp.concatenate([obs_rows.reshape(devices, slot_rows, feat_count), code], axis=1)
    got = lax.all_to_all(packed, ("lon", "lat"), split_axis=0, concat_axis=0, tiled=True)
    got_rows = got[:, :slot_rows].reshape(devices * slot_rows, feat_count)
    got_code = got[:, slot_rows : slot_rows + code_rows].reshape(devices, code_rows * feat_count)
    got_code = got_code.astype(jnp.int32)
    got_ids = (got_code[:, :slot_rows] * ID_BASE + got_code[:, slot_rows : 2 * slot_rows]).reshape(-1)

    cell_iota = jnp.arange(cell_count, dtype=jnp.int32)
    onehot = (got_ids[:, None] == cell_iota[None, :]).astype(jnp.bfloat16)
    cell_sums = lax.dot_general(
        onehot, got_rows, (((0,), (0,)), ((), ())), preferred_element_type=jnp.float32
    )
    density = jnp.sum(onehot.astype(jnp.float32), axis=0)
    inv_root = lax.rsqrt(density + 1.0)
    features = (cell_sums * inv_root[:, None]).astype(jnp.bfloat16)
    start_act = (
        jnp.dot(features, w_embed, preferred_element_type=jnp.float32)
        + jnp.log1p(density)[:, None] * w_density.astype(jnp.float32)[None, :]
    )
    activation = start_act.astype(jnp.bfloat16).reshape(height, tile_width, channels)

    act = widen(activation, margin)
    stored_acts = [act]
    stored_pre = []
    for layer_index in range(layer_count):
        out_margin = margin - layer_index - 1
        preact = conv_valid(act, kernels[layer_index])
        act = (crop(act, 1).astype(jnp.float32) + jax.nn.silu(preact)).astype(jnp.bfloat16)
        act = jnp.where(lat_mask(act.shape[0], out_margin, height), act, jnp.zeros_like(act))
        stored_pre.append(preact)
        stored_acts.append(act)
    encoded = crop(act, margin - layer_count)

    grad_scale = 1.0 / math.sqrt(cell_count * devices)
    back = cot_wide
    reduced = [None] * layer_count
    for layer_index in reversed(range(layer_count)):
        back_margin = layer_index + 1
        preact = crop(stored_pre[layer_index], margin - layer_index - 1 - back_margin)
        sigmoid_v = jax.nn.sigmoid(preact)
        slope = (
            back.astype(jnp.float32) * (sigmoid_v * (1.0 + preact * (1.0 - sigmoid_v)))
        ).astype(jnp.bfloat16)
        slope = jnp.where(lat_mask(slope.shape[0], back_margin, height), slope, jnp.zeros_like(slope))
        slope_flat = crop(slope, back_margin).reshape(cell_count, channels)
        act_in = crop(stored_acts[layer_index], margin - layer_index - 1)
        tap_rows = []
        for row_off in range(3):
            tap_cols = []
            for col_off in range(3):
                window = act_in[row_off : row_off + height, col_off : col_off + tile_width].reshape(
                    cell_count, channels
                )
                tap_cols.append(
                    lax.dot_general(
                        window,
                        slope_flat,
                        (((0,), (0,)), ((), ())),
                        preferred_element_type=jnp.float32,
                    )
                )
            tap_rows.append(jnp.stack(tap_cols))
        tap_grad = jnp.stack(tap_rows)
        flipped = jnp.transpose(kernels[layer_index][::-1, ::-1], (0, 1, 3, 2))
        spread = conv_valid(slope, flipped)
        back = lax.optimization_barrier(
            (crop(back, 1).astype(jnp.float32) + spread).astype(jnp.bfloat16)
        )
        if layer_index > 0:
            reduced[layer_index] = reduce_replicated([tap_grad])
        else:
            last_grad = tap_grad
    back_flat = back.reshape(cell_count, channels)
    embed_grad = lax.dot_general(
        features, back_flat, (((0,), (0,)), ((), ())), preferred_element_type=jnp.float32
    )
    reduced[0] = reduce_replicated([last_grad, embed_grad])
    cell_grad = (
        lax.dot_general(
            back_flat, w_embed, (((1,), (1,)), ((), ())), preferred_element_type=jnp.float32
        )
        * inv_root[:, None]
    ).astype(jnp.bfloat16)
    picked = jnp.dot(onehot, cell_grad, preferred_element_type=jnp.float32).astype(jnp.bfloat16)
    grad_obs = lax.all_to_all(picked, ("lon", "lat"), split_axis=0, concat_axis=0, tiled=True)

    tap_size = kernels[0].size
    gathered = [
        lax.all_gather((part * grad_scale).astype(jnp.bfloat16), ("lon", "lat"), axis=0, tiled=True)
        for part in reduced
    ]
    kernel_out = jnp.stack(
        [gathered[0][:tap_size]] + [gathered[index] for index in range(1, layer_count)]
    ).reshape(kernels.shape)
    embed_out = gathered[0][tap_size:].reshape(w_embed.shape)
    return (encoded, kernel_out, embed_out, grad_obs)


def solution(mesh):
    placed = (
        P(("lon", "lat"), None),
        P(("lon", "lat")),
        P(("lon", "lat"), None),
        P(),
        P(),
        P(),
        P("lat", "lon", None),
    )
    return jax.shard_map(
        on_device,
        mesh=mesh,
        in_specs=placed,
        out_specs=(P("lat", "lon", None), P(), P(), P(("lon", "lat"), None)),
        check_vma=False,
    )
```

```python
import math

import jax
import jax.numpy as jnp
from jax import lax
from jax.sharding import PartitionSpec as P

ID_BASE = 128


def shift_pairs(count, step, periodic):
    pairs = []
    for source in range(count):
        target = source + step
        if 0 <= target < count:
            pairs.append((source, target))
        elif periodic:
            pairs.append((source, target % count))
    return pairs


def widen(block, depth):
    lon_count = lax.axis_size("lon")
    lat_count = lax.axis_size("lat")
    west = lax.ppermute(block[:, -depth:], "lon", shift_pairs(lon_count, 1, True))
    east = lax.ppermute(block[:, :depth], "lon", shift_pairs(lon_count, -1, True))
    block = jnp.concatenate([west, block, east], axis=1)
    north = lax.ppermute(block[-depth:], "lat", shift_pairs(lat_count, 1, False))
    south = lax.ppermute(block[:depth], "lat", shift_pairs(lat_count, -1, False))
    return jnp.concatenate([north, block, south], axis=0)


def lat_mask(rows, margin, height):
    lat_index = lax.axis_index("lat")
    lat_count = lax.axis_size("lat")
    global_row = lat_index * height - margin + jnp.arange(rows, dtype=jnp.int32)
    return ((global_row >= 0) & (global_row < lat_count * height))[:, None, None]


def crop(field, margin):
    if margin == 0:
        return field
    return field[margin:-margin, margin:-margin]


def conv_valid(padded, kernel):
    return lax.conv_general_dilated(
        padded[None],
        kernel,
        (1, 1),
        "VALID",
        dimension_numbers=("NHWC", "HWIO", "NHWC"),
        preferred_element_type=jnp.float32,
    )[0]


def cube_steps():
    steps = []
    for axis in ("lon", "lat"):
        count = lax.axis_size(axis)
        bit = 1
        while bit < count:
            steps.append((axis, bit, [(i, i ^ bit) for i in range(count)]))
            bit *= 2
    return steps


def reduce_replicated(parts):
    part = jnp.concatenate([piece.reshape(-1) for piece in parts])
    for axis, bit, pairs in cube_steps():
        half = part.shape[0] // 2
        mine = (lax.axis_index(axis) // bit) % 2
        keep = lax.dynamic_slice_in_dim(part, mine * half, half)
        give = lax.dynamic_slice_in_dim(part, (1 - mine) * half, half)
        got = lax.ppermute(give.astype(jnp.bfloat16), axis, pairs)
        part = keep + got.astype(jnp.float32)
    return part


def gather_replicated(part):
    for axis, bit, pairs in reversed(cube_steps()):
        mine = (lax.axis_index(axis) // bit) % 2
        got = lax.ppermute(part, axis, pairs)
        first = jnp.where(mine == 0, part, got)
        second = jnp.where(mine == 0, got, part)
        part = jnp.concatenate([first, second])
    return part


def on_device(obs_rows, cell_ids, counts, w_embed, w_density, kernels, cotangent):
    lon_count = lax.axis_size("lon")
    lat_count = lax.axis_size("lat")
    devices = lon_count * lat_count
    height, tile_width, channels = cotangent.shape
    cell_count = height * tile_width
    slot_rows = obs_rows.shape[0] // devices
    feat_count = obs_rows.shape[1]
    layer_count = kernels.shape[0]
    margin = 2 * layer_count

    cot_wide = widen(cotangent, layer_count)

    live_mask = jnp.arange(slot_rows, dtype=jnp.int32)[None, :] < counts[0][:, None]
    slot_ids = cell_ids.reshape(devices, slot_rows)
    id_high = jnp.where(live_mask, slot_ids // ID_BASE, -1)
    id_low = jnp.where(live_mask, slot_ids % ID_BASE, -1)
    code = jnp.concatenate([id_high, id_low], axis=1).astype(jnp.bfloat16)
    code_rows = -(-2 * slot_rows // feat_count)
    code_pad = -(-code_rows // 16) * 16
    code = jnp.pad(code, ((0, 0), (0, code_rows * feat_count - 2 * slot_rows)))
    code = code.reshape(devices, code_rows, feat_count)
    code = jnp.pad(code, ((0, 0), (0, code_pad - code_rows), (0, 0)))
    packed = jnp.concatenate([obs_rows.reshape(devices, slot_rows, feat_count), code], axis=1)
    got = lax.all_to_all(packed, ("lon", "lat"), split_axis=0, concat_axis=0, tiled=True)
    got_rows = got[:, :slot_rows].reshape(devices * slot_rows, feat_count)
    got_code = got[:, slot_rows : slot_rows + code_rows].reshape(devices, code_rows * feat_count)
    got_code = got_code.astype(jnp.int32)
    got_ids = (got_code[:, :slot_rows] * ID_BASE + got_code[:, slot_rows : 2 * slot_rows]).reshape(-1)

    cell_iota = jnp.arange(cell_count, dtype=jnp.int32)
    onehot = (got_ids[:, None] == cell_iota[None, :]).astype(jnp.bfloat16)
    cell_sums = lax.dot_general(
        onehot, got_rows, (((0,), (0,)), ((), ())), preferred_element_type=jnp.float32
    )
    density = jnp.sum(onehot.astype(jnp.float32), axis=0)
    inv_root = lax.rsqrt(density + 1.0)
    features = (cell_sums * inv_root[:, None]).astype(jnp.bfloat16)
    start_act = (
        jnp.dot(features, w_embed, preferred_element_type=jnp.float32)
        + jnp.log1p(density)[:, None] * w_density.astype(jnp.float32)[None, :]
    )
    activation = start_act.astype(jnp.bfloat16).reshape(height, tile_width, channels)

    act = widen(activation, margin)
    stored_acts = [act]
    stored_pre = []
    for layer_index in range(layer_count):
        out_margin = margin - layer_index - 1
        preact = conv_valid(act, kernels[layer_index])
        act = (crop(act, 1).astype(jnp.float32) + jax.nn.silu(preact)).astype(jnp.bfloat16)
        act = jnp.where(lat_mask(act.shape[0], out_margin, height), act, jnp.zeros_like(act))
        stored_pre.append(preact)
        stored_acts.append(act)
    encoded = crop(act, margin - layer_count)

    grad_scale = 1.0 / math.sqrt(cell_count * devices)
    back = cot_wide
    reduced = [None] * layer_count
    for layer_index in reversed(range(layer_count)):
        back_margin = layer_index + 1
        preact = crop(stored_pre[layer_index], margin - layer_index - 1 - back_margin)
        sigmoid_v = jax.nn.sigmoid(preact)
        slope = (
            back.astype(jnp.float32) * (sigmoid_v * (1.0 + preact * (1.0 - sigmoid_v)))
        ).astype(jnp.bfloat16)
        slope = jnp.where(lat_mask(slope.shape[0], back_margin, height), slope, jnp.zeros_like(slope))
        slope_flat = crop(slope, back_margin).reshape(cell_count, channels)
        act_in = crop(stored_acts[layer_index], margin - layer_index - 1)
        tap_rows = []
        for row_off in range(3):
            tap_cols = []
            for col_off in range(3):
                window = act_in[row_off : row_off + height, col_off : col_off + tile_width].reshape(
                    cell_count, channels
                )
                tap_cols.append(
                    lax.dot_general(
                        window,
                        slope_flat,
                        (((0,), (0,)), ((), ())),
                        preferred_element_type=jnp.float32,
                    )
                )
            tap_rows.append(jnp.stack(tap_cols))
        tap_grad = jnp.stack(tap_rows)
        flipped = jnp.transpose(kernels[layer_index][::-1, ::-1], (0, 1, 3, 2))
        spread = conv_valid(slope, flipped)
        back = lax.optimization_barrier(
            (crop(back, 1).astype(jnp.float32) + spread).astype(jnp.bfloat16)
        )
        if layer_index > 0:
            reduced[layer_index] = reduce_replicated([tap_grad])
        else:
            last_grad = tap_grad
    back_flat = back.reshape(cell_count, channels)
    embed_grad = lax.dot_general(
        features, back_flat, (((0,), (0,)), ((), ())), preferred_element_type=jnp.float32
    )
    reduced[0] = reduce_replicated([last_grad, embed_grad])
    cell_grad = (
        lax.dot_general(
            back_flat, w_embed, (((1,), (1,)), ((), ())), preferred_element_type=jnp.float32
        )
        * inv_root[:, None]
    ).astype(jnp.bfloat16)
    picked = jnp.dot(onehot, cell_grad, preferred_element_type=jnp.float32).astype(jnp.bfloat16)
    grad_obs = lax.all_to_all(picked, ("lon", "lat"), split_axis=0, concat_axis=0, tiled=True)

    tap_size = kernels[0].size
    gathered = [
        gather_replicated((part * grad_scale).astype(jnp.bfloat16)) for part in reduced
    ]
    kernel_out = jnp.stack(
        [gathered[0][:tap_size]] + [gathered[index] for index in range(1, layer_count)]
    ).reshape(kernels.shape)
    embed_out = gathered[0][tap_size:].reshape(w_embed.shape)
    return (encoded, kernel_out, embed_out, grad_obs)


def solution(mesh):
    placed = (
        P(("lon", "lat"), None),
        P(("lon", "lat")),
        P(("lon", "lat"), None),
        P(),
        P(),
        P(),
        P("lat", "lon", None),
    )
    return jax.shard_map(
        on_device,
        mesh=mesh,
        in_specs=placed,
        out_specs=(P("lat", "lon", None), P(), P(), P(("lon", "lat"), None)),
        check_vma=False,
    )
```

```python
import math

import jax
import jax.numpy as jnp
from jax import lax
from jax.sharding import PartitionSpec as P

ID_BASE = 128


def shift_pairs(count, step, periodic):
    pairs = []
    for source in range(count):
        target = source + step
        if 0 <= target < count:
            pairs.append((source, target))
        elif periodic:
            pairs.append((source, target % count))
    return pairs


def widen(block, depth):
    lon_count = lax.axis_size("lon")
    lat_count = lax.axis_size("lat")
    west = lax.ppermute(block[:, -depth:], "lon", shift_pairs(lon_count, 1, True))
    east = lax.ppermute(block[:, :depth], "lon", shift_pairs(lon_count, -1, True))
    block = jnp.concatenate([west, block, east], axis=1)
    north = lax.ppermute(block[-depth:], "lat", shift_pairs(lat_count, 1, False))
    south = lax.ppermute(block[:depth], "lat", shift_pairs(lat_count, -1, False))
    return jnp.concatenate([north, block, south], axis=0)


def lat_mask(rows, margin, height):
    lat_index = lax.axis_index("lat")
    lat_count = lax.axis_size("lat")
    global_row = lat_index * height - margin + jnp.arange(rows, dtype=jnp.int32)
    return ((global_row >= 0) & (global_row < lat_count * height))[:, None, None]


def crop(field, margin):
    if margin == 0:
        return field
    return field[margin:-margin, margin:-margin]


def conv_valid(padded, kernel):
    return lax.conv_general_dilated(
        padded[None],
        kernel,
        (1, 1),
        "VALID",
        dimension_numbers=("NHWC", "HWIO", "NHWC"),
        preferred_element_type=jnp.float32,
    )[0]


def cube_steps():
    steps = []
    for axis in ("lon", "lat"):
        count = lax.axis_size(axis)
        bit = 1
        while bit < count:
            steps.append((axis, bit, [(i, i ^ bit) for i in range(count)]))
            bit *= 2
    return steps


def reduce_replicated(part, steps):
    for axis, bit, pairs in steps:
        half = part.shape[0] // 2
        mine = (lax.axis_index(axis) // bit) % 2
        keep = lax.dynamic_slice_in_dim(part, mine * half, half)
        give = lax.dynamic_slice_in_dim(part, (1 - mine) * half, half)
        got = lax.ppermute(give.astype(jnp.bfloat16), axis, pairs)
        part = keep + got.astype(jnp.float32)
    return part


def gather_replicated(part, steps):
    for axis, bit, pairs in reversed(steps):
        mine = (lax.axis_index(axis) // bit) % 2
        got = lax.ppermute(part, axis, pairs)
        first = jnp.where(mine == 0, part, got)
        second = jnp.where(mine == 0, got, part)
        part = jnp.concatenate([first, second])
    return part


def all_sum(pieces, scale, streams=3):
    flat = jnp.concatenate([piece.reshape(-1) for piece in pieces])
    steps = cube_steps()
    devices = 2 ** len(steps)
    unit = devices * 16 * streams
    total = flat.shape[0]
    flat = jnp.pad(flat, (0, -(-total // unit) * unit - total))
    size = flat.shape[0] // streams
    middle = steps[1:-1] if len(steps) > 2 else []
    outs = []
    for stream in range(streams):
        shift = stream % len(middle) if middle else 0
        order = steps[:1] + middle[shift:] + middle[:shift] + steps[len(middle) + 1 :]
        if len(steps) <= 2:
            order = steps
        part = reduce_replicated(flat[stream * size : (stream + 1) * size], order)
        outs.append(gather_replicated((part * scale).astype(jnp.bfloat16), order))
    return jnp.concatenate(outs)[:total]


def on_device(obs_rows, cell_ids, counts, w_embed, w_density, kernels, cotangent):
    lon_count = lax.axis_size("lon")
    lat_count = lax.axis_size("lat")
    devices = lon_count * lat_count
    height, tile_width, channels = cotangent.shape
    cell_count = height * tile_width
    slot_rows = obs_rows.shape[0] // devices
    feat_count = obs_rows.shape[1]
    layer_count = kernels.shape[0]
    margin = 2 * layer_count

    cot_wide = widen(cotangent, layer_count)

    live_mask = jnp.arange(slot_rows, dtype=jnp.int32)[None, :] < counts[0][:, None]
    slot_ids = cell_ids.reshape(devices, slot_rows)
    id_high = jnp.where(live_mask, slot_ids // ID_BASE, -1)
    id_low = jnp.where(live_mask, slot_ids % ID_BASE, -1)
    code = jnp.concatenate([id_high, id_low], axis=1).astype(jnp.bfloat16)
    code_rows = -(-2 * slot_rows // feat_count)
    code_pad = -(-code_rows // 16) * 16
    code = jnp.pad(code, ((0, 0), (0, code_rows * feat_count - 2 * slot_rows)))
    code = code.reshape(devices, code_rows, feat_count)
    code = jnp.pad(code, ((0, 0), (0, code_pad - code_rows), (0, 0)))
    packed = jnp.concatenate([obs_rows.reshape(devices, slot_rows, feat_count), code], axis=1)
    got = lax.all_to_all(packed, ("lon", "lat"), split_axis=0, concat_axis=0, tiled=True)
    got_rows = got[:, :slot_rows].reshape(devices * slot_rows, feat_count)
    got_code = got[:, slot_rows : slot_rows + code_rows].reshape(devices, code_rows * feat_count)
    got_code = got_code.astype(jnp.int32)
    got_ids = (got_code[:, :slot_rows] * ID_BASE + got_code[:, slot_rows : 2 * slot_rows]).reshape(-1)

    cell_iota = jnp.arange(cell_count, dtype=jnp.int32)
    onehot = (got_ids[:, None] == cell_iota[None, :]).astype(jnp.bfloat16)
    cell_sums = lax.dot_general(
        onehot, got_rows, (((0,), (0,)), ((), ())), preferred_element_type=jnp.float32
    )
    density = jnp.sum(onehot.astype(jnp.float32), axis=0)
    inv_root = lax.rsqrt(density + 1.0)
    features = (cell_sums * inv_root[:, None]).astype(jnp.bfloat16)
    start_act = (
        jnp.dot(features, w_embed, preferred_element_type=jnp.float32)
        + jnp.log1p(density)[:, None] * w_density.astype(jnp.float32)[None, :]
    )
    activation = start_act.astype(jnp.bfloat16).reshape(height, tile_width, channels)

    act = widen(activation, margin)
    stored_acts = [act]
    stored_pre = []
    for layer_index in range(layer_count):
        out_margin = margin - layer_index - 1
        preact = conv_valid(act, kernels[layer_index])
        act = (crop(act, 1).astype(jnp.float32) + jax.nn.silu(preact)).astype(jnp.bfloat16)
        act = jnp.where(lat_mask(act.shape[0], out_margin, height), act, jnp.zeros_like(act))
        stored_pre.append(preact)
        stored_acts.append(act)
    encoded = crop(act, margin - layer_count)

    grad_scale = 1.0 / math.sqrt(cell_count * devices)
    back = cot_wide
    grads = [None] * layer_count
    for layer_index in reversed(range(layer_count)):
        back_margin = layer_index + 1
        preact = crop(stored_pre[layer_index], margin - layer_index - 1 - back_margin)
        sigmoid_v = jax.nn.sigmoid(preact)
        slope = (
            back.astype(jnp.float32) * (sigmoid_v * (1.0 + preact * (1.0 - sigmoid_v)))
        ).astype(jnp.bfloat16)
        slope = jnp.where(lat_mask(slope.shape[0], back_margin, height), slope, jnp.zeros_like(slope))
        slope_flat = crop(slope, back_margin).reshape(cell_count, channels)
        act_in = crop(stored_acts[layer_index], margin - layer_index - 1)
        tap_rows = []
        for row_off in range(3):
            tap_cols = []
            for col_off in range(3):
                window = act_in[row_off : row_off + height, col_off : col_off + tile_width].reshape(
                    cell_count, channels
                )
                tap_cols.append(
                    lax.dot_general(
                        window,
                        slope_flat,
                        (((0,), (0,)), ((), ())),
                        preferred_element_type=jnp.float32,
                    )
                )
            tap_rows.append(jnp.stack(tap_cols))
        tap_grad = jnp.stack(tap_rows)
        flipped = jnp.transpose(kernels[layer_index][::-1, ::-1], (0, 1, 3, 2))
        spread = conv_valid(slope, flipped)
        back = lax.optimization_barrier(
            (crop(back, 1).astype(jnp.float32) + spread).astype(jnp.bfloat16)
        )
        grads[layer_index] = tap_grad
    back_flat = back.reshape(cell_count, channels)
    embed_grad = lax.dot_general(
        features, back_flat, (((0,), (0,)), ((), ())), preferred_element_type=jnp.float32
    )
    cell_grad = (
        lax.dot_general(
            back_flat, w_embed, (((1,), (1,)), ((), ())), preferred_element_type=jnp.float32
        )
        * inv_root[:, None]
    ).astype(jnp.bfloat16)
    picked = jnp.dot(onehot, cell_grad, preferred_element_type=jnp.float32).astype(jnp.bfloat16)
    grad_obs = lax.all_to_all(picked, ("lon", "lat"), split_axis=0, concat_axis=0, tiled=True)

    summed = all_sum(grads + [embed_grad], grad_scale)
    kernel_out = summed[: kernels.size].reshape(kernels.shape)
    embed_out = summed[kernels.size :].reshape(w_embed.shape)
    return (encoded, kernel_out, embed_out, grad_obs)


def solution(mesh):
    placed = (
        P(("lon", "lat"), None),
        P(("lon", "lat")),
        P(("lon", "lat"), None),
        P(),
        P(),
        P(),
        P("lat", "lon", None),
    )
    return jax.shard_map(
        on_device,
        mesh=mesh,
        in_specs=placed,
        out_specs=(P("lat", "lon", None), P(), P(), P(("lon", "lat"), None)),
        check_vma=False,
    )
```

```python
import math

import jax
import jax.numpy as jnp
from jax import lax
from jax.sharding import PartitionSpec as P

ID_BASE = 128


def shift_pairs(count, step, periodic):
    pairs = []
    for source in range(count):
        target = source + step
        if 0 <= target < count:
            pairs.append((source, target))
        elif periodic:
            pairs.append((source, target % count))
    return pairs


def widen(block, depth):
    lon_count = lax.axis_size("lon")
    lat_count = lax.axis_size("lat")
    west = lax.ppermute(block[:, -depth:], "lon", shift_pairs(lon_count, 1, True))
    east = lax.ppermute(block[:, :depth], "lon", shift_pairs(lon_count, -1, True))
    block = jnp.concatenate([west, block, east], axis=1)
    north = lax.ppermute(block[-depth:], "lat", shift_pairs(lat_count, 1, False))
    south = lax.ppermute(block[:depth], "lat", shift_pairs(lat_count, -1, False))
    return jnp.concatenate([north, block, south], axis=0)


def lat_mask(rows, margin, height):
    lat_index = lax.axis_index("lat")
    lat_count = lax.axis_size("lat")
    global_row = lat_index * height - margin + jnp.arange(rows, dtype=jnp.int32)
    return ((global_row >= 0) & (global_row < lat_count * height))[:, None, None]


def crop(field, margin):
    if margin == 0:
        return field
    return field[margin:-margin, margin:-margin]


def conv_valid(padded, kernel):
    return lax.conv_general_dilated(
        padded[None],
        kernel,
        (1, 1),
        "VALID",
        dimension_numbers=("NHWC", "HWIO", "NHWC"),
        preferred_element_type=jnp.float32,
    )[0]


def cube_steps():
    steps = []
    for axis in ("lon", "lat"):
        count = lax.axis_size(axis)
        bit = 1
        while bit < count:
            steps.append((axis, bit, [(i, i ^ bit) for i in range(count)]))
            bit *= 2
    return steps


def reduce_replicated(part, steps):
    for axis, bit, pairs in steps:
        half = part.shape[0] // 2
        mine = (lax.axis_index(axis) // bit) % 2
        keep = lax.dynamic_slice_in_dim(part, mine * half, half)
        give = lax.dynamic_slice_in_dim(part, (1 - mine) * half, half)
        got = lax.ppermute(give.astype(jnp.bfloat16), axis, pairs)
        part = keep + got.astype(jnp.float32)
    return part


def gather_replicated(part, steps):
    for axis, bit, pairs in reversed(steps):
        mine = (lax.axis_index(axis) // bit) % 2
        got = lax.ppermute(part, axis, pairs)
        first = jnp.where(mine == 0, part, got)
        second = jnp.where(mine == 0, got, part)
        part = jnp.concatenate([first, second])
    return part


def all_sum(pieces, scale, streams=3):
    lanes = pieces[0].shape[-1]
    flat = jnp.concatenate([piece.reshape(-1, lanes) for piece in pieces])
    steps = cube_steps()
    devices = 2 ** len(steps)
    unit = devices * 16
    total = flat.shape[0]
    units = -(-total // unit)
    flat = jnp.pad(flat, ((0, units * unit - total), (0, 0)))
    middle = steps[1:-1] if len(steps) > 2 else []
    outs = []
    begin = 0
    for stream in range(streams):
        count = units // streams + (1 if stream < units % streams else 0)
        if count == 0:
            continue
        shift = stream % len(middle) if middle else 0
        order = steps[:1] + middle[shift:] + middle[:shift] + steps[len(middle) + 1 :]
        if len(steps) <= 2:
            order = steps
        part = reduce_replicated(flat[begin : begin + count * unit], order)
        outs.append(gather_replicated((part * scale).astype(jnp.bfloat16), order))
        begin += count * unit
    return jnp.concatenate(outs)[:total]


def on_device(obs_rows, cell_ids, counts, w_embed, w_density, kernels, cotangent):
    lon_count = lax.axis_size("lon")
    lat_count = lax.axis_size("lat")
    devices = lon_count * lat_count
    height, tile_width, channels = cotangent.shape
    cell_count = height * tile_width
    slot_rows = obs_rows.shape[0] // devices
    feat_count = obs_rows.shape[1]
    layer_count = kernels.shape[0]
    margin = 2 * layer_count

    cot_wide = widen(cotangent, layer_count)

    live_mask = jnp.arange(slot_rows, dtype=jnp.int32)[None, :] < counts[0][:, None]
    slot_ids = cell_ids.reshape(devices, slot_rows)
    id_high = jnp.where(live_mask, slot_ids // ID_BASE, -1)
    id_low = jnp.where(live_mask, slot_ids % ID_BASE, -1)
    code = jnp.concatenate([id_high, id_low], axis=1).astype(jnp.bfloat16)
    code_rows = -(-2 * slot_rows // feat_count)
    code_pad = -(-code_rows // 16) * 16
    code = jnp.pad(code, ((0, 0), (0, code_rows * feat_count - 2 * slot_rows)))
    code = code.reshape(devices, code_rows, feat_count)
    code = jnp.pad(code, ((0, 0), (0, code_pad - code_rows), (0, 0)))
    packed = jnp.concatenate([obs_rows.reshape(devices, slot_rows, feat_count), code], axis=1)
    got = lax.all_to_all(packed, ("lon", "lat"), split_axis=0, concat_axis=0, tiled=True)
    got_rows = got[:, :slot_rows].reshape(devices * slot_rows, feat_count)
    got_code = got[:, slot_rows : slot_rows + code_rows].reshape(devices, code_rows * feat_count)
    got_code = got_code.astype(jnp.int32)
    got_ids = (got_code[:, :slot_rows] * ID_BASE + got_code[:, slot_rows : 2 * slot_rows]).reshape(-1)

    cell_iota = jnp.arange(cell_count, dtype=jnp.int32)
    onehot = (got_ids[:, None] == cell_iota[None, :]).astype(jnp.bfloat16)
    cell_sums = lax.dot_general(
        onehot, got_rows, (((0,), (0,)), ((), ())), preferred_element_type=jnp.float32
    )
    density = jnp.sum(onehot.astype(jnp.float32), axis=0)
    inv_root = lax.rsqrt(density + 1.0)
    features = (cell_sums * inv_root[:, None]).astype(jnp.bfloat16)
    start_act = (
        jnp.dot(features, w_embed, preferred_element_type=jnp.float32)
        + jnp.log1p(density)[:, None] * w_density.astype(jnp.float32)[None, :]
    )
    activation = start_act.astype(jnp.bfloat16).reshape(height, tile_width, channels)

    act = widen(activation, margin)
    stored_acts = [act]
    stored_pre = []
    for layer_index in range(layer_count):
        out_margin = margin - layer_index - 1
        preact = conv_valid(act, kernels[layer_index])
        act = (crop(act, 1).astype(jnp.float32) + jax.nn.silu(preact)).astype(jnp.bfloat16)
        act = jnp.where(lat_mask(act.shape[0], out_margin, height), act, jnp.zeros_like(act))
        stored_pre.append(preact)
        stored_acts.append(act)
    encoded = crop(act, margin - layer_count)

    grad_scale = 1.0 / math.sqrt(cell_count * devices)
    back = cot_wide
    grads = [None] * layer_count
    for layer_index in reversed(range(layer_count)):
        back_margin = layer_index + 1
        preact = crop(stored_pre[layer_index], margin - layer_index - 1 - back_margin)
        sigmoid_v = jax.nn.sigmoid(preact)
        slope = (
            back.astype(jnp.float32) * (sigmoid_v * (1.0 + preact * (1.0 - sigmoid_v)))
        ).astype(jnp.bfloat16)
        slope = jnp.where(lat_mask(slope.shape[0], back_margin, height), slope, jnp.zeros_like(slope))
        slope_flat = crop(slope, back_margin).reshape(cell_count, channels)
        act_in = crop(stored_acts[layer_index], margin - layer_index - 1)
        tap_rows = []
        for row_off in range(3):
            tap_cols = []
            for col_off in range(3):
                window = act_in[row_off : row_off + height, col_off : col_off + tile_width].reshape(
                    cell_count, channels
                )
                tap_cols.append(
                    lax.dot_general(
                        window,
                        slope_flat,
                        (((0,), (0,)), ((), ())),
                        preferred_element_type=jnp.float32,
                    )
                )
            tap_rows.append(jnp.stack(tap_cols))
        tap_grad = jnp.stack(tap_rows)
        flipped = jnp.transpose(kernels[layer_index][::-1, ::-1], (0, 1, 3, 2))
        spread = conv_valid(slope, flipped)
        back = lax.optimization_barrier(
            (crop(back, 1).astype(jnp.float32) + spread).astype(jnp.bfloat16)
        )
        grads[layer_index] = tap_grad
    back_flat = back.reshape(cell_count, channels)
    embed_grad = lax.dot_general(
        features, back_flat, (((0,), (0,)), ((), ())), preferred_element_type=jnp.float32
    )
    cell_grad = (
        lax.dot_general(
            back_flat, w_embed, (((1,), (1,)), ((), ())), preferred_element_type=jnp.float32
        )
        * inv_root[:, None]
    ).astype(jnp.bfloat16)
    picked = jnp.dot(onehot, cell_grad, preferred_element_type=jnp.float32).astype(jnp.bfloat16)
    grad_obs = lax.all_to_all(picked, ("lon", "lat"), split_axis=0, concat_axis=0, tiled=True)

    summed = all_sum(grads + [embed_grad], grad_scale)
    tap_rows_n = kernels.size // channels
    kernel_out = summed[:tap_rows_n].reshape(kernels.shape)
    embed_out = summed[tap_rows_n:]
    return (encoded, kernel_out, embed_out, grad_obs)


def solution(mesh):
    placed = (
        P(("lon", "lat"), None),
        P(("lon", "lat")),
        P(("lon", "lat"), None),
        P(),
        P(),
        P(),
        P("lat", "lon", None),
    )
    return jax.shard_map(
        on_device,
        mesh=mesh,
        in_specs=placed,
        out_specs=(P("lat", "lon", None), P(), P(), P(("lon", "lat"), None)),
        check_vma=False,
    )
```

```python
import math

import jax
import jax.numpy as jnp
from jax import lax
from jax.sharding import PartitionSpec as P

ID_BASE = 128


def shift_pairs(count, step, periodic):
    pairs = []
    for source in range(count):
        target = source + step
        if 0 <= target < count:
            pairs.append((source, target))
        elif periodic:
            pairs.append((source, target % count))
    return pairs


def widen(block, depth):
    lon_count = lax.axis_size("lon")
    lat_count = lax.axis_size("lat")
    west = lax.ppermute(block[:, -depth:], "lon", shift_pairs(lon_count, 1, True))
    east = lax.ppermute(block[:, :depth], "lon", shift_pairs(lon_count, -1, True))
    block = jnp.concatenate([west, block, east], axis=1)
    north = lax.ppermute(block[-depth:], "lat", shift_pairs(lat_count, 1, False))
    south = lax.ppermute(block[:depth], "lat", shift_pairs(lat_count, -1, False))
    return jnp.concatenate([north, block, south], axis=0)


def lat_mask(rows, margin, height):
    lat_index = lax.axis_index("lat")
    lat_count = lax.axis_size("lat")
    global_row = lat_index * height - margin + jnp.arange(rows, dtype=jnp.int32)
    return ((global_row >= 0) & (global_row < lat_count * height))[:, None, None]


def crop(field, margin):
    if margin == 0:
        return field
    return field[margin:-margin, margin:-margin]


def conv_valid(padded, kernel):
    return lax.conv_general_dilated(
        padded[None],
        kernel,
        (1, 1),
        "VALID",
        dimension_numbers=("NHWC", "HWIO", "NHWC"),
        preferred_element_type=jnp.float32,
    )[0]


def cube_steps():
    steps = []
    for axis in ("lon", "lat"):
        count = lax.axis_size(axis)
        bit = 1
        while bit < count:
            steps.append((axis, bit, [(i, i ^ bit) for i in range(count)]))
            bit *= 2
    return steps


def reduce_replicated(part, steps):
    for axis, bit, pairs in steps:
        half = part.shape[0] // 2
        mine = (lax.axis_index(axis) // bit) % 2
        keep = lax.dynamic_slice_in_dim(part, mine * half, half)
        give = lax.dynamic_slice_in_dim(part, (1 - mine) * half, half)
        got = lax.ppermute(give.astype(jnp.bfloat16), axis, pairs)
        part = keep + got.astype(jnp.float32)
    return part


def gather_replicated(part, steps):
    for axis, bit, pairs in reversed(steps):
        mine = (lax.axis_index(axis) // bit) % 2
        got = lax.ppermute(part, axis, pairs)
        first = jnp.where(mine == 0, part, got)
        second = jnp.where(mine == 0, got, part)
        part = jnp.concatenate([first, second])
    return part


def all_sum(pieces, scale, streams=1):
    lanes = pieces[0].shape[-1]
    flat = jnp.concatenate([piece.reshape(-1, lanes) for piece in pieces])
    steps = cube_steps()
    devices = 2 ** len(steps)
    unit = devices * 16
    total = flat.shape[0]
    units = -(-total // unit)
    flat = jnp.pad(flat, ((0, units * unit - total), (0, 0)))
    middle = steps[1:-1] if len(steps) > 2 else []
    outs = []
    begin = 0
    for stream in range(streams):
        count = units // streams + (1 if stream < units % streams else 0)
        if count == 0:
            continue
        shift = stream % len(middle) if middle else 0
        order = steps[:1] + middle[shift:] + middle[:shift] + steps[len(middle) + 1 :]
        if len(steps) <= 2:
            order = steps
        part = reduce_replicated(flat[begin : begin + count * unit], order)
        outs.append(gather_replicated((part * scale).astype(jnp.bfloat16), order))
        begin += count * unit
    return jnp.concatenate(outs)[:total]


def on_device(obs_rows, cell_ids, counts, w_embed, w_density, kernels, cotangent):
    lon_count = lax.axis_size("lon")
    lat_count = lax.axis_size("lat")
    devices = lon_count * lat_count
    height, tile_width, channels = cotangent.shape
    cell_count = height * tile_width
    slot_rows = obs_rows.shape[0] // devices
    feat_count = obs_rows.shape[1]
    layer_count = kernels.shape[0]
    margin = 2 * layer_count

    cot_wide = widen(cotangent, layer_count)

    live_mask = jnp.arange(slot_rows, dtype=jnp.int32)[None, :] < counts[0][:, None]
    slot_ids = cell_ids.reshape(devices, slot_rows)
    id_high = jnp.where(live_mask, slot_ids // ID_BASE, -1)
    id_low = jnp.where(live_mask, slot_ids % ID_BASE, -1)
    code = jnp.concatenate([id_high, id_low], axis=1).astype(jnp.bfloat16)
    code_rows = -(-2 * slot_rows // feat_count)
    code_pad = -(-code_rows // 16) * 16
    code = jnp.pad(code, ((0, 0), (0, code_rows * feat_count - 2 * slot_rows)))
    code = code.reshape(devices, code_rows, feat_count)
    code = jnp.pad(code, ((0, 0), (0, code_pad - code_rows), (0, 0)))
    packed = jnp.concatenate([obs_rows.reshape(devices, slot_rows, feat_count), code], axis=1)
    got = lax.all_to_all(packed, ("lon", "lat"), split_axis=0, concat_axis=0, tiled=True)
    got_rows = got[:, :slot_rows].reshape(devices * slot_rows, feat_count)
    got_code = got[:, slot_rows : slot_rows + code_rows].reshape(devices, code_rows * feat_count)
    got_code = got_code.astype(jnp.int32)
    got_ids = (got_code[:, :slot_rows] * ID_BASE + got_code[:, slot_rows : 2 * slot_rows]).reshape(-1)

    cell_iota = jnp.arange(cell_count, dtype=jnp.int32)
    onehot = (got_ids[:, None] == cell_iota[None, :]).astype(jnp.bfloat16)
    cell_sums = lax.dot_general(
        onehot, got_rows, (((0,), (0,)), ((), ())), preferred_element_type=jnp.float32
    )
    density = jnp.sum(onehot.astype(jnp.float32), axis=0)
    inv_root = lax.rsqrt(density + 1.0)
    features = (cell_sums * inv_root[:, None]).astype(jnp.bfloat16)
    start_act = (
        jnp.dot(features, w_embed, preferred_element_type=jnp.float32)
        + jnp.log1p(density)[:, None] * w_density.astype(jnp.float32)[None, :]
    )
    activation = start_act.astype(jnp.bfloat16).reshape(height, tile_width, channels)

    act = widen(activation, margin)
    stored_acts = [act]
    stored_pre = []
    for layer_index in range(layer_count):
        out_margin = margin - layer_index - 1
        preact = conv_valid(act, kernels[layer_index])
        act = (crop(act, 1).astype(jnp.float32) + jax.nn.silu(preact)).astype(jnp.bfloat16)
        act = jnp.where(lat_mask(act.shape[0], out_margin, height), act, jnp.zeros_like(act))
        stored_pre.append(preact)
        stored_acts.append(act)
    encoded = crop(act, margin - layer_count)

    grad_scale = 1.0 / math.sqrt(cell_count * devices)
    back = cot_wide
    grads = [None] * layer_count
    for layer_index in reversed(range(layer_count)):
        back_margin = layer_index + 1
        preact = crop(stored_pre[layer_index], margin - layer_index - 1 - back_margin)
        sigmoid_v = jax.nn.sigmoid(preact)
        slope = (
            back.astype(jnp.float32) * (sigmoid_v * (1.0 + preact * (1.0 - sigmoid_v)))
        ).astype(jnp.bfloat16)
        slope = jnp.where(lat_mask(slope.shape[0], back_margin, height), slope, jnp.zeros_like(slope))
        slope_flat = crop(slope, back_margin).reshape(cell_count, channels)
        act_in = crop(stored_acts[layer_index], margin - layer_index - 1)
        tap_rows = []
        for row_off in range(3):
            tap_cols = []
            for col_off in range(3):
                window = act_in[row_off : row_off + height, col_off : col_off + tile_width].reshape(
                    cell_count, channels
                )
                tap_cols.append(
                    lax.dot_general(
                        window,
                        slope_flat,
                        (((0,), (0,)), ((), ())),
                        preferred_element_type=jnp.float32,
                    )
                )
            tap_rows.append(jnp.stack(tap_cols))
        tap_grad = jnp.stack(tap_rows)
        flipped = jnp.transpose(kernels[layer_index][::-1, ::-1], (0, 1, 3, 2))
        spread = conv_valid(slope, flipped)
        back = lax.optimization_barrier(
            (crop(back, 1).astype(jnp.float32) + spread).astype(jnp.bfloat16)
        )
        grads[layer_index] = tap_grad
    back_flat = back.reshape(cell_count, channels)
    embed_grad = lax.dot_general(
        features, back_flat, (((0,), (0,)), ((), ())), preferred_element_type=jnp.float32
    )
    cell_grad = (
        lax.dot_general(
            back_flat, w_embed, (((1,), (1,)), ((), ())), preferred_element_type=jnp.float32
        )
        * inv_root[:, None]
    ).astype(jnp.bfloat16)
    picked = jnp.dot(onehot, cell_grad, preferred_element_type=jnp.float32).astype(jnp.bfloat16)
    grad_obs = lax.all_to_all(picked, ("lon", "lat"), split_axis=0, concat_axis=0, tiled=True)

    summed = all_sum(grads + [embed_grad], grad_scale)
    tap_rows_n = kernels.size // channels
    kernel_out = summed[:tap_rows_n].reshape(kernels.shape)
    embed_out = summed[tap_rows_n:]
    return (encoded, kernel_out, embed_out, grad_obs)


def solution(mesh):
    placed = (
        P(("lon", "lat"), None),
        P(("lon", "lat")),
        P(("lon", "lat"), None),
        P(),
        P(),
        P(),
        P("lat", "lon", None),
    )
    return jax.shard_map(
        on_device,
        mesh=mesh,
        in_specs=placed,
        out_specs=(P("lat", "lon", None), P(), P(), P(("lon", "lat"), None)),
        check_vma=False,
    )
```

```python
import math

import jax
import jax.numpy as jnp
from jax import lax
from jax.sharding import PartitionSpec as P

ID_BASE = 128


def shift_pairs(count, step, periodic):
    pairs = []
    for source in range(count):
        target = source + step
        if 0 <= target < count:
            pairs.append((source, target))
        elif periodic:
            pairs.append((source, target % count))
    return pairs


def widen(block, depth):
    lon_count = lax.axis_size("lon")
    lat_count = lax.axis_size("lat")
    west = lax.ppermute(block[:, -depth:], "lon", shift_pairs(lon_count, 1, True))
    east = lax.ppermute(block[:, :depth], "lon", shift_pairs(lon_count, -1, True))
    block = jnp.concatenate([west, block, east], axis=1)
    north = lax.ppermute(block[-depth:], "lat", shift_pairs(lat_count, 1, False))
    south = lax.ppermute(block[:depth], "lat", shift_pairs(lat_count, -1, False))
    return jnp.concatenate([north, block, south], axis=0)


def lat_mask(rows, margin, height):
    lat_index = lax.axis_index("lat")
    lat_count = lax.axis_size("lat")
    global_row = lat_index * height - margin + jnp.arange(rows, dtype=jnp.int32)
    return ((global_row >= 0) & (global_row < lat_count * height))[:, None, None]


def crop(field, margin):
    if margin == 0:
        return field
    return field[margin:-margin, margin:-margin]


def conv_valid(padded, kernel):
    return lax.conv_general_dilated(
        padded[None],
        kernel,
        (1, 1),
        "VALID",
        dimension_numbers=("NHWC", "HWIO", "NHWC"),
        preferred_element_type=jnp.float32,
    )[0]


def cube_steps():
    steps = []
    for axis in ("lon", "lat"):
        count = lax.axis_size(axis)
        bit = 1
        while bit < count:
            steps.append((axis, bit, [(i, i ^ bit) for i in range(count)]))
            bit *= 2
    return steps


def reduce_replicated(part, steps):
    for axis, bit, pairs in steps:
        half = part.shape[0] // 2
        mine = (lax.axis_index(axis) // bit) % 2
        keep = lax.dynamic_slice_in_dim(part, mine * half, half)
        give = lax.dynamic_slice_in_dim(part, (1 - mine) * half, half)
        got = lax.ppermute(give.astype(jnp.bfloat16), axis, pairs)
        part = keep + got.astype(jnp.float32)
    return part


def gather_replicated(part, steps):
    for axis, bit, pairs in reversed(steps):
        mine = (lax.axis_index(axis) // bit) % 2
        got = lax.ppermute(part, axis, pairs)
        first = jnp.where(mine == 0, part, got)
        second = jnp.where(mine == 0, got, part)
        part = jnp.concatenate([first, second])
    return part


def all_sum(pieces, scale, streams=3):
    lanes = pieces[0].shape[-1]
    flat = jnp.concatenate([piece.reshape(-1, lanes) for piece in pieces])
    steps = cube_steps()
    devices = 2 ** len(steps)
    unit = devices * 16
    total = flat.shape[0]
    units = -(-total // unit)
    flat = jnp.pad(flat, ((0, units * unit - total), (0, 0)))
    middle = steps[1:-1] if len(steps) > 2 else []
    outs = []
    begin = 0
    for stream in range(streams):
        count = units // streams + (1 if stream < units % streams else 0)
        if count == 0:
            continue
        shift = stream % len(middle) if middle else 0
        order = steps[:1] + middle[shift:] + middle[:shift] + steps[len(middle) + 1 :]
        if len(steps) <= 2:
            order = steps
        part = reduce_replicated(flat[begin : begin + count * unit], order)
        outs.append(gather_replicated((part * scale).astype(jnp.bfloat16), order))
        begin += count * unit
    return jnp.concatenate(outs)[:total]


def on_device(obs_rows, cell_ids, counts, w_embed, w_density, kernels, cotangent):
    lon_count = lax.axis_size("lon")
    lat_count = lax.axis_size("lat")
    devices = lon_count * lat_count
    height, tile_width, channels = cotangent.shape
    cell_count = height * tile_width
    slot_rows = obs_rows.shape[0] // devices
    feat_count = obs_rows.shape[1]
    layer_count = kernels.shape[0]
    margin = 2 * layer_count

    cot_wide = widen(cotangent, layer_count)

    live_mask = jnp.arange(slot_rows, dtype=jnp.int32)[None, :] < counts[0][:, None]
    slot_ids = cell_ids.reshape(devices, slot_rows)
    id_high = jnp.where(live_mask, slot_ids // ID_BASE, -1)
    id_low = jnp.where(live_mask, slot_ids % ID_BASE, -1)
    code = jnp.concatenate([id_high, id_low], axis=1).astype(jnp.bfloat16)
    code_rows = -(-2 * slot_rows // feat_count)
    code_pad = -(-code_rows // 16) * 16
    code = jnp.pad(code, ((0, 0), (0, code_rows * feat_count - 2 * slot_rows)))
    code = code.reshape(devices, code_rows, feat_count)
    code = jnp.pad(code, ((0, 0), (0, code_pad - code_rows), (0, 0)))
    packed = jnp.concatenate([obs_rows.reshape(devices, slot_rows, feat_count), code], axis=1)
    got = lax.all_to_all(packed, ("lon", "lat"), split_axis=0, concat_axis=0, tiled=True)
    got_rows = got[:, :slot_rows].reshape(devices * slot_rows, feat_count)
    got_code = got[:, slot_rows : slot_rows + code_rows].reshape(devices, code_rows * feat_count)
    got_code = got_code.astype(jnp.int32)
    got_ids = (got_code[:, :slot_rows] * ID_BASE + got_code[:, slot_rows : 2 * slot_rows]).reshape(-1)

    cell_iota = jnp.arange(cell_count, dtype=jnp.int32)
    onehot = (got_ids[:, None] == cell_iota[None, :]).astype(jnp.bfloat16)
    cell_sums = lax.dot_general(
        onehot, got_rows, (((0,), (0,)), ((), ())), preferred_element_type=jnp.float32
    )
    density = jnp.sum(onehot.astype(jnp.float32), axis=0)
    inv_root = lax.rsqrt(density + 1.0)
    features = (cell_sums * inv_root[:, None]).astype(jnp.bfloat16)
    start_act = (
        jnp.dot(features, w_embed, preferred_element_type=jnp.float32)
        + jnp.log1p(density)[:, None] * w_density.astype(jnp.float32)[None, :]
    )
    activation = start_act.astype(jnp.bfloat16).reshape(height, tile_width, channels)

    act = widen(activation, margin)
    stored_acts = [act]
    stored_pre = []
    for layer_index in range(layer_count):
        out_margin = margin - layer_index - 1
        preact = conv_valid(act, kernels[layer_index])
        act = (crop(act, 1).astype(jnp.float32) + jax.nn.silu(preact)).astype(jnp.bfloat16)
        act = jnp.where(lat_mask(act.shape[0], out_margin, height), act, jnp.zeros_like(act))
        stored_pre.append(preact)
        stored_acts.append(act)
    encoded = crop(act, margin - layer_count)

    grad_scale = 1.0 / math.sqrt(cell_count * devices)
    back = cot_wide
    grads = [None] * layer_count
    for layer_index in reversed(range(layer_count)):
        back_margin = layer_index + 1
        preact = crop(stored_pre[layer_index], margin - layer_index - 1 - back_margin)
        sigmoid_v = jax.nn.sigmoid(preact)
        slope = (
            back.astype(jnp.float32) * (sigmoid_v * (1.0 + preact * (1.0 - sigmoid_v)))
        ).astype(jnp.bfloat16)
        slope = jnp.where(lat_mask(slope.shape[0], back_margin, height), slope, jnp.zeros_like(slope))
        act_in = crop(stored_acts[layer_index], margin - layer_index - 1)
        tap_grad = lax.conv_general_dilated(
            act_in[None],
            crop(slope, back_margin)[:, :, None, :],
            (1, 1),
            "VALID",
            dimension_numbers=("CHWN", "HWIO", "HWNC"),
            preferred_element_type=jnp.float32,
        )
        flipped = jnp.transpose(kernels[layer_index][::-1, ::-1], (0, 1, 3, 2))
        spread = conv_valid(slope, flipped)
        back = lax.optimization_barrier(
            (crop(back, 1).astype(jnp.float32) + spread).astype(jnp.bfloat16)
        )
        grads[layer_index] = tap_grad
    back_flat = back.reshape(cell_count, channels)
    embed_grad = lax.dot_general(
        features, back_flat, (((0,), (0,)), ((), ())), preferred_element_type=jnp.float32
    )
    cell_grad = (
        lax.dot_general(
            back_flat, w_embed, (((1,), (1,)), ((), ())), preferred_element_type=jnp.float32
        )
        * inv_root[:, None]
    ).astype(jnp.bfloat16)
    picked = jnp.dot(onehot, cell_grad, preferred_element_type=jnp.float32).astype(jnp.bfloat16)
    grad_obs = lax.all_to_all(picked, ("lon", "lat"), split_axis=0, concat_axis=0, tiled=True)

    summed = all_sum(grads + [embed_grad], grad_scale)
    tap_rows_n = kernels.size // channels
    kernel_out = summed[:tap_rows_n].reshape(kernels.shape)
    embed_out = summed[tap_rows_n:]
    return (encoded, kernel_out, embed_out, grad_obs)


def solution(mesh):
    placed = (
        P(("lon", "lat"), None),
        P(("lon", "lat")),
        P(("lon", "lat"), None),
        P(),
        P(),
        P(),
        P("lat", "lon", None),
    )
    return jax.shard_map(
        on_device,
        mesh=mesh,
        in_specs=placed,
        out_specs=(P("lat", "lon", None), P(), P(), P(("lon", "lat"), None)),
        check_vma=False,
    )
```

```python
import math

import jax
import jax.numpy as jnp
from jax import lax
from jax.sharding import PartitionSpec as P

ID_BASE = 128


def shift_pairs(count, step, periodic):
    pairs = []
    for source in range(count):
        target = source + step
        if 0 <= target < count:
            pairs.append((source, target))
        elif periodic:
            pairs.append((source, target % count))
    return pairs


def widen(block, depth):
    lon_count = lax.axis_size("lon")
    lat_count = lax.axis_size("lat")
    west = lax.ppermute(block[:, -depth:], "lon", shift_pairs(lon_count, 1, True))
    east = lax.ppermute(block[:, :depth], "lon", shift_pairs(lon_count, -1, True))
    block = jnp.concatenate([west, block, east], axis=1)
    north = lax.ppermute(block[-depth:], "lat", shift_pairs(lat_count, 1, False))
    south = lax.ppermute(block[:depth], "lat", shift_pairs(lat_count, -1, False))
    return jnp.concatenate([north, block, south], axis=0)


def lat_mask(rows, margin, height):
    lat_index = lax.axis_index("lat")
    lat_count = lax.axis_size("lat")
    global_row = lat_index * height - margin + jnp.arange(rows, dtype=jnp.int32)
    return ((global_row >= 0) & (global_row < lat_count * height))[:, None, None]


def crop(field, margin):
    if margin == 0:
        return field
    return field[margin:-margin, margin:-margin]


def conv_valid(padded, kernel):
    return lax.conv_general_dilated(
        padded[None],
        kernel,
        (1, 1),
        "VALID",
        dimension_numbers=("NHWC", "HWIO", "NHWC"),
        preferred_element_type=jnp.float32,
    )[0]


def cube_steps():
    steps = []
    for axis in ("lon", "lat"):
        count = lax.axis_size(axis)
        bit = 1
        while bit < count:
            steps.append((axis, bit, [(i, i ^ bit) for i in range(count)]))
            bit *= 2
    return steps


def reduce_replicated(part, steps):
    for axis, bit, pairs in steps:
        half = part.shape[0] // 2
        mine = (lax.axis_index(axis) // bit) % 2
        keep = lax.dynamic_slice_in_dim(part, mine * half, half)
        give = lax.dynamic_slice_in_dim(part, (1 - mine) * half, half)
        got = lax.ppermute(give.astype(jnp.bfloat16), axis, pairs)
        part = keep + got.astype(jnp.float32)
    return part


def gather_replicated(part, steps):
    for axis, bit, pairs in reversed(steps):
        mine = (lax.axis_index(axis) // bit) % 2
        got = lax.ppermute(part, axis, pairs)
        first = jnp.where(mine == 0, part, got)
        second = jnp.where(mine == 0, got, part)
        part = jnp.concatenate([first, second])
    return part


def all_sum(pieces, scale, streams=6):
    lanes = pieces[0].shape[-1]
    flat = jnp.concatenate([piece.reshape(-1, lanes) for piece in pieces])
    steps = cube_steps()
    devices = 2 ** len(steps)
    unit = devices * 16
    total = flat.shape[0]
    units = -(-total // unit)
    flat = jnp.pad(flat, ((0, units * unit - total), (0, 0)))
    middle = steps[1:-1] if len(steps) > 2 else []
    outs = []
    begin = 0
    for stream in range(streams):
        count = units // streams + (1 if stream < units % streams else 0)
        if count == 0:
            continue
        shift = stream % len(middle) if middle else 0
        order = steps[:1] + middle[shift:] + middle[:shift] + steps[len(middle) + 1 :]
        if len(steps) <= 2:
            order = steps
        part = reduce_replicated(flat[begin : begin + count * unit], order)
        outs.append(gather_replicated((part * scale).astype(jnp.bfloat16), order))
        begin += count * unit
    return jnp.concatenate(outs)[:total]


def on_device(obs_rows, cell_ids, counts, w_embed, w_density, kernels, cotangent):
    lon_count = lax.axis_size("lon")
    lat_count = lax.axis_size("lat")
    devices = lon_count * lat_count
    height, tile_width, channels = cotangent.shape
    cell_count = height * tile_width
    slot_rows = obs_rows.shape[0] // devices
    feat_count = obs_rows.shape[1]
    layer_count = kernels.shape[0]
    margin = 2 * layer_count

    cot_wide = widen(cotangent, layer_count)

    live_mask = jnp.arange(slot_rows, dtype=jnp.int32)[None, :] < counts[0][:, None]
    slot_ids = cell_ids.reshape(devices, slot_rows)
    id_high = jnp.where(live_mask, slot_ids // ID_BASE, -1)
    id_low = jnp.where(live_mask, slot_ids % ID_BASE, -1)
    code = jnp.concatenate([id_high, id_low], axis=1).astype(jnp.bfloat16)
    code_rows = -(-2 * slot_rows // feat_count)
    code_pad = -(-code_rows // 16) * 16
    code = jnp.pad(code, ((0, 0), (0, code_rows * feat_count - 2 * slot_rows)))
    code = code.reshape(devices, code_rows, feat_count)
    code = jnp.pad(code, ((0, 0), (0, code_pad - code_rows), (0, 0)))
    packed = jnp.concatenate([obs_rows.reshape(devices, slot_rows, feat_count), code], axis=1)
    got = lax.all_to_all(packed, ("lon", "lat"), split_axis=0, concat_axis=0, tiled=True)
    got_rows = got[:, :slot_rows].reshape(devices * slot_rows, feat_count)
    got_code = got[:, slot_rows : slot_rows + code_rows].reshape(devices, code_rows * feat_count)
    got_code = got_code.astype(jnp.int32)
    got_ids = (got_code[:, :slot_rows] * ID_BASE + got_code[:, slot_rows : 2 * slot_rows]).reshape(-1)

    cell_iota = jnp.arange(cell_count, dtype=jnp.int32)
    onehot = (got_ids[:, None] == cell_iota[None, :]).astype(jnp.bfloat16)
    cell_sums = lax.dot_general(
        onehot, got_rows, (((0,), (0,)), ((), ())), preferred_element_type=jnp.float32
    )
    density = jnp.sum(onehot.astype(jnp.float32), axis=0)
    inv_root = lax.rsqrt(density + 1.0)
    features = (cell_sums * inv_root[:, None]).astype(jnp.bfloat16)
    start_act = (
        jnp.dot(features, w_embed, preferred_element_type=jnp.float32)
        + jnp.log1p(density)[:, None] * w_density.astype(jnp.float32)[None, :]
    )
    activation = start_act.astype(jnp.bfloat16).reshape(height, tile_width, channels)

    act = widen(activation, margin)
    stored_acts = [act]
    stored_pre = []
    for layer_index in range(layer_count):
        out_margin = margin - layer_index - 1
        preact = conv_valid(act, kernels[layer_index])
        act = (crop(act, 1).astype(jnp.float32) + jax.nn.silu(preact)).astype(jnp.bfloat16)
        act = jnp.where(lat_mask(act.shape[0], out_margin, height), act, jnp.zeros_like(act))
        stored_pre.append(preact)
        stored_acts.append(act)
    encoded = crop(act, margin - layer_count)

    grad_scale = 1.0 / math.sqrt(cell_count * devices)
    back = cot_wide
    grads = [None] * layer_count
    for layer_index in reversed(range(layer_count)):
        back_margin = layer_index + 1
        preact = crop(stored_pre[layer_index], margin - layer_index - 1 - back_margin)
        sigmoid_v = jax.nn.sigmoid(preact)
        slope = (
            back.astype(jnp.float32) * (sigmoid_v * (1.0 + preact * (1.0 - sigmoid_v)))
        ).astype(jnp.bfloat16)
        slope = jnp.where(lat_mask(slope.shape[0], back_margin, height), slope, jnp.zeros_like(slope))
        slope_flat = crop(slope, back_margin).reshape(cell_count, channels)
        act_in = crop(stored_acts[layer_index], margin - layer_index - 1)
        tap_rows = []
        for row_off in range(3):
            tap_cols = []
            for col_off in range(3):
                window = act_in[row_off : row_off + height, col_off : col_off + tile_width].reshape(
                    cell_count, channels
                )
                tap_cols.append(
                    lax.dot_general(
                        window,
                        slope_flat,
                        (((0,), (0,)), ((), ())),
                        preferred_element_type=jnp.float32,
                    )
                )
            tap_rows.append(jnp.stack(tap_cols))
        tap_grad = jnp.stack(tap_rows)
        flipped = jnp.transpose(kernels[layer_index][::-1, ::-1], (0, 1, 3, 2))
        spread = conv_valid(slope, flipped)
        back = lax.optimization_barrier(
            (crop(back, 1).astype(jnp.float32) + spread).astype(jnp.bfloat16)
        )
        grads[layer_index] = tap_grad
    back_flat = back.reshape(cell_count, channels)
    embed_grad = lax.dot_general(
        features, back_flat, (((0,), (0,)), ((), ())), preferred_element_type=jnp.float32
    )
    cell_grad = (
        lax.dot_general(
            back_flat, w_embed, (((1,), (1,)), ((), ())), preferred_element_type=jnp.float32
        )
        * inv_root[:, None]
    ).astype(jnp.bfloat16)
    picked = jnp.dot(onehot, cell_grad, preferred_element_type=jnp.float32).astype(jnp.bfloat16)
    grad_obs = lax.all_to_all(picked, ("lon", "lat"), split_axis=0, concat_axis=0, tiled=True)

    summed = all_sum(grads + [embed_grad], grad_scale)
    tap_rows_n = kernels.size // channels
    kernel_out = summed[:tap_rows_n].reshape(kernels.shape)
    embed_out = summed[tap_rows_n:]
    return (encoded, kernel_out, embed_out, grad_obs)


def solution(mesh):
    placed = (
        P(("lon", "lat"), None),
        P(("lon", "lat")),
        P(("lon", "lat"), None),
        P(),
        P(),
        P(),
        P("lat", "lon", None),
    )
    return jax.shard_map(
        on_device,
        mesh=mesh,
        in_specs=placed,
        out_specs=(P("lat", "lon", None), P(), P(), P(("lon", "lat"), None)),
        check_vma=False,
    )
```

```python
import math

import jax
import jax.numpy as jnp
from jax import lax
from jax.sharding import PartitionSpec as P

ID_BASE = 128


def grid_pairs(lon_step, lat_step):
    lon_count = lax.axis_size("lon")
    lat_count = lax.axis_size("lat")
    pairs = []
    for lon_source in range(lon_count):
        for lat_source in range(lat_count):
            lat_target = lat_source + lat_step
            if 0 <= lat_target < lat_count:
                lon_target = (lon_source + lon_step) % lon_count
                pairs.append((lon_source * lat_count + lat_source, lon_target * lat_count + lat_target))
    return pairs


def widen(block, depth):
    def moved(piece, lon_step, lat_step):
        return lax.ppermute(piece, ("lon", "lat"), grid_pairs(lon_step, lat_step))

    top = block[-depth:]
    bottom = block[:depth]
    north = jnp.concatenate(
        [moved(top[:, -depth:], 1, 1), moved(top, 0, 1), moved(top[:, :depth], -1, 1)], axis=1
    )
    middle = jnp.concatenate(
        [moved(block[:, -depth:], 1, 0), block, moved(block[:, :depth], -1, 0)], axis=1
    )
    south = jnp.concatenate(
        [moved(bottom[:, -depth:], 1, -1), moved(bottom, 0, -1), moved(bottom[:, :depth], -1, -1)],
        axis=1,
    )
    return jnp.concatenate([north, middle, south], axis=0)


def lat_mask(rows, margin, height):
    lat_index = lax.axis_index("lat")
    lat_count = lax.axis_size("lat")
    global_row = lat_index * height - margin + jnp.arange(rows, dtype=jnp.int32)
    return ((global_row >= 0) & (global_row < lat_count * height))[:, None, None]


def crop(field, margin):
    if margin == 0:
        return field
    return field[margin:-margin, margin:-margin]


def conv_valid(padded, kernel):
    return lax.conv_general_dilated(
        padded[None],
        kernel,
        (1, 1),
        "VALID",
        dimension_numbers=("NHWC", "HWIO", "NHWC"),
        preferred_element_type=jnp.float32,
    )[0]


def cube_steps():
    steps = []
    for axis in ("lon", "lat"):
        count = lax.axis_size(axis)
        bit = 1
        while bit < count:
            steps.append((axis, bit, [(i, i ^ bit) for i in range(count)]))
            bit *= 2
    return steps


def reduce_replicated(part, steps):
    for axis, bit, pairs in steps:
        half = part.shape[0] // 2
        mine = (lax.axis_index(axis) // bit) % 2
        keep = lax.dynamic_slice_in_dim(part, mine * half, half)
        give = lax.dynamic_slice_in_dim(part, (1 - mine) * half, half)
        got = lax.ppermute(give.astype(jnp.bfloat16), axis, pairs)
        part = keep + got.astype(jnp.float32)
    return part


def gather_replicated(part, steps):
    for axis, bit, pairs in reversed(steps):
        mine = (lax.axis_index(axis) // bit) % 2
        got = lax.ppermute(part, axis, pairs)
        first = jnp.where(mine == 0, part, got)
        second = jnp.where(mine == 0, got, part)
        part = jnp.concatenate([first, second])
    return part


def all_sum(pieces, scale, streams=3):
    lanes = pieces[0].shape[-1]
    flat = jnp.concatenate([piece.reshape(-1, lanes) for piece in pieces])
    steps = cube_steps()
    devices = 2 ** len(steps)
    unit = devices * 16
    total = flat.shape[0]
    units = -(-total // unit)
    flat = jnp.pad(flat, ((0, units * unit - total), (0, 0)))
    middle = steps[1:-1] if len(steps) > 2 else []
    outs = []
    begin = 0
    for stream in range(streams):
        count = units // streams + (1 if stream < units % streams else 0)
        if count == 0:
            continue
        shift = stream % len(middle) if middle else 0
        order = steps[:1] + middle[shift:] + middle[:shift] + steps[len(middle) + 1 :]
        if len(steps) <= 2:
            order = steps
        part = reduce_replicated(flat[begin : begin + count * unit], order)
        outs.append(gather_replicated((part * scale).astype(jnp.bfloat16), order))
        begin += count * unit
    return jnp.concatenate(outs)[:total]


def on_device(obs_rows, cell_ids, counts, w_embed, w_density, kernels, cotangent):
    lon_count = lax.axis_size("lon")
    lat_count = lax.axis_size("lat")
    devices = lon_count * lat_count
    height, tile_width, channels = cotangent.shape
    cell_count = height * tile_width
    slot_rows = obs_rows.shape[0] // devices
    feat_count = obs_rows.shape[1]
    layer_count = kernels.shape[0]
    margin = 2 * layer_count

    cot_wide = widen(cotangent, layer_count)

    live_mask = jnp.arange(slot_rows, dtype=jnp.int32)[None, :] < counts[0][:, None]
    slot_ids = cell_ids.reshape(devices, slot_rows)
    id_high = jnp.where(live_mask, slot_ids // ID_BASE, -1)
    id_low = jnp.where(live_mask, slot_ids % ID_BASE, -1)
    code = jnp.concatenate([id_high, id_low], axis=1).astype(jnp.bfloat16)
    code_rows = -(-2 * slot_rows // feat_count)
    code_pad = -(-code_rows // 16) * 16
    code = jnp.pad(code, ((0, 0), (0, code_rows * feat_count - 2 * slot_rows)))
    code = code.reshape(devices, code_rows, feat_count)
    code = jnp.pad(code, ((0, 0), (0, code_pad - code_rows), (0, 0)))
    packed = jnp.concatenate([obs_rows.reshape(devices, slot_rows, feat_count), code], axis=1)
    got = lax.all_to_all(packed, ("lon", "lat"), split_axis=0, concat_axis=0, tiled=True)
    got_rows = got[:, :slot_rows].reshape(devices * slot_rows, feat_count)
    got_code = got[:, slot_rows : slot_rows + code_rows].reshape(devices, code_rows * feat_count)
    got_code = got_code.astype(jnp.int32)
    got_ids = (got_code[:, :slot_rows] * ID_BASE + got_code[:, slot_rows : 2 * slot_rows]).reshape(-1)

    cell_iota = jnp.arange(cell_count, dtype=jnp.int32)
    onehot = (got_ids[:, None] == cell_iota[None, :]).astype(jnp.bfloat16)
    cell_sums = lax.dot_general(
        onehot, got_rows, (((0,), (0,)), ((), ())), preferred_element_type=jnp.float32
    )
    density = jnp.sum(onehot.astype(jnp.float32), axis=0)
    inv_root = lax.rsqrt(density + 1.0)
    features = (cell_sums * inv_root[:, None]).astype(jnp.bfloat16)
    start_act = (
        jnp.dot(features, w_embed, preferred_element_type=jnp.float32)
        + jnp.log1p(density)[:, None] * w_density.astype(jnp.float32)[None, :]
    )
    activation = start_act.astype(jnp.bfloat16).reshape(height, tile_width, channels)

    act = widen(activation, margin)
    stored_acts = [act]
    stored_pre = []
    for layer_index in range(layer_count):
        out_margin = margin - layer_index - 1
        preact = conv_valid(act, kernels[layer_index])
        act = (crop(act, 1).astype(jnp.float32) + jax.nn.silu(preact)).astype(jnp.bfloat16)
        act = jnp.where(lat_mask(act.shape[0], out_margin, height), act, jnp.zeros_like(act))
        stored_pre.append(preact)
        stored_acts.append(act)
    encoded = crop(act, margin - layer_count)

    grad_scale = 1.0 / math.sqrt(cell_count * devices)
    back = cot_wide
    grads = [None] * layer_count
    for layer_index in reversed(range(layer_count)):
        back_margin = layer_index + 1
        preact = crop(stored_pre[layer_index], margin - layer_index - 1 - back_margin)
        sigmoid_v = jax.nn.sigmoid(preact)
        slope = (
            back.astype(jnp.float32) * (sigmoid_v * (1.0 + preact * (1.0 - sigmoid_v)))
        ).astype(jnp.bfloat16)
        slope = jnp.where(lat_mask(slope.shape[0], back_margin, height), slope, jnp.zeros_like(slope))
        slope_flat = crop(slope, back_margin).reshape(cell_count, channels)
        act_in = crop(stored_acts[layer_index], margin - layer_index - 1)
        tap_rows = []
        for row_off in range(3):
            tap_cols = []
            for col_off in range(3):
                window = act_in[row_off : row_off + height, col_off : col_off + tile_width].reshape(
                    cell_count, channels
                )
                tap_cols.append(
                    lax.dot_general(
                        window,
                        slope_flat,
                        (((0,), (0,)), ((), ())),
                        preferred_element_type=jnp.float32,
                    )
                )
            tap_rows.append(jnp.stack(tap_cols))
        tap_grad = jnp.stack(tap_rows)
        flipped = jnp.transpose(kernels[layer_index][::-1, ::-1], (0, 1, 3, 2))
        spread = conv_valid(slope, flipped)
        back = lax.optimization_barrier(
            (crop(back, 1).astype(jnp.float32) + spread).astype(jnp.bfloat16)
        )
        grads[layer_index] = tap_grad
    back_flat = back.reshape(cell_count, channels)
    embed_grad = lax.dot_general(
        features, back_flat, (((0,), (0,)), ((), ())), preferred_element_type=jnp.float32
    )
    cell_grad = (
        lax.dot_general(
            back_flat, w_embed, (((1,), (1,)), ((), ())), preferred_element_type=jnp.float32
        )
        * inv_root[:, None]
    ).astype(jnp.bfloat16)
    picked = jnp.dot(onehot, cell_grad, preferred_element_type=jnp.float32).astype(jnp.bfloat16)
    grad_obs = lax.all_to_all(picked, ("lon", "lat"), split_axis=0, concat_axis=0, tiled=True)

    summed = all_sum(grads + [embed_grad], grad_scale)
    tap_rows_n = kernels.size // channels
    kernel_out = summed[:tap_rows_n].reshape(kernels.shape)
    embed_out = summed[tap_rows_n:]
    return (encoded, kernel_out, embed_out, grad_obs)


def solution(mesh):
    placed = (
        P(("lon", "lat"), None),
        P(("lon", "lat")),
        P(("lon", "lat"), None),
        P(),
        P(),
        P(),
        P("lat", "lon", None),
    )
    return jax.shard_map(
        on_device,
        mesh=mesh,
        in_specs=placed,
        out_specs=(P("lat", "lon", None), P(), P(), P(("lon", "lat"), None)),
        check_vma=False,
    )
```

```python
import math

import jax
import jax.numpy as jnp
from jax import lax
from jax.sharding import PartitionSpec as P

ID_BASE = 128


def shift_pairs(count, step, periodic):
    pairs = []
    for source in range(count):
        target = source + step
        if 0 <= target < count:
            pairs.append((source, target))
        elif periodic:
            pairs.append((source, target % count))
    return pairs


def widen(block, depth):
    lon_count = lax.axis_size("lon")
    lat_count = lax.axis_size("lat")
    west = lax.ppermute(block[:, -depth:], "lon", shift_pairs(lon_count, 1, True))
    east = lax.ppermute(block[:, :depth], "lon", shift_pairs(lon_count, -1, True))
    block = jnp.concatenate([west, block, east], axis=1)
    north = lax.ppermute(block[-depth:], "lat", shift_pairs(lat_count, 1, False))
    south = lax.ppermute(block[:depth], "lat", shift_pairs(lat_count, -1, False))
    return jnp.concatenate([north, block, south], axis=0)


def lat_mask(rows, margin, height):
    lat_index = lax.axis_index("lat")
    lat_count = lax.axis_size("lat")
    global_row = lat_index * height - margin + jnp.arange(rows, dtype=jnp.int32)
    return ((global_row >= 0) & (global_row < lat_count * height))[:, None, None]


def crop(field, margin):
    if margin == 0:
        return field
    return field[margin:-margin, margin:-margin]


def conv_valid(padded, kernel):
    return lax.conv_general_dilated(
        padded[None],
        kernel,
        (1, 1),
        "VALID",
        dimension_numbers=("NHWC", "HWIO", "NHWC"),
        preferred_element_type=jnp.float32,
    )[0]


def cube_steps():
    steps = []
    for axis in ("lon", "lat"):
        count = lax.axis_size(axis)
        bit = 1
        while bit < count:
            steps.append((axis, bit, [(i, i ^ bit) for i in range(count)]))
            bit *= 2
    return steps


def reduce_replicated(part, steps):
    for axis, bit, pairs in steps:
        half = part.shape[0] // 2
        mine = (lax.axis_index(axis) // bit) % 2
        keep = lax.dynamic_slice_in_dim(part, mine * half, half)
        give = lax.dynamic_slice_in_dim(part, (1 - mine) * half, half)
        got = lax.ppermute(give.astype(jnp.bfloat16), axis, pairs)
        part = keep + got.astype(jnp.float32)
    return part


def gather_replicated(part, steps):
    for axis, bit, pairs in reversed(steps):
        mine = (lax.axis_index(axis) // bit) % 2
        got = lax.ppermute(part, axis, pairs)
        first = jnp.where(mine == 0, part, got)
        second = jnp.where(mine == 0, got, part)
        part = jnp.concatenate([first, second])
    return part


def all_sum(pieces, scale, streams=3):
    lanes = pieces[0].shape[-1]
    flat = jnp.concatenate([piece.reshape(-1, lanes) for piece in pieces])
    steps = cube_steps()
    devices = 2 ** len(steps)
    unit = devices * 16
    total = flat.shape[0]
    units = -(-total // unit)
    flat = jnp.pad(flat, ((0, units * unit - total), (0, 0)))
    middle = steps[1:-1] if len(steps) > 2 else []
    outs = []
    begin = 0
    for stream in range(streams):
        count = units // streams + (1 if stream < units % streams else 0)
        if count == 0:
            continue
        shift = stream % len(middle) if middle else 0
        order = steps[:1] + middle[shift:] + middle[:shift] + steps[len(middle) + 1 :]
        if len(steps) <= 2:
            order = steps
        part = reduce_replicated(flat[begin : begin + count * unit], order)
        outs.append(gather_replicated((part * scale).astype(jnp.bfloat16), order))
        begin += count * unit
    return jnp.concatenate(outs)[:total]


def on_device(obs_rows, cell_ids, counts, w_embed, w_density, kernels, cotangent):
    lon_count = lax.axis_size("lon")
    lat_count = lax.axis_size("lat")
    devices = lon_count * lat_count
    height, tile_width, channels = cotangent.shape
    cell_count = height * tile_width
    slot_rows = obs_rows.shape[0] // devices
    feat_count = obs_rows.shape[1]
    layer_count = kernels.shape[0]
    margin = 2 * layer_count

    live_mask = jnp.arange(slot_rows, dtype=jnp.int32)[None, :] < counts[0][:, None]
    slot_ids = cell_ids.reshape(devices, slot_rows)
    id_high = jnp.where(live_mask, slot_ids // ID_BASE, -1)
    id_low = jnp.where(live_mask, slot_ids % ID_BASE, -1)
    code = jnp.concatenate([id_high, id_low], axis=1).astype(jnp.bfloat16)
    code_rows = -(-2 * slot_rows // feat_count)
    code_pad = -(-code_rows // 16) * 16
    code = jnp.pad(code, ((0, 0), (0, code_rows * feat_count - 2 * slot_rows)))
    code = code.reshape(devices, code_rows, feat_count)
    code = jnp.pad(code, ((0, 0), (0, code_pad - code_rows), (0, 0)))
    packed = jnp.concatenate([obs_rows.reshape(devices, slot_rows, feat_count), code], axis=1)
    got = lax.all_to_all(packed, ("lon", "lat"), split_axis=0, concat_axis=0, tiled=True)
    got_rows = got[:, :slot_rows].reshape(devices * slot_rows, feat_count)
    got_code = got[:, slot_rows : slot_rows + code_rows].reshape(devices, code_rows * feat_count)
    got_code = got_code.astype(jnp.int32)
    got_ids = (got_code[:, :slot_rows] * ID_BASE + got_code[:, slot_rows : 2 * slot_rows]).reshape(-1)

    cell_iota = jnp.arange(cell_count, dtype=jnp.int32)
    onehot = (got_ids[:, None] == cell_iota[None, :]).astype(jnp.bfloat16)
    cell_sums = lax.dot_general(
        onehot, got_rows, (((0,), (0,)), ((), ())), preferred_element_type=jnp.float32
    )
    density = jnp.sum(onehot.astype(jnp.float32), axis=0)
    inv_root = lax.rsqrt(density + 1.0)
    features = (cell_sums * inv_root[:, None]).astype(jnp.bfloat16)
    start_act = (
        jnp.dot(features, w_embed, preferred_element_type=jnp.float32)
        + jnp.log1p(density)[:, None] * w_density.astype(jnp.float32)[None, :]
    )
    activation = start_act.astype(jnp.bfloat16).reshape(height, tile_width, channels)

    wide = widen(jnp.concatenate([activation, cotangent], axis=-1), margin)
    act = wide[..., :channels]
    cot_wide = crop(wide[..., channels:], margin - layer_count)
    stored_acts = [act]
    stored_pre = []
    for layer_index in range(layer_count):
        out_margin = margin - layer_index - 1
        preact = conv_valid(act, kernels[layer_index])
        act = (crop(act, 1).astype(jnp.float32) + jax.nn.silu(preact)).astype(jnp.bfloat16)
        act = jnp.where(lat_mask(act.shape[0], out_margin, height), act, jnp.zeros_like(act))
        stored_pre.append(preact)
        stored_acts.append(act)
    encoded = crop(act, margin - layer_count)

    grad_scale = 1.0 / math.sqrt(cell_count * devices)
    back = cot_wide
    grads = [None] * layer_count
    for layer_index in reversed(range(layer_count)):
        back_margin = layer_index + 1
        preact = crop(stored_pre[layer_index], margin - layer_index - 1 - back_margin)
        sigmoid_v = jax.nn.sigmoid(preact)
        slope = (
            back.astype(jnp.float32) * (sigmoid_v * (1.0 + preact * (1.0 - sigmoid_v)))
        ).astype(jnp.bfloat16)
        slope = jnp.where(lat_mask(slope.shape[0], back_margin, height), slope, jnp.zeros_like(slope))
        slope_flat = crop(slope, back_margin).reshape(cell_count, channels)
        act_in = crop(stored_acts[layer_index], margin - layer_index - 1)
        tap_rows = []
        for row_off in range(3):
            tap_cols = []
            for col_off in range(3):
                window = act_in[row_off : row_off + height, col_off : col_off + tile_width].reshape(
                    cell_count, channels
                )
                tap_cols.append(
                    lax.dot_general(
                        window,
                        slope_flat,
                        (((0,), (0,)), ((), ())),
                        preferred_element_type=jnp.float32,
                    )
                )
            tap_rows.append(jnp.stack(tap_cols))
        tap_grad = jnp.stack(tap_rows)
        flipped = jnp.transpose(kernels[layer_index][::-1, ::-1], (0, 1, 3, 2))
        spread = conv_valid(slope, flipped)
        back = lax.optimization_barrier(
            (crop(back, 1).astype(jnp.float32) + spread).astype(jnp.bfloat16)
        )
        grads[layer_index] = tap_grad
    back_flat = back.reshape(cell_count, channels)
    embed_grad = lax.dot_general(
        features, back_flat, (((0,), (0,)), ((), ())), preferred_element_type=jnp.float32
    )
    cell_grad = (
        lax.dot_general(
            back_flat, w_embed, (((1,), (1,)), ((), ())), preferred_element_type=jnp.float32
        )
        * inv_root[:, None]
    ).astype(jnp.bfloat16)
    picked = jnp.dot(onehot, cell_grad, preferred_element_type=jnp.float32).astype(jnp.bfloat16)
    grad_obs = lax.all_to_all(picked, ("lon", "lat"), split_axis=0, concat_axis=0, tiled=True)

    summed = all_sum(grads + [embed_grad], grad_scale)
    tap_rows_n = kernels.size // channels
    kernel_out = summed[:tap_rows_n].reshape(kernels.shape)
    embed_out = summed[tap_rows_n:]
    return (encoded, kernel_out, embed_out, grad_obs)


def solution(mesh):
    placed = (
        P(("lon", "lat"), None),
        P(("lon", "lat")),
        P(("lon", "lat"), None),
        P(),
        P(),
        P(),
        P("lat", "lon", None),
    )
    return jax.shard_map(
        on_device,
        mesh=mesh,
        in_specs=placed,
        out_specs=(P("lat", "lon", None), P(), P(), P(("lon", "lat"), None)),
        check_vma=False,
    )
```

```python
import math

import jax
import jax.numpy as jnp
from jax import lax
from jax.sharding import PartitionSpec as P

ID_BASE = 128


def shift_pairs(count, step, periodic):
    pairs = []
    for source in range(count):
        target = source + step
        if 0 <= target < count:
            pairs.append((source, target))
        elif periodic:
            pairs.append((source, target % count))
    return pairs


def widen(block, depth):
    lon_count = lax.axis_size("lon")
    lat_count = lax.axis_size("lat")
    west = lax.ppermute(block[:, -depth:], "lon", shift_pairs(lon_count, 1, True))
    east = lax.ppermute(block[:, :depth], "lon", shift_pairs(lon_count, -1, True))
    block = jnp.concatenate([west, block, east], axis=1)
    north = lax.ppermute(block[-depth:], "lat", shift_pairs(lat_count, 1, False))
    south = lax.ppermute(block[:depth], "lat", shift_pairs(lat_count, -1, False))
    return jnp.concatenate([north, block, south], axis=0)


def lat_mask(rows, margin, height):
    lat_index = lax.axis_index("lat")
    lat_count = lax.axis_size("lat")
    global_row = lat_index * height - margin + jnp.arange(rows, dtype=jnp.int32)
    return ((global_row >= 0) & (global_row < lat_count * height))[:, None, None]


def crop(field, margin):
    if margin == 0:
        return field
    return field[margin:-margin, margin:-margin]


def conv_valid(padded, kernel):
    return lax.conv_general_dilated(
        padded[None],
        kernel,
        (1, 1),
        "VALID",
        dimension_numbers=("NHWC", "HWIO", "NHWC"),
        preferred_element_type=jnp.float32,
    )[0]


def cube_steps():
    steps = []
    for axis in ("lon", "lat"):
        count = lax.axis_size(axis)
        bit = 1
        while bit < count:
            steps.append((axis, bit, [(i, i ^ bit) for i in range(count)]))
            bit *= 2
    return steps


def reduce_replicated(part, steps):
    for axis, bit, pairs in steps:
        half = part.shape[0] // 2
        mine = (lax.axis_index(axis) // bit) % 2
        keep = lax.dynamic_slice_in_dim(part, mine * half, half)
        give = lax.dynamic_slice_in_dim(part, (1 - mine) * half, half)
        got = lax.ppermute(give.astype(jnp.bfloat16), axis, pairs)
        part = keep + got.astype(jnp.float32)
    return part


def gather_replicated(part, steps):
    for axis, bit, pairs in reversed(steps):
        mine = (lax.axis_index(axis) // bit) % 2
        got = lax.ppermute(part, axis, pairs)
        first = jnp.where(mine == 0, part, got)
        second = jnp.where(mine == 0, got, part)
        part = jnp.concatenate([first, second])
    return part


def all_sum(pieces, scale, streams=3):
    lanes = pieces[0].shape[-1]
    flat = jnp.concatenate([piece.reshape(-1, lanes) for piece in pieces])
    total = flat.shape[0]
    steps = cube_steps()
    if len(steps) < 3:
        unit = (2 ** len(steps)) * 16
        flat = jnp.pad(flat, ((0, -(-total // unit) * unit - total), (0, 0)))
        part = reduce_replicated(flat, steps)
        return gather_replicated((part * scale).astype(jnp.bfloat16), steps)[:total]
    first, middle, last = steps[:1], steps[1:-1], steps[-1:]
    unit = (2 ** len(middle)) * 32
    units = -(-total // (2 * unit))
    flat = jnp.pad(flat, ((0, 2 * units * unit - total), (0, 0)))
    part = reduce_replicated(flat, first)
    orders = []
    segs = []
    begin = 0
    for stream in range(streams):
        count = units // streams + (1 if stream < units % streams else 0)
        if count == 0:
            continue
        shift = stream % len(middle)
        order = middle[shift:] + middle[:shift]
        segs.append(reduce_replicated(part[begin : begin + count * unit], order))
        orders.append(order)
        begin += count * unit
    seg_rows = [seg.shape[0] for seg in segs]
    part = reduce_replicated(jnp.concatenate(segs), last)
    part = gather_replicated((part * scale).astype(jnp.bfloat16), last)
    outs = []
    begin = 0
    for order, rows in zip(orders, seg_rows):
        outs.append(gather_replicated(part[begin : begin + rows], order))
        begin += rows
    return gather_replicated(jnp.concatenate(outs), first)[:total]


def on_device(obs_rows, cell_ids, counts, w_embed, w_density, kernels, cotangent):
    lon_count = lax.axis_size("lon")
    lat_count = lax.axis_size("lat")
    devices = lon_count * lat_count
    height, tile_width, channels = cotangent.shape
    cell_count = height * tile_width
    slot_rows = obs_rows.shape[0] // devices
    feat_count = obs_rows.shape[1]
    layer_count = kernels.shape[0]
    margin = 2 * layer_count

    cot_wide = widen(cotangent, layer_count)

    live_mask = jnp.arange(slot_rows, dtype=jnp.int32)[None, :] < counts[0][:, None]
    slot_ids = cell_ids.reshape(devices, slot_rows)
    id_high = jnp.where(live_mask, slot_ids // ID_BASE, -1)
    id_low = jnp.where(live_mask, slot_ids % ID_BASE, -1)
    code = jnp.concatenate([id_high, id_low], axis=1).astype(jnp.bfloat16)
    code_rows = -(-2 * slot_rows // feat_count)
    code_pad = -(-code_rows // 16) * 16
    code = jnp.pad(code, ((0, 0), (0, code_rows * feat_count - 2 * slot_rows)))
    code = code.reshape(devices, code_rows, feat_count)
    code = jnp.pad(code, ((0, 0), (0, code_pad - code_rows), (0, 0)))
    packed = jnp.concatenate([obs_rows.reshape(devices, slot_rows, feat_count), code], axis=1)
    got = lax.all_to_all(packed, ("lon", "lat"), split_axis=0, concat_axis=0, tiled=True)
    got_rows = got[:, :slot_rows].reshape(devices * slot_rows, feat_count)
    got_code = got[:, slot_rows : slot_rows + code_rows].reshape(devices, code_rows * feat_count)
    got_code = got_code.astype(jnp.int32)
    got_ids = (got_code[:, :slot_rows] * ID_BASE + got_code[:, slot_rows : 2 * slot_rows]).reshape(-1)

    cell_iota = jnp.arange(cell_count, dtype=jnp.int32)
    onehot = (got_ids[:, None] == cell_iota[None, :]).astype(jnp.bfloat16)
    cell_sums = lax.dot_general(
        onehot, got_rows, (((0,), (0,)), ((), ())), preferred_element_type=jnp.float32
    )
    density = jnp.sum(onehot.astype(jnp.float32), axis=0)
    inv_root = lax.rsqrt(density + 1.0)
    features = (cell_sums * inv_root[:, None]).astype(jnp.bfloat16)
    start_act = (
        jnp.dot(features, w_embed, preferred_element_type=jnp.float32)
        + jnp.log1p(density)[:, None] * w_density.astype(jnp.float32)[None, :]
    )
    activation = start_act.astype(jnp.bfloat16).reshape(height, tile_width, channels)

    act = widen(activation, margin)
    stored_acts = [act]
    stored_pre = []
    for layer_index in range(layer_count):
        out_margin = margin - layer_index - 1
        preact = conv_valid(act, kernels[layer_index])
        act = (crop(act, 1).astype(jnp.float32) + jax.nn.silu(preact)).astype(jnp.bfloat16)
        act = jnp.where(lat_mask(act.shape[0], out_margin, height), act, jnp.zeros_like(act))
        stored_pre.append(preact)
        stored_acts.append(act)
    encoded = crop(act, margin - layer_count)

    grad_scale = 1.0 / math.sqrt(cell_count * devices)
    back = cot_wide
    grads = [None] * layer_count
    for layer_index in reversed(range(layer_count)):
        back_margin = layer_index + 1
        preact = crop(stored_pre[layer_index], margin - layer_index - 1 - back_margin)
        sigmoid_v = jax.nn.sigmoid(preact)
        slope = (
            back.astype(jnp.float32) * (sigmoid_v * (1.0 + preact * (1.0 - sigmoid_v)))
        ).astype(jnp.bfloat16)
        slope = jnp.where(lat_mask(slope.shape[0], back_margin, height), slope, jnp.zeros_like(slope))
        slope_flat = crop(slope, back_margin).reshape(cell_count, channels)
        act_in = crop(stored_acts[layer_index], margin - layer_index - 1)
        tap_rows = []
        for row_off in range(3):
            tap_cols = []
            for col_off in range(3):
                window = act_in[row_off : row_off + height, col_off : col_off + tile_width].reshape(
                    cell_count, channels
                )
                tap_cols.append(
                    lax.dot_general(
                        window,
                        slope_flat,
                        (((0,), (0,)), ((), ())),
                        preferred_element_type=jnp.float32,
                    )
                )
            tap_rows.append(jnp.stack(tap_cols))
        tap_grad = jnp.stack(tap_rows)
        flipped = jnp.transpose(kernels[layer_index][::-1, ::-1], (0, 1, 3, 2))
        spread = conv_valid(slope, flipped)
        back = lax.optimization_barrier(
            (crop(back, 1).astype(jnp.float32) + spread).astype(jnp.bfloat16)
        )
        grads[layer_index] = tap_grad
    back_flat = back.reshape(cell_count, channels)
    embed_grad = lax.dot_general(
        features, back_flat, (((0,), (0,)), ((), ())), preferred_element_type=jnp.float32
    )
    cell_grad = (
        lax.dot_general(
            back_flat, w_embed, (((1,), (1,)), ((), ())), preferred_element_type=jnp.float32
        )
        * inv_root[:, None]
    ).astype(jnp.bfloat16)
    picked = jnp.dot(onehot, cell_grad, preferred_element_type=jnp.float32).astype(jnp.bfloat16)
    grad_obs = lax.all_to_all(picked, ("lon", "lat"), split_axis=0, concat_axis=0, tiled=True)

    summed = all_sum(grads + [embed_grad], grad_scale)
    tap_rows_n = kernels.size // channels
    kernel_out = summed[:tap_rows_n].reshape(kernels.shape)
    embed_out = summed[tap_rows_n:]
    return (encoded, kernel_out, embed_out, grad_obs)


def solution(mesh):
    placed = (
        P(("lon", "lat"), None),
        P(("lon", "lat")),
        P(("lon", "lat"), None),
        P(),
        P(),
        P(),
        P("lat", "lon", None),
    )
    return jax.shard_map(
        on_device,
        mesh=mesh,
        in_specs=placed,
        out_specs=(P("lat", "lon", None), P(), P(), P(("lon", "lat"), None)),
        check_vma=False,
    )
```

```python
import math

import jax
import jax.numpy as jnp
from jax import lax
from jax.sharding import PartitionSpec as P

ID_BASE = 128


def shift_pairs(count, step, periodic):
    pairs = []
    for source in range(count):
        target = source + step
        if 0 <= target < count:
            pairs.append((source, target))
        elif periodic:
            pairs.append((source, target % count))
    return pairs


def widen(block, depth):
    lon_count = lax.axis_size("lon")
    lat_count = lax.axis_size("lat")
    west = lax.ppermute(block[:, -depth:], "lon", shift_pairs(lon_count, 1, True))
    east = lax.ppermute(block[:, :depth], "lon", shift_pairs(lon_count, -1, True))
    block = jnp.concatenate([west, block, east], axis=1)
    north = lax.ppermute(block[-depth:], "lat", shift_pairs(lat_count, 1, False))
    south = lax.ppermute(block[:depth], "lat", shift_pairs(lat_count, -1, False))
    return jnp.concatenate([north, block, south], axis=0)


def lat_mask(rows, margin, height):
    lat_index = lax.axis_index("lat")
    lat_count = lax.axis_size("lat")
    global_row = lat_index * height - margin + jnp.arange(rows, dtype=jnp.int32)
    return ((global_row >= 0) & (global_row < lat_count * height))[:, None, None]


def crop(field, margin):
    if margin == 0:
        return field
    return field[margin:-margin, margin:-margin]


def conv_valid(padded, kernel):
    return lax.conv_general_dilated(
        padded[None],
        kernel,
        (1, 1),
        "VALID",
        dimension_numbers=("NHWC", "HWIO", "NHWC"),
        preferred_element_type=jnp.float32,
    )[0]


def cube_steps():
    steps = []
    for axis in ("lon", "lat"):
        count = lax.axis_size(axis)
        bit = 1
        while bit < count:
            steps.append((axis, bit, [(i, i ^ bit) for i in range(count)]))
            bit *= 2
    return steps


def reduce_replicated(part, steps):
    for axis, bit, pairs in steps:
        half = part.shape[0] // 2
        mine = (lax.axis_index(axis) // bit) % 2
        keep = lax.dynamic_slice_in_dim(part, mine * half, half)
        give = lax.dynamic_slice_in_dim(part, (1 - mine) * half, half)
        got = lax.ppermute(give.astype(jnp.bfloat16), axis, pairs)
        part = keep + got.astype(jnp.float32)
    return part


def gather_replicated(part, steps):
    for axis, bit, pairs in reversed(steps):
        mine = (lax.axis_index(axis) // bit) % 2
        got = lax.ppermute(part, axis, pairs)
        first = jnp.where(mine == 0, part, got)
        second = jnp.where(mine == 0, got, part)
        part = jnp.concatenate([first, second])
    return part


def all_sum(pieces, scale, streams=3):
    lanes = pieces[0].shape[-1]
    flat = jnp.concatenate([piece.reshape(-1, lanes) for piece in pieces])
    steps = cube_steps()
    devices = 2 ** len(steps)
    unit = devices * 16
    total = flat.shape[0]
    units = -(-total // unit)
    flat = jnp.pad(flat, ((0, units * unit - total), (0, 0)))
    middle = steps[1:-1] if len(steps) > 2 else []
    outs = []
    begin = 0
    for stream in range(streams):
        count = units // streams + (1 if stream < units % streams else 0)
        if count == 0:
            continue
        shift = stream % len(middle) if middle else 0
        order = steps[:1] + middle[shift:] + middle[:shift] + steps[len(middle) + 1 :]
        if len(steps) <= 2:
            order = steps
        part = reduce_replicated(flat[begin : begin + count * unit], order)
        outs.append(gather_replicated((part * scale).astype(jnp.bfloat16), order))
        begin += count * unit
    return jnp.concatenate(outs)[:total]


def on_device(obs_rows, cell_ids, counts, w_embed, w_density, kernels, cotangent):
    lon_count = lax.axis_size("lon")
    lat_count = lax.axis_size("lat")
    devices = lon_count * lat_count
    height, tile_width, channels = cotangent.shape
    cell_count = height * tile_width
    slot_rows = obs_rows.shape[0] // devices
    feat_count = obs_rows.shape[1]
    layer_count = kernels.shape[0]
    margin = 2 * layer_count

    cot_wide = widen(cotangent, layer_count)

    live_mask = jnp.arange(slot_rows, dtype=jnp.int32)[None, :] < counts[0][:, None]
    slot_ids = cell_ids.reshape(devices, slot_rows)
    id_high = jnp.where(live_mask, slot_ids // ID_BASE, -1)
    id_low = jnp.where(live_mask, slot_ids % ID_BASE, -1)
    code = jnp.concatenate([id_high, id_low], axis=1).astype(jnp.bfloat16)
    code_rows = -(-2 * slot_rows // feat_count)
    code_pad = -(-code_rows // 16) * 16
    code = jnp.pad(code, ((0, 0), (0, code_rows * feat_count - 2 * slot_rows)))
    code = code.reshape(devices, code_rows, feat_count)
    code = jnp.pad(code, ((0, 0), (0, code_pad - code_rows), (0, 0)))
    packed = jnp.concatenate([obs_rows.reshape(devices, slot_rows, feat_count), code], axis=1)
    got = lax.all_to_all(packed, ("lon", "lat"), split_axis=0, concat_axis=0, tiled=True)
    got_rows = got[:, :slot_rows].reshape(devices * slot_rows, feat_count)
    got_code = got[:, slot_rows : slot_rows + code_rows].reshape(devices, code_rows * feat_count)
    got_code = got_code.astype(jnp.int32)
    got_ids = (got_code[:, :slot_rows] * ID_BASE + got_code[:, slot_rows : 2 * slot_rows]).reshape(-1)

    cell_iota = jnp.arange(cell_count, dtype=jnp.int32)
    onehot = (got_ids[:, None] == cell_iota[None, :]).astype(jnp.bfloat16)
    cell_sums = lax.dot_general(
        onehot, got_rows, (((0,), (0,)), ((), ())), preferred_element_type=jnp.float32
    )
    density = jnp.sum(onehot.astype(jnp.float32), axis=0)
    inv_root = lax.rsqrt(density + 1.0)
    features = (cell_sums * inv_root[:, None]).astype(jnp.bfloat16)
    start_act = (
        jnp.dot(features, w_embed, preferred_element_type=jnp.float32)
        + jnp.log1p(density)[:, None] * w_density.astype(jnp.float32)[None, :]
    )
    activation = start_act.astype(jnp.bfloat16).reshape(height, tile_width, channels)

    act = widen(activation, margin)
    stored_acts = [act]
    stored_pre = []
    for layer_index in range(layer_count):
        out_margin = margin - layer_index - 1
        preact = conv_valid(act, kernels[layer_index])
        act = (crop(act, 1).astype(jnp.float32) + jax.nn.silu(preact)).astype(jnp.bfloat16)
        act = jnp.where(lat_mask(act.shape[0], out_margin, height), act, jnp.zeros_like(act))
        stored_pre.append(preact)
        stored_acts.append(act)
    encoded = crop(act, margin - layer_count)

    grad_scale = 1.0 / math.sqrt(cell_count * devices)
    back = cot_wide
    grads = [None] * layer_count
    for layer_index in reversed(range(layer_count)):
        back_margin = layer_index + 1
        preact = crop(stored_pre[layer_index], margin - layer_index - 1 - back_margin)
        sigmoid_v = jax.nn.sigmoid(preact)
        slope = (
            back.astype(jnp.float32) * (sigmoid_v * (1.0 + preact * (1.0 - sigmoid_v)))
        ).astype(jnp.bfloat16)
        slope = jnp.where(lat_mask(slope.shape[0], back_margin, height), slope, jnp.zeros_like(slope))
        slope_flat = crop(slope, back_margin).reshape(cell_count, channels)
        act_in = crop(stored_acts[layer_index], margin - layer_index - 1)
        patches = jnp.concatenate(
            [
                act_in[row_off : row_off + height, col_off : col_off + tile_width]
                for row_off in range(3)
                for col_off in range(3)
            ],
            axis=-1,
        ).reshape(cell_count, 9 * channels)
        tap_grad = lax.dot_general(
            patches, slope_flat, (((0,), (0,)), ((), ())), preferred_element_type=jnp.float32
        )
        flipped = jnp.transpose(kernels[layer_index][::-1, ::-1], (0, 1, 3, 2))
        spread = conv_valid(slope, flipped)
        back = lax.optimization_barrier(
            (crop(back, 1).astype(jnp.float32) + spread).astype(jnp.bfloat16)
        )
        grads[layer_index] = tap_grad
    back_flat = back.reshape(cell_count, channels)
    embed_grad = lax.dot_general(
        features, back_flat, (((0,), (0,)), ((), ())), preferred_element_type=jnp.float32
    )
    cell_grad = (
        lax.dot_general(
            back_flat, w_embed, (((1,), (1,)), ((), ())), preferred_element_type=jnp.float32
        )
        * inv_root[:, None]
    ).astype(jnp.bfloat16)
    picked = jnp.dot(onehot, cell_grad, preferred_element_type=jnp.float32).astype(jnp.bfloat16)
    grad_obs = lax.all_to_all(picked, ("lon", "lat"), split_axis=0, concat_axis=0, tiled=True)

    summed = all_sum(grads + [embed_grad], grad_scale)
    tap_rows_n = kernels.size // channels
    kernel_out = summed[:tap_rows_n].reshape(kernels.shape)
    embed_out = summed[tap_rows_n:]
    return (encoded, kernel_out, embed_out, grad_obs)


def solution(mesh):
    placed = (
        P(("lon", "lat"), None),
        P(("lon", "lat")),
        P(("lon", "lat"), None),
        P(),
        P(),
        P(),
        P("lat", "lon", None),
    )
    return jax.shard_map(
        on_device,
        mesh=mesh,
        in_specs=placed,
        out_specs=(P("lat", "lon", None), P(), P(), P(("lon", "lat"), None)),
        check_vma=False,
    )
```

```python
import math

import jax
import jax.numpy as jnp
from jax import lax
from jax.sharding import PartitionSpec as P

ID_BASE = 128


def shift_pairs(count, step, periodic):
    pairs = []
    for source in range(count):
        target = source + step
        if 0 <= target < count:
            pairs.append((source, target))
        elif periodic:
            pairs.append((source, target % count))
    return pairs


def widen(block, depth):
    lon_count = lax.axis_size("lon")
    lat_count = lax.axis_size("lat")
    west = lax.ppermute(block[:, -depth:], "lon", shift_pairs(lon_count, 1, True))
    east = lax.ppermute(block[:, :depth], "lon", shift_pairs(lon_count, -1, True))
    block = jnp.concatenate([west, block, east], axis=1)
    north = lax.ppermute(block[-depth:], "lat", shift_pairs(lat_count, 1, False))
    south = lax.ppermute(block[:depth], "lat", shift_pairs(lat_count, -1, False))
    return jnp.concatenate([north, block, south], axis=0)


def lat_mask(rows, margin, height):
    lat_index = lax.axis_index("lat")
    lat_count = lax.axis_size("lat")
    global_row = lat_index * height - margin + jnp.arange(rows, dtype=jnp.int32)
    return ((global_row >= 0) & (global_row < lat_count * height))[:, None, None]


def crop(field, margin):
    if margin == 0:
        return field
    return field[margin:-margin, margin:-margin]


def conv_valid(padded, kernel):
    return lax.conv_general_dilated(
        padded[None],
        kernel,
        (1, 1),
        "VALID",
        dimension_numbers=("NHWC", "HWIO", "NHWC"),
        preferred_element_type=jnp.float32,
    )[0]


def cube_steps():
    steps = []
    for axis in ("lon", "lat"):
        count = lax.axis_size(axis)
        bit = 1
        while bit < count:
            steps.append((axis, bit, [(i, i ^ bit) for i in range(count)]))
            bit *= 2
    return steps


def reduce_replicated(part, steps):
    for axis, bit, pairs in steps:
        half = part.shape[0] // 2
        mine = (lax.axis_index(axis) // bit) % 2
        keep = lax.dynamic_slice_in_dim(part, mine * half, half)
        give = lax.dynamic_slice_in_dim(part, (1 - mine) * half, half)
        got = lax.ppermute(give.astype(jnp.bfloat16), axis, pairs)
        part = keep + got.astype(jnp.float32)
    return part


def gather_replicated(part, steps):
    for axis, bit, pairs in reversed(steps):
        mine = (lax.axis_index(axis) // bit) % 2
        got = lax.ppermute(part, axis, pairs)
        first = jnp.where(mine == 0, part, got)
        second = jnp.where(mine == 0, got, part)
        part = jnp.concatenate([first, second])
    return part


def all_sum(pieces, scale, streams=3):
    lanes = pieces[0].shape[-1]
    flat = jnp.concatenate([piece.reshape(-1, lanes) for piece in pieces])
    steps = cube_steps()
    devices = 2 ** len(steps)
    unit = devices * 16
    total = flat.shape[0]
    units = -(-total // unit)
    flat = jnp.pad(flat, ((0, units * unit - total), (0, 0)))
    middle = steps[1:-1] if len(steps) > 2 else []
    outs = []
    begin = 0
    for stream in range(streams):
        count = units // streams + (1 if stream < units % streams else 0)
        if count == 0:
            continue
        shift = stream % len(middle) if middle else 0
        order = steps[:1] + middle[shift:] + middle[:shift] + steps[len(middle) + 1 :]
        if len(steps) <= 2:
            order = steps
        part = reduce_replicated(flat[begin : begin + count * unit], order)
        outs.append(gather_replicated((part * scale).astype(jnp.bfloat16), order))
        begin += count * unit
    return jnp.concatenate(outs)[:total]


def on_device(obs_rows, cell_ids, counts, w_embed, w_density, kernels, cotangent):
    lon_count = lax.axis_size("lon")
    lat_count = lax.axis_size("lat")
    devices = lon_count * lat_count
    height, tile_width, channels = cotangent.shape
    cell_count = height * tile_width
    slot_rows = obs_rows.shape[0] // devices
    feat_count = obs_rows.shape[1]
    layer_count = kernels.shape[0]
    margin = 2 * layer_count

    cot_wide = widen(cotangent, layer_count)

    live_mask = jnp.arange(slot_rows, dtype=jnp.int32)[None, :] < counts[0][:, None]
    slot_ids = cell_ids.reshape(devices, slot_rows)
    id_high = jnp.where(live_mask, slot_ids // ID_BASE, -1)
    id_low = jnp.where(live_mask, slot_ids % ID_BASE, -1)
    code = jnp.concatenate([id_high, id_low], axis=1).astype(jnp.bfloat16)
    code_rows = -(-2 * slot_rows // feat_count)
    code_pad = -(-code_rows // 16) * 16
    code = jnp.pad(code, ((0, 0), (0, code_rows * feat_count - 2 * slot_rows)))
    code = code.reshape(devices, code_rows, feat_count)
    code = jnp.pad(code, ((0, 0), (0, code_pad - code_rows), (0, 0)))
    packed = jnp.concatenate([obs_rows.reshape(devices, slot_rows, feat_count), code], axis=1)
    got = lax.all_to_all(packed, ("lon", "lat"), split_axis=0, concat_axis=0, tiled=True)
    got_rows = got[:, :slot_rows].reshape(devices * slot_rows, feat_count)
    got_code = got[:, slot_rows : slot_rows + code_rows].reshape(devices, code_rows * feat_count)
    got_code = got_code.astype(jnp.int32)
    got_ids = (got_code[:, :slot_rows] * ID_BASE + got_code[:, slot_rows : 2 * slot_rows]).reshape(-1)

    cell_iota = jnp.arange(cell_count, dtype=jnp.int32)
    onehot = (got_ids[:, None] == cell_iota[None, :]).astype(jnp.bfloat16)
    cell_sums = lax.dot_general(
        onehot, got_rows, (((0,), (0,)), ((), ())), preferred_element_type=jnp.float32
    )
    density = jnp.sum(onehot.astype(jnp.float32), axis=0)
    inv_root = lax.rsqrt(density + 1.0)
    features = (cell_sums * inv_root[:, None]).astype(jnp.bfloat16)
    start_act = (
        jnp.dot(features, w_embed, preferred_element_type=jnp.float32)
        + jnp.log1p(density)[:, None] * w_density.astype(jnp.float32)[None, :]
    )
    activation = start_act.astype(jnp.bfloat16).reshape(height, tile_width, channels)

    act = widen(activation, margin)
    stored_acts = [act]
    stored_pre = []
    for layer_index in range(layer_count):
        out_margin = margin - layer_index - 1
        preact = conv_valid(act, kernels[layer_index])
        act = (crop(act, 1).astype(jnp.float32) + jax.nn.silu(preact)).astype(jnp.bfloat16)
        act = jnp.where(lat_mask(act.shape[0], out_margin, height), act, jnp.zeros_like(act))
        stored_pre.append(preact)
        stored_acts.append(act)
    encoded = crop(act, margin - layer_count)

    grad_scale = 1.0 / math.sqrt(cell_count * devices)
    back = cot_wide
    grads = [None] * layer_count
    for layer_index in reversed(range(layer_count)):
        back_margin = layer_index + 1
        preact = crop(stored_pre[layer_index], margin - layer_index - 1 - back_margin)
        sigmoid_v = jax.nn.sigmoid(preact)
        slope = (
            back.astype(jnp.float32) * (sigmoid_v * (1.0 + preact * (1.0 - sigmoid_v)))
        ).astype(jnp.bfloat16)
        slope = jnp.where(lat_mask(slope.shape[0], back_margin, height), slope, jnp.zeros_like(slope))
        slope_flat = crop(slope, back_margin).reshape(cell_count, channels)
        act_in = crop(stored_acts[layer_index], margin - layer_index - 1)
        patches = jnp.concatenate(
            [
                act_in[row_off : row_off + height, col_off : col_off + tile_width]
                for row_off in range(3)
                for col_off in range(3)
            ],
            axis=-1,
        ).reshape(cell_count, 9 * channels)
        tap_grad = lax.dot_general(
            patches, slope_flat, (((0,), (0,)), ((), ())), preferred_element_type=jnp.float32
        )
        flipped = jnp.transpose(kernels[layer_index][::-1, ::-1], (0, 1, 3, 2))
        spread = conv_valid(slope, flipped)
        back = lax.optimization_barrier(
            (crop(back, 1).astype(jnp.float32) + spread).astype(jnp.bfloat16)
        )
        grads[layer_index] = tap_grad
    back_flat = back.reshape(cell_count, channels)
    embed_grad = lax.dot_general(
        features, back_flat, (((0,), (0,)), ((), ())), preferred_element_type=jnp.float32
    )
    cell_grad = (
        lax.dot_general(
            back_flat, w_embed, (((1,), (1,)), ((), ())), preferred_element_type=jnp.float32
        )
        * inv_root[:, None]
    ).astype(jnp.bfloat16)
    picked = jnp.dot(onehot, cell_grad, preferred_element_type=jnp.float32).astype(jnp.bfloat16)

    summed = all_sum(grads + [embed_grad], grad_scale)
    picked, summed = lax.optimization_barrier((picked, summed))
    grad_obs = lax.all_to_all(picked, ("lon", "lat"), split_axis=0, concat_axis=0, tiled=True)
    tap_rows_n = kernels.size // channels
    kernel_out = summed[:tap_rows_n].reshape(kernels.shape)
    embed_out = summed[tap_rows_n:]
    return (encoded, kernel_out, embed_out, grad_obs)


def solution(mesh):
    placed = (
        P(("lon", "lat"), None),
        P(("lon", "lat")),
        P(("lon", "lat"), None),
        P(),
        P(),
        P(),
        P("lat", "lon", None),
    )
    return jax.shard_map(
        on_device,
        mesh=mesh,
        in_specs=placed,
        out_specs=(P("lat", "lon", None), P(), P(), P(("lon", "lat"), None)),
        check_vma=False,
    )
```

```python
import math

import jax
import jax.numpy as jnp
from jax import lax
from jax.sharding import PartitionSpec as P

ID_BASE = 128


def shift_pairs(count, step, periodic):
    pairs = []
    for source in range(count):
        target = source + step
        if 0 <= target < count:
            pairs.append((source, target))
        elif periodic:
            pairs.append((source, target % count))
    return pairs


def widen(block, depth):
    lon_count = lax.axis_size("lon")
    lat_count = lax.axis_size("lat")
    west = lax.ppermute(block[:, -depth:], "lon", shift_pairs(lon_count, 1, True))
    east = lax.ppermute(block[:, :depth], "lon", shift_pairs(lon_count, -1, True))
    block = jnp.concatenate([west, block, east], axis=1)
    north = lax.ppermute(block[-depth:], "lat", shift_pairs(lat_count, 1, False))
    south = lax.ppermute(block[:depth], "lat", shift_pairs(lat_count, -1, False))
    return jnp.concatenate([north, block, south], axis=0)


def lat_mask(rows, margin, height):
    lat_index = lax.axis_index("lat")
    lat_count = lax.axis_size("lat")
    global_row = lat_index * height - margin + jnp.arange(rows, dtype=jnp.int32)
    return ((global_row >= 0) & (global_row < lat_count * height))[:, None, None]


def crop(field, margin):
    if margin == 0:
        return field
    return field[margin:-margin, margin:-margin]


def conv_valid(padded, kernel):
    return lax.conv_general_dilated(
        padded[None],
        kernel,
        (1, 1),
        "VALID",
        dimension_numbers=("NHWC", "HWIO", "NHWC"),
        preferred_element_type=jnp.float32,
    )[0]


def cube_steps():
    steps = []
    for axis in ("lon", "lat"):
        count = lax.axis_size(axis)
        bit = 1
        while bit < count:
            steps.append((axis, bit, [(i, i ^ bit) for i in range(count)]))
            bit *= 2
    return steps


def reduce_replicated(part, steps):
    for axis, bit, pairs in steps:
        half = part.shape[0] // 2
        mine = (lax.axis_index(axis) // bit) % 2
        keep = lax.dynamic_slice_in_dim(part, mine * half, half)
        give = lax.dynamic_slice_in_dim(part, (1 - mine) * half, half)
        got = lax.ppermute(give.astype(jnp.bfloat16), axis, pairs)
        part = keep + got.astype(jnp.float32)
    return part


def gather_replicated(part, steps):
    for axis, bit, pairs in reversed(steps):
        mine = (lax.axis_index(axis) // bit) % 2
        got = lax.ppermute(part, axis, pairs)
        first = jnp.where(mine == 0, part, got)
        second = jnp.where(mine == 0, got, part)
        part = jnp.concatenate([first, second])
    return part


def all_sum(pieces, scale, streams=4):
    lanes = pieces[0].shape[-1]
    flat = jnp.concatenate([piece.reshape(-1, lanes) for piece in pieces])
    steps = cube_steps()
    devices = 2 ** len(steps)
    unit = devices * 16
    total = flat.shape[0]
    units = -(-total // unit)
    flat = jnp.pad(flat, ((0, units * unit - total), (0, 0)))
    middle = steps[:-1] if len(steps) > 1 else []
    outs = []
    begin = 0
    for stream in range(streams):
        count = units // streams + (1 if stream < units % streams else 0)
        if count == 0:
            continue
        shift = stream % len(middle) if middle else 0
        order = middle[shift:] + middle[:shift] + steps[len(middle) :]
        part = reduce_replicated(flat[begin : begin + count * unit], order)
        outs.append(gather_replicated((part * scale).astype(jnp.bfloat16), order))
        begin += count * unit
    return jnp.concatenate(outs)[:total]


def on_device(obs_rows, cell_ids, counts, w_embed, w_density, kernels, cotangent):
    lon_count = lax.axis_size("lon")
    lat_count = lax.axis_size("lat")
    devices = lon_count * lat_count
    height, tile_width, channels = cotangent.shape
    cell_count = height * tile_width
    slot_rows = obs_rows.shape[0] // devices
    feat_count = obs_rows.shape[1]
    layer_count = kernels.shape[0]
    margin = 2 * layer_count

    cot_wide = widen(cotangent, layer_count)

    live_mask = jnp.arange(slot_rows, dtype=jnp.int32)[None, :] < counts[0][:, None]
    slot_ids = cell_ids.reshape(devices, slot_rows)
    id_high = jnp.where(live_mask, slot_ids // ID_BASE, -1)
    id_low = jnp.where(live_mask, slot_ids % ID_BASE, -1)
    code = jnp.concatenate([id_high, id_low], axis=1).astype(jnp.bfloat16)
    code_rows = -(-2 * slot_rows // feat_count)
    code_pad = -(-code_rows // 16) * 16
    code = jnp.pad(code, ((0, 0), (0, code_rows * feat_count - 2 * slot_rows)))
    code = code.reshape(devices, code_rows, feat_count)
    code = jnp.pad(code, ((0, 0), (0, code_pad - code_rows), (0, 0)))
    packed = jnp.concatenate([obs_rows.reshape(devices, slot_rows, feat_count), code], axis=1)
    got = lax.all_to_all(packed, ("lon", "lat"), split_axis=0, concat_axis=0, tiled=True)
    got_rows = got[:, :slot_rows].reshape(devices * slot_rows, feat_count)
    got_code = got[:, slot_rows : slot_rows + code_rows].reshape(devices, code_rows * feat_count)
    got_code = got_code.astype(jnp.int32)
    got_ids = (got_code[:, :slot_rows] * ID_BASE + got_code[:, slot_rows : 2 * slot_rows]).reshape(-1)

    cell_iota = jnp.arange(cell_count, dtype=jnp.int32)
    onehot = (got_ids[:, None] == cell_iota[None, :]).astype(jnp.bfloat16)
    cell_sums = lax.dot_general(
        onehot, got_rows, (((0,), (0,)), ((), ())), preferred_element_type=jnp.float32
    )
    density = jnp.sum(onehot.astype(jnp.float32), axis=0)
    inv_root = lax.rsqrt(density + 1.0)
    features = (cell_sums * inv_root[:, None]).astype(jnp.bfloat16)
    start_act = (
        jnp.dot(features, w_embed, preferred_element_type=jnp.float32)
        + jnp.log1p(density)[:, None] * w_density.astype(jnp.float32)[None, :]
    )
    activation = start_act.astype(jnp.bfloat16).reshape(height, tile_width, channels)

    act = widen(activation, margin)
    stored_acts = [act]
    stored_pre = []
    for layer_index in range(layer_count):
        out_margin = margin - layer_index - 1
        preact = conv_valid(act, kernels[layer_index])
        act = (crop(act, 1).astype(jnp.float32) + jax.nn.silu(preact)).astype(jnp.bfloat16)
        act = jnp.where(lat_mask(act.shape[0], out_margin, height), act, jnp.zeros_like(act))
        stored_pre.append(preact)
        stored_acts.append(act)
    encoded = crop(act, margin - layer_count)

    grad_scale = 1.0 / math.sqrt(cell_count * devices)
    back = cot_wide
    grads = [None] * layer_count
    for layer_index in reversed(range(layer_count)):
        back_margin = layer_index + 1
        preact = crop(stored_pre[layer_index], margin - layer_index - 1 - back_margin)
        sigmoid_v = jax.nn.sigmoid(preact)
        slope = (
            back.astype(jnp.float32) * (sigmoid_v * (1.0 + preact * (1.0 - sigmoid_v)))
        ).astype(jnp.bfloat16)
        slope = jnp.where(lat_mask(slope.shape[0], back_margin, height), slope, jnp.zeros_like(slope))
        slope_flat = crop(slope, back_margin).reshape(cell_count, channels)
        act_in = crop(stored_acts[layer_index], margin - layer_index - 1)
        patches = jnp.concatenate(
            [
                act_in[row_off : row_off + height, col_off : col_off + tile_width]
                for row_off in range(3)
                for col_off in range(3)
            ],
            axis=-1,
        ).reshape(cell_count, 9 * channels)
        tap_grad = lax.dot_general(
            patches, slope_flat, (((0,), (0,)), ((), ())), preferred_element_type=jnp.float32
        )
        flipped = jnp.transpose(kernels[layer_index][::-1, ::-1], (0, 1, 3, 2))
        spread = conv_valid(slope, flipped)
        back = lax.optimization_barrier(
            (crop(back, 1).astype(jnp.float32) + spread).astype(jnp.bfloat16)
        )
        grads[layer_index] = tap_grad
    back_flat = back.reshape(cell_count, channels)
    embed_grad = lax.dot_general(
        features, back_flat, (((0,), (0,)), ((), ())), preferred_element_type=jnp.float32
    )
    cell_grad = (
        lax.dot_general(
            back_flat, w_embed, (((1,), (1,)), ((), ())), preferred_element_type=jnp.float32
        )
        * inv_root[:, None]
    ).astype(jnp.bfloat16)
    picked = jnp.dot(onehot, cell_grad, preferred_element_type=jnp.float32).astype(jnp.bfloat16)
    grad_obs = lax.all_to_all(picked, ("lon", "lat"), split_axis=0, concat_axis=0, tiled=True)

    summed = all_sum(grads + [embed_grad], grad_scale)
    tap_rows_n = kernels.size // channels
    kernel_out = summed[:tap_rows_n].reshape(kernels.shape)
    embed_out = summed[tap_rows_n:]
    return (encoded, kernel_out, embed_out, grad_obs)


def solution(mesh):
    placed = (
        P(("lon", "lat"), None),
        P(("lon", "lat")),
        P(("lon", "lat"), None),
        P(),
        P(),
        P(),
        P("lat", "lon", None),
    )
    return jax.shard_map(
        on_device,
        mesh=mesh,
        in_specs=placed,
        out_specs=(P("lat", "lon", None), P(), P(), P(("lon", "lat"), None)),
        check_vma=False,
    )
```

```python
import math

import jax
import jax.numpy as jnp
from jax import lax
from jax.sharding import PartitionSpec as P

ID_BASE = 128


def shift_pairs(count, step, periodic):
    pairs = []
    for source in range(count):
        target = source + step
        if 0 <= target < count:
            pairs.append((source, target))
        elif periodic:
            pairs.append((source, target % count))
    return pairs


def widen(block, depth):
    lon_count = lax.axis_size("lon")
    lat_count = lax.axis_size("lat")
    west = lax.ppermute(block[:, -depth:], "lon", shift_pairs(lon_count, 1, True))
    east = lax.ppermute(block[:, :depth], "lon", shift_pairs(lon_count, -1, True))
    block = jnp.concatenate([west, block, east], axis=1)
    north = lax.ppermute(block[-depth:], "lat", shift_pairs(lat_count, 1, False))
    south = lax.ppermute(block[:depth], "lat", shift_pairs(lat_count, -1, False))
    return jnp.concatenate([north, block, south], axis=0)


def lat_mask(rows, margin, height):
    lat_index = lax.axis_index("lat")
    lat_count = lax.axis_size("lat")
    global_row = lat_index * height - margin + jnp.arange(rows, dtype=jnp.int32)
    return ((global_row >= 0) & (global_row < lat_count * height))[:, None, None]


def crop(field, margin):
    if margin == 0:
        return field
    return field[margin:-margin, margin:-margin]


def conv_valid(padded, kernel):
    return lax.conv_general_dilated(
        padded[None],
        kernel,
        (1, 1),
        "VALID",
        dimension_numbers=("NHWC", "HWIO", "NHWC"),
        preferred_element_type=jnp.float32,
    )[0]


def cube_steps():
    steps = []
    for axis in ("lon", "lat"):
        count = lax.axis_size(axis)
        bit = 1
        while bit < count:
            steps.append((axis, bit, [(i, i ^ bit) for i in range(count)]))
            bit *= 2
    return steps


def reduce_replicated(part, steps):
    for axis, bit, pairs in steps:
        half = part.shape[0] // 2
        mine = (lax.axis_index(axis) // bit) % 2
        keep = lax.dynamic_slice_in_dim(part, mine * half, half)
        give = lax.dynamic_slice_in_dim(part, (1 - mine) * half, half)
        got = lax.ppermute(give.astype(jnp.bfloat16), axis, pairs)
        part = keep + got.astype(jnp.float32)
    return part


def gather_replicated(part, steps):
    for axis, bit, pairs in reversed(steps):
        mine = (lax.axis_index(axis) // bit) % 2
        got = lax.ppermute(part, axis, pairs)
        first = jnp.where(mine == 0, part, got)
        second = jnp.where(mine == 0, got, part)
        part = jnp.concatenate([first, second])
    return part


def all_sum(groups, scale):
    steps = cube_steps()
    devices = 2 ** len(steps)
    unit = devices * 16
    middle = steps[1:-1] if len(steps) > 2 else []
    outs = []
    for stream, pieces in enumerate(groups):
        lanes = pieces[0].shape[-1]
        flat = jnp.concatenate([piece.reshape(-1, lanes) for piece in pieces])
        total = flat.shape[0]
        flat = jnp.pad(flat, ((0, -(-total // unit) * unit - total), (0, 0)))
        shift = stream % len(middle) if middle else 0
        order = steps[:1] + middle[shift:] + middle[:shift] + steps[len(middle) + 1 :]
        if len(steps) <= 2:
            order = steps
        part = reduce_replicated(flat, order)
        outs.append(gather_replicated((part * scale).astype(jnp.bfloat16), order)[:total])
    return outs


def on_device(obs_rows, cell_ids, counts, w_embed, w_density, kernels, cotangent):
    lon_count = lax.axis_size("lon")
    lat_count = lax.axis_size("lat")
    devices = lon_count * lat_count
    height, tile_width, channels = cotangent.shape
    cell_count = height * tile_width
    slot_rows = obs_rows.shape[0] // devices
    feat_count = obs_rows.shape[1]
    layer_count = kernels.shape[0]
    margin = 2 * layer_count

    cot_wide = widen(cotangent, layer_count)

    live_mask = jnp.arange(slot_rows, dtype=jnp.int32)[None, :] < counts[0][:, None]
    slot_ids = cell_ids.reshape(devices, slot_rows)
    id_high = jnp.where(live_mask, slot_ids // ID_BASE, -1)
    id_low = jnp.where(live_mask, slot_ids % ID_BASE, -1)
    code = jnp.concatenate([id_high, id_low], axis=1).astype(jnp.bfloat16)
    code_rows = -(-2 * slot_rows // feat_count)
    code_pad = -(-code_rows // 16) * 16
    code = jnp.pad(code, ((0, 0), (0, code_rows * feat_count - 2 * slot_rows)))
    code = code.reshape(devices, code_rows, feat_count)
    code = jnp.pad(code, ((0, 0), (0, code_pad - code_rows), (0, 0)))
    packed = jnp.concatenate([obs_rows.reshape(devices, slot_rows, feat_count), code], axis=1)
    got = lax.all_to_all(packed, ("lon", "lat"), split_axis=0, concat_axis=0, tiled=True)
    got_rows = got[:, :slot_rows].reshape(devices * slot_rows, feat_count)
    got_code = got[:, slot_rows : slot_rows + code_rows].reshape(devices, code_rows * feat_count)
    got_code = got_code.astype(jnp.int32)
    got_ids = (got_code[:, :slot_rows] * ID_BASE + got_code[:, slot_rows : 2 * slot_rows]).reshape(-1)

    cell_iota = jnp.arange(cell_count, dtype=jnp.int32)
    onehot = (got_ids[:, None] == cell_iota[None, :]).astype(jnp.bfloat16)
    cell_sums = lax.dot_general(
        onehot, got_rows, (((0,), (0,)), ((), ())), preferred_element_type=jnp.float32
    )
    density = jnp.sum(onehot.astype(jnp.float32), axis=0)
    inv_root = lax.rsqrt(density + 1.0)
    features = (cell_sums * inv_root[:, None]).astype(jnp.bfloat16)
    start_act = (
        jnp.dot(features, w_embed, preferred_element_type=jnp.float32)
        + jnp.log1p(density)[:, None] * w_density.astype(jnp.float32)[None, :]
    )
    activation = start_act.astype(jnp.bfloat16).reshape(height, tile_width, channels)

    act = widen(activation, margin)
    stored_acts = [act]
    stored_pre = []
    for layer_index in range(layer_count):
        out_margin = margin - layer_index - 1
        preact = conv_valid(act, kernels[layer_index])
        act = (crop(act, 1).astype(jnp.float32) + jax.nn.silu(preact)).astype(jnp.bfloat16)
        act = jnp.where(lat_mask(act.shape[0], out_margin, height), act, jnp.zeros_like(act))
        stored_pre.append(preact)
        stored_acts.append(act)
    encoded = crop(act, margin - layer_count)

    grad_scale = 1.0 / math.sqrt(cell_count * devices)
    back = cot_wide
    grads = [None] * layer_count
    for layer_index in reversed(range(layer_count)):
        back_margin = layer_index + 1
        preact = crop(stored_pre[layer_index], margin - layer_index - 1 - back_margin)
        sigmoid_v = jax.nn.sigmoid(preact)
        slope = (
            back.astype(jnp.float32) * (sigmoid_v * (1.0 + preact * (1.0 - sigmoid_v)))
        ).astype(jnp.bfloat16)
        slope = jnp.where(lat_mask(slope.shape[0], back_margin, height), slope, jnp.zeros_like(slope))
        slope_flat = crop(slope, back_margin).reshape(cell_count, channels)
        act_in = crop(stored_acts[layer_index], margin - layer_index - 1)
        patches = jnp.concatenate(
            [
                act_in[row_off : row_off + height, col_off : col_off + tile_width]
                for row_off in range(3)
                for col_off in range(3)
            ],
            axis=-1,
        ).reshape(cell_count, 9 * channels)
        tap_grad = lax.dot_general(
            patches, slope_flat, (((0,), (0,)), ((), ())), preferred_element_type=jnp.float32
        )
        flipped = jnp.transpose(kernels[layer_index][::-1, ::-1], (0, 1, 3, 2))
        spread = conv_valid(slope, flipped)
        back = lax.optimization_barrier(
            (crop(back, 1).astype(jnp.float32) + spread).astype(jnp.bfloat16)
        )
        grads[layer_index] = tap_grad
    back_flat = back.reshape(cell_count, channels)
    embed_grad = lax.dot_general(
        features, back_flat, (((0,), (0,)), ((), ())), preferred_element_type=jnp.float32
    )
    cell_grad = (
        lax.dot_general(
            back_flat, w_embed, (((1,), (1,)), ((), ())), preferred_element_type=jnp.float32
        )
        * inv_root[:, None]
    ).astype(jnp.bfloat16)
    picked = jnp.dot(onehot, cell_grad, preferred_element_type=jnp.float32).astype(jnp.bfloat16)
    grad_obs = lax.all_to_all(picked, ("lon", "lat"), split_axis=0, concat_axis=0, tiled=True)

    groups = [[grads[index]] for index in reversed(range(1, layer_count))]
    summed = all_sum(groups + [[grads[0], embed_grad]], grad_scale)
    tap_rows_n = kernels[0].size // channels
    kernel_out = jnp.concatenate(
        [summed[-1][:tap_rows_n]] + [summed[layer_count - 1 - index] for index in range(1, layer_count)]
    ).reshape(kernels.shape)
    embed_out = summed[-1][tap_rows_n:]
    return (encoded, kernel_out, embed_out, grad_obs)


def solution(mesh):
    placed = (
        P(("lon", "lat"), None),
        P(("lon", "lat")),
        P(("lon", "lat"), None),
        P(),
        P(),
        P(),
        P("lat", "lon", None),
    )
    return jax.shard_map(
        on_device,
        mesh=mesh,
        in_specs=placed,
        out_specs=(P("lat", "lon", None), P(), P(), P(("lon", "lat"), None)),
        check_vma=False,
    )
```

```python
import math

import jax
import jax.numpy as jnp
from jax import lax
from jax.sharding import PartitionSpec as P

ID_BASE = 128


def shift_pairs(count, step, periodic):
    pairs = []
    for source in range(count):
        target = source + step
        if 0 <= target < count:
            pairs.append((source, target))
        elif periodic:
            pairs.append((source, target % count))
    return pairs


def widen(block, depth):
    lon_count = lax.axis_size("lon")
    lat_count = lax.axis_size("lat")
    west = lax.ppermute(block[:, -depth:], "lon", shift_pairs(lon_count, 1, True))
    east = lax.ppermute(block[:, :depth], "lon", shift_pairs(lon_count, -1, True))
    block = jnp.concatenate([west, block, east], axis=1)
    north = lax.ppermute(block[-depth:], "lat", shift_pairs(lat_count, 1, False))
    south = lax.ppermute(block[:depth], "lat", shift_pairs(lat_count, -1, False))
    return jnp.concatenate([north, block, south], axis=0)


def lat_mask(rows, margin, height):
    lat_index = lax.axis_index("lat")
    lat_count = lax.axis_size("lat")
    global_row = lat_index * height - margin + jnp.arange(rows, dtype=jnp.int32)
    return ((global_row >= 0) & (global_row < lat_count * height))[:, None, None]


def crop(field, margin):
    if margin == 0:
        return field
    return field[margin:-margin, margin:-margin]


def conv_valid(padded, kernel):
    return lax.conv_general_dilated(
        padded[None],
        kernel,
        (1, 1),
        "VALID",
        dimension_numbers=("NHWC", "HWIO", "NHWC"),
        preferred_element_type=jnp.float32,
    )[0]


def cube_steps():
    steps = []
    for axis in ("lon", "lat"):
        count = lax.axis_size(axis)
        bit = 1
        while bit < count:
            steps.append((axis, bit, [(i, i ^ bit) for i in range(count)]))
            bit *= 2
    return steps


def reduce_replicated(part, steps):
    for axis, bit, pairs in steps:
        half = part.shape[0] // 2
        mine = (lax.axis_index(axis) // bit) % 2
        keep = lax.dynamic_slice_in_dim(part, mine * half, half)
        give = lax.dynamic_slice_in_dim(part, (1 - mine) * half, half)
        got = lax.ppermute(give.astype(jnp.bfloat16), axis, pairs)
        part = keep + got.astype(jnp.float32)
    return part


def gather_replicated(part, steps):
    for axis, bit, pairs in reversed(steps):
        mine = (lax.axis_index(axis) // bit) % 2
        got = lax.ppermute(part, axis, pairs)
        first = jnp.where(mine == 0, part, got)
        second = jnp.where(mine == 0, got, part)
        part = jnp.concatenate([first, second])
    return part


def all_sum(pieces, scale, hold, streams=3):
    lanes = pieces[0].shape[-1]
    flat = jnp.concatenate([piece.reshape(-1, lanes) for piece in pieces])
    steps = cube_steps()
    devices = 2 ** len(steps)
    unit = devices * 16
    total = flat.shape[0]
    units = -(-total // unit)
    flat = jnp.pad(flat, ((0, units * unit - total), (0, 0)))
    middle = steps[1:-1] if len(steps) > 2 else []
    orders = []
    parts = []
    begin = 0
    for stream in range(streams):
        count = units // streams + (1 if stream < units % streams else 0)
        if count == 0:
            continue
        shift = stream % len(middle) if middle else 0
        order = steps[:1] + middle[shift:] + middle[:shift] + steps[len(middle) + 1 :]
        if len(steps) <= 2:
            order = steps
        parts.append(reduce_replicated(flat[begin : begin + count * unit], order[:1]))
        orders.append(order)
        begin += count * unit
    hold, parts = lax.optimization_barrier((hold, parts))
    outs = []
    for part, order in zip(parts, orders):
        part = reduce_replicated(part, order[1:])
        outs.append(gather_replicated((part * scale).astype(jnp.bfloat16), order))
    return jnp.concatenate(outs)[:total], hold


def on_device(obs_rows, cell_ids, counts, w_embed, w_density, kernels, cotangent):
    lon_count = lax.axis_size("lon")
    lat_count = lax.axis_size("lat")
    devices = lon_count * lat_count
    height, tile_width, channels = cotangent.shape
    cell_count = height * tile_width
    slot_rows = obs_rows.shape[0] // devices
    feat_count = obs_rows.shape[1]
    layer_count = kernels.shape[0]
    margin = 2 * layer_count

    cot_wide = widen(cotangent, layer_count)

    live_mask = jnp.arange(slot_rows, dtype=jnp.int32)[None, :] < counts[0][:, None]
    slot_ids = cell_ids.reshape(devices, slot_rows)
    id_high = jnp.where(live_mask, slot_ids // ID_BASE, -1)
    id_low = jnp.where(live_mask, slot_ids % ID_BASE, -1)
    code = jnp.concatenate([id_high, id_low], axis=1).astype(jnp.bfloat16)
    code_rows = -(-2 * slot_rows // feat_count)
    code_pad = -(-code_rows // 16) * 16
    code = jnp.pad(code, ((0, 0), (0, code_rows * feat_count - 2 * slot_rows)))
    code = code.reshape(devices, code_rows, feat_count)
    code = jnp.pad(code, ((0, 0), (0, code_pad - code_rows), (0, 0)))
    packed = jnp.concatenate([obs_rows.reshape(devices, slot_rows, feat_count), code], axis=1)
    got = lax.all_to_all(packed, ("lon", "lat"), split_axis=0, concat_axis=0, tiled=True)
    got_rows = got[:, :slot_rows].reshape(devices * slot_rows, feat_count)
    got_code = got[:, slot_rows : slot_rows + code_rows].reshape(devices, code_rows * feat_count)
    got_code = got_code.astype(jnp.int32)
    got_ids = (got_code[:, :slot_rows] * ID_BASE + got_code[:, slot_rows : 2 * slot_rows]).reshape(-1)

    cell_iota = jnp.arange(cell_count, dtype=jnp.int32)
    onehot = (got_ids[:, None] == cell_iota[None, :]).astype(jnp.bfloat16)
    cell_sums = lax.dot_general(
        onehot, got_rows, (((0,), (0,)), ((), ())), preferred_element_type=jnp.float32
    )
    density = jnp.sum(onehot.astype(jnp.float32), axis=0)
    inv_root = lax.rsqrt(density + 1.0)
    features = (cell_sums * inv_root[:, None]).astype(jnp.bfloat16)
    start_act = (
        jnp.dot(features, w_embed, preferred_element_type=jnp.float32)
        + jnp.log1p(density)[:, None] * w_density.astype(jnp.float32)[None, :]
    )
    activation = start_act.astype(jnp.bfloat16).reshape(height, tile_width, channels)

    act = widen(activation, margin)
    stored_acts = [act]
    stored_pre = []
    for layer_index in range(layer_count):
        out_margin = margin - layer_index - 1
        preact = conv_valid(act, kernels[layer_index])
        act = (crop(act, 1).astype(jnp.float32) + jax.nn.silu(preact)).astype(jnp.bfloat16)
        act = jnp.where(lat_mask(act.shape[0], out_margin, height), act, jnp.zeros_like(act))
        stored_pre.append(preact)
        stored_acts.append(act)
    encoded = crop(act, margin - layer_count)

    grad_scale = 1.0 / math.sqrt(cell_count * devices)
    back = cot_wide
    grads = [None] * layer_count
    for layer_index in reversed(range(layer_count)):
        back_margin = layer_index + 1
        preact = crop(stored_pre[layer_index], margin - layer_index - 1 - back_margin)
        sigmoid_v = jax.nn.sigmoid(preact)
        slope = (
            back.astype(jnp.float32) * (sigmoid_v * (1.0 + preact * (1.0 - sigmoid_v)))
        ).astype(jnp.bfloat16)
        slope = jnp.where(lat_mask(slope.shape[0], back_margin, height), slope, jnp.zeros_like(slope))
        slope_flat = crop(slope, back_margin).reshape(cell_count, channels)
        act_in = crop(stored_acts[layer_index], margin - layer_index - 1)
        patches = jnp.concatenate(
            [
                act_in[row_off : row_off + height, col_off : col_off + tile_width]
                for row_off in range(3)
                for col_off in range(3)
            ],
            axis=-1,
        ).reshape(cell_count, 9 * channels)
        tap_grad = lax.dot_general(
            patches, slope_flat, (((0,), (0,)), ((), ())), preferred_element_type=jnp.float32
        )
        flipped = jnp.transpose(kernels[layer_index][::-1, ::-1], (0, 1, 3, 2))
        spread = conv_valid(slope, flipped)
        back = lax.optimization_barrier(
            (crop(back, 1).astype(jnp.float32) + spread).astype(jnp.bfloat16)
        )
        grads[layer_index] = tap_grad
    back_flat = back.reshape(cell_count, channels)
    embed_grad = lax.dot_general(
        features, back_flat, (((0,), (0,)), ((), ())), preferred_element_type=jnp.float32
    )
    cell_grad = (
        lax.dot_general(
            back_flat, w_embed, (((1,), (1,)), ((), ())), preferred_element_type=jnp.float32
        )
        * inv_root[:, None]
    ).astype(jnp.bfloat16)
    picked = jnp.dot(onehot, cell_grad, preferred_element_type=jnp.float32).astype(jnp.bfloat16)

    summed, picked = all_sum(grads + [embed_grad], grad_scale, picked)
    grad_obs = lax.all_to_all(picked, ("lon", "lat"), split_axis=0, concat_axis=0, tiled=True)
    tap_rows_n = kernels.size // channels
    kernel_out = summed[:tap_rows_n].reshape(kernels.shape)
    embed_out = summed[tap_rows_n:]
    return (encoded, kernel_out, embed_out, grad_obs)


def solution(mesh):
    placed = (
        P(("lon", "lat"), None),
        P(("lon", "lat")),
        P(("lon", "lat"), None),
        P(),
        P(),
        P(),
        P("lat", "lon", None),
    )
    return jax.shard_map(
        on_device,
        mesh=mesh,
        in_specs=placed,
        out_specs=(P("lat", "lon", None), P(), P(), P(("lon", "lat"), None)),
        check_vma=False,
    )
```

```python
import math

import jax
import jax.numpy as jnp
from jax import lax
from jax.sharding import PartitionSpec as P

ID_BASE = 128


def shift_pairs(count, step, periodic):
    pairs = []
    for source in range(count):
        target = source + step
        if 0 <= target < count:
            pairs.append((source, target))
        elif periodic:
            pairs.append((source, target % count))
    return pairs


def widen(block, depth):
    lon_count = lax.axis_size("lon")
    lat_count = lax.axis_size("lat")
    west = lax.ppermute(block[:, -depth:], "lon", shift_pairs(lon_count, 1, True))
    east = lax.ppermute(block[:, :depth], "lon", shift_pairs(lon_count, -1, True))
    block = jnp.concatenate([west, block, east], axis=1)
    north = lax.ppermute(block[-depth:], "lat", shift_pairs(lat_count, 1, False))
    south = lax.ppermute(block[:depth], "lat", shift_pairs(lat_count, -1, False))
    return jnp.concatenate([north, block, south], axis=0)


def lat_mask(rows, margin, height):
    lat_index = lax.axis_index("lat")
    lat_count = lax.axis_size("lat")
    global_row = lat_index * height - margin + jnp.arange(rows, dtype=jnp.int32)
    return ((global_row >= 0) & (global_row < lat_count * height))[:, None, None]


def crop(field, margin):
    if margin == 0:
        return field
    return field[margin:-margin, margin:-margin]


def conv_valid(padded, kernel):
    return lax.conv_general_dilated(
        padded[None],
        kernel,
        (1, 1),
        "VALID",
        dimension_numbers=("NHWC", "HWIO", "NHWC"),
        preferred_element_type=jnp.float32,
    )[0]


def cube_steps():
    steps = []
    for axis in ("lon", "lat"):
        count = lax.axis_size(axis)
        bit = 1
        while bit < count:
            steps.append((axis, bit, [(i, i ^ bit) for i in range(count)]))
            bit *= 2
    return steps


def reduce_replicated(part, steps):
    for axis, bit, pairs in steps:
        half = part.shape[0] // 2
        mine = (lax.axis_index(axis) // bit) % 2
        keep = lax.dynamic_slice_in_dim(part, mine * half, half)
        give = lax.dynamic_slice_in_dim(part, (1 - mine) * half, half)
        got = lax.ppermute(give.astype(jnp.bfloat16), axis, pairs)
        part = keep + got.astype(jnp.float32)
    return part


def gather_replicated(part, steps):
    for axis, bit, pairs in reversed(steps):
        mine = (lax.axis_index(axis) // bit) % 2
        got = lax.ppermute(part, axis, pairs)
        first = jnp.where(mine == 0, part, got)
        second = jnp.where(mine == 0, got, part)
        part = jnp.concatenate([first, second])
    return part


def all_sum(pieces, scale, hold, streams=3):
    lanes = pieces[0].shape[-1]
    flat = jnp.concatenate([piece.reshape(-1, lanes) for piece in pieces])
    steps = cube_steps()
    devices = 2 ** len(steps)
    unit = devices * 16
    total = flat.shape[0]
    units = -(-total // unit)
    flat = jnp.pad(flat, ((0, units * unit - total), (0, 0)))
    middle = steps[1:-1] if len(steps) > 2 else []
    orders = []
    parts = []
    begin = 0
    for stream in range(streams):
        count = units // streams + (1 if stream < units % streams else 0)
        if count == 0:
            continue
        shift = stream % len(middle) if middle else 0
        order = steps[:1] + middle[shift:] + middle[:shift] + steps[len(middle) + 1 :]
        if len(steps) <= 2:
            order = steps
        parts.append(reduce_replicated(flat[begin : begin + count * unit], order[:2]))
        orders.append(order)
        begin += count * unit
    hold, parts = lax.optimization_barrier((hold, parts))
    outs = []
    for part, order in zip(parts, orders):
        part = reduce_replicated(part, order[2:])
        outs.append(gather_replicated((part * scale).astype(jnp.bfloat16), order))
    return jnp.concatenate(outs)[:total], hold


def on_device(obs_rows, cell_ids, counts, w_embed, w_density, kernels, cotangent):
    lon_count = lax.axis_size("lon")
    lat_count = lax.axis_size("lat")
    devices = lon_count * lat_count
    height, tile_width, channels = cotangent.shape
    cell_count = height * tile_width
    slot_rows = obs_rows.shape[0] // devices
    feat_count = obs_rows.shape[1]
    layer_count = kernels.shape[0]
    margin = 2 * layer_count

    cot_wide = widen(cotangent, layer_count)

    live_mask = jnp.arange(slot_rows, dtype=jnp.int32)[None, :] < counts[0][:, None]
    slot_ids = cell_ids.reshape(devices, slot_rows)
    id_high = jnp.where(live_mask, slot_ids // ID_BASE, -1)
    id_low = jnp.where(live_mask, slot_ids % ID_BASE, -1)
    code = jnp.concatenate([id_high, id_low], axis=1).astype(jnp.bfloat16)
    code_rows = -(-2 * slot_rows // feat_count)
    code_pad = -(-code_rows // 16) * 16
    code = jnp.pad(code, ((0, 0), (0, code_rows * feat_count - 2 * slot_rows)))
    code = code.reshape(devices, code_rows, feat_count)
    code = jnp.pad(code, ((0, 0), (0, code_pad - code_rows), (0, 0)))
    packed = jnp.concatenate([obs_rows.reshape(devices, slot_rows, feat_count), code], axis=1)
    got = lax.all_to_all(packed, ("lon", "lat"), split_axis=0, concat_axis=0, tiled=True)
    got_rows = got[:, :slot_rows].reshape(devices * slot_rows, feat_count)
    got_code = got[:, slot_rows : slot_rows + code_rows].reshape(devices, code_rows * feat_count)
    got_code = got_code.astype(jnp.int32)
    got_ids = (got_code[:, :slot_rows] * ID_BASE + got_code[:, slot_rows : 2 * slot_rows]).reshape(-1)

    cell_iota = jnp.arange(cell_count, dtype=jnp.int32)
    onehot = (got_ids[:, None] == cell_iota[None, :]).astype(jnp.bfloat16)
    cell_sums = lax.dot_general(
        onehot, got_rows, (((0,), (0,)), ((), ())), preferred_element_type=jnp.float32
    )
    density = jnp.sum(onehot.astype(jnp.float32), axis=0)
    inv_root = lax.rsqrt(density + 1.0)
    features = (cell_sums * inv_root[:, None]).astype(jnp.bfloat16)
    start_act = (
        jnp.dot(features, w_embed, preferred_element_type=jnp.float32)
        + jnp.log1p(density)[:, None] * w_density.astype(jnp.float32)[None, :]
    )
    activation = start_act.astype(jnp.bfloat16).reshape(height, tile_width, channels)

    act = widen(activation, margin)
    stored_acts = [act]
    stored_pre = []
    for layer_index in range(layer_count):
        out_margin = margin - layer_index - 1
        preact = conv_valid(act, kernels[layer_index])
        act = (crop(act, 1).astype(jnp.float32) + jax.nn.silu(preact)).astype(jnp.bfloat16)
        act = jnp.where(lat_mask(act.shape[0], out_margin, height), act, jnp.zeros_like(act))
        stored_pre.append(preact)
        stored_acts.append(act)
    encoded = crop(act, margin - layer_count)

    grad_scale = 1.0 / math.sqrt(cell_count * devices)
    back = cot_wide
    grads = [None] * layer_count
    for layer_index in reversed(range(layer_count)):
        back_margin = layer_index + 1
        preact = crop(stored_pre[layer_index], margin - layer_index - 1 - back_margin)
        sigmoid_v = jax.nn.sigmoid(preact)
        slope = (
            back.astype(jnp.float32) * (sigmoid_v * (1.0 + preact * (1.0 - sigmoid_v)))
        ).astype(jnp.bfloat16)
        slope = jnp.where(lat_mask(slope.shape[0], back_margin, height), slope, jnp.zeros_like(slope))
        slope_flat = crop(slope, back_margin).reshape(cell_count, channels)
        act_in = crop(stored_acts[layer_index], margin - layer_index - 1)
        patches = jnp.concatenate(
            [
                act_in[row_off : row_off + height, col_off : col_off + tile_width]
                for row_off in range(3)
                for col_off in range(3)
            ],
            axis=-1,
        ).reshape(cell_count, 9 * channels)
        tap_grad = lax.dot_general(
            patches, slope_flat, (((0,), (0,)), ((), ())), preferred_element_type=jnp.float32
        )
        flipped = jnp.transpose(kernels[layer_index][::-1, ::-1], (0, 1, 3, 2))
        spread = conv_valid(slope, flipped)
        back = lax.optimization_barrier(
            (crop(back, 1).astype(jnp.float32) + spread).astype(jnp.bfloat16)
        )
        grads[layer_index] = tap_grad
    back_flat = back.reshape(cell_count, channels)
    embed_grad = lax.dot_general(
        features, back_flat, (((0,), (0,)), ((), ())), preferred_element_type=jnp.float32
    )
    cell_grad = (
        lax.dot_general(
            back_flat, w_embed, (((1,), (1,)), ((), ())), preferred_element_type=jnp.float32
        )
        * inv_root[:, None]
    ).astype(jnp.bfloat16)
    picked = jnp.dot(onehot, cell_grad, preferred_element_type=jnp.float32).astype(jnp.bfloat16)

    summed, picked = all_sum(grads + [embed_grad], grad_scale, picked)
    grad_obs = lax.all_to_all(picked, ("lon", "lat"), split_axis=0, concat_axis=0, tiled=True)
    tap_rows_n = kernels.size // channels
    kernel_out = summed[:tap_rows_n].reshape(kernels.shape)
    embed_out = summed[tap_rows_n:]
    return (encoded, kernel_out, embed_out, grad_obs)


def solution(mesh):
    placed = (
        P(("lon", "lat"), None),
        P(("lon", "lat")),
        P(("lon", "lat"), None),
        P(),
        P(),
        P(),
        P("lat", "lon", None),
    )
    return jax.shard_map(
        on_device,
        mesh=mesh,
        in_specs=placed,
        out_specs=(P("lat", "lon", None), P(), P(), P(("lon", "lat"), None)),
        check_vma=False,
    )
```

```python
import math

import jax
import jax.numpy as jnp
from jax import lax
from jax.sharding import PartitionSpec as P

ID_BASE = 128


def shift_pairs(count, step, periodic):
    pairs = []
    for source in range(count):
        target = source + step
        if 0 <= target < count:
            pairs.append((source, target))
        elif periodic:
            pairs.append((source, target % count))
    return pairs


def widen(block, depth):
    lon_count = lax.axis_size("lon")
    lat_count = lax.axis_size("lat")
    west = lax.ppermute(block[:, -depth:], "lon", shift_pairs(lon_count, 1, True))
    east = lax.ppermute(block[:, :depth], "lon", shift_pairs(lon_count, -1, True))
    block = jnp.concatenate([west, block, east], axis=1)
    north = lax.ppermute(block[-depth:], "lat", shift_pairs(lat_count, 1, False))
    south = lax.ppermute(block[:depth], "lat", shift_pairs(lat_count, -1, False))
    return jnp.concatenate([north, block, south], axis=0)


def lat_mask(rows, margin, height):
    lat_index = lax.axis_index("lat")
    lat_count = lax.axis_size("lat")
    global_row = lat_index * height - margin + jnp.arange(rows, dtype=jnp.int32)
    return ((global_row >= 0) & (global_row < lat_count * height))[:, None, None]


def crop(field, margin):
    if margin == 0:
        return field
    return field[margin:-margin, margin:-margin]


def conv_valid(padded, kernel):
    return lax.conv_general_dilated(
        padded[None],
        kernel,
        (1, 1),
        "VALID",
        dimension_numbers=("NHWC", "HWIO", "NHWC"),
        preferred_element_type=jnp.float32,
    )[0]


def cube_steps():
    steps = []
    for axis in ("lon", "lat"):
        count = lax.axis_size(axis)
        bit = 1
        while bit < count:
            steps.append((axis, bit, [(i, i ^ bit) for i in range(count)]))
            bit *= 2
    return steps


def reduce_replicated(part, steps):
    for axis, bit, pairs in steps:
        half = part.shape[0] // 2
        mine = (lax.axis_index(axis) // bit) % 2
        keep = lax.dynamic_slice_in_dim(part, mine * half, half)
        give = lax.dynamic_slice_in_dim(part, (1 - mine) * half, half)
        got = lax.ppermute(give.astype(jnp.bfloat16), axis, pairs)
        part = keep + got.astype(jnp.float32)
    return part


def gather_replicated(part, steps):
    for axis, bit, pairs in reversed(steps):
        mine = (lax.axis_index(axis) // bit) % 2
        got = lax.ppermute(part, axis, pairs)
        first = jnp.where(mine == 0, part, got)
        second = jnp.where(mine == 0, got, part)
        part = jnp.concatenate([first, second])
    return part


def all_sum(pieces, scale, hold, streams=3):
    lanes = pieces[0].shape[-1]
    flat = jnp.concatenate([piece.reshape(-1, lanes) for piece in pieces])
    total = flat.shape[0]
    steps = cube_steps()
    if len(steps) < 3:
        unit = (2 ** len(steps)) * 16
        flat = jnp.pad(flat, ((0, -(-total // unit) * unit - total), (0, 0)))
        part = reduce_replicated(flat, steps)
        hold, part = lax.optimization_barrier((hold, part))
        return gather_replicated((part * scale).astype(jnp.bfloat16), steps)[:total], hold
    first, middle, last = steps[:1], steps[1:-1], steps[-1:]
    unit = (2 ** len(middle)) * 32
    units = -(-total // (2 * unit))
    flat = jnp.pad(flat, ((0, 2 * units * unit - total), (0, 0)))
    part = reduce_replicated(flat, first)
    hold, part = lax.optimization_barrier((hold, part))
    orders = []
    segs = []
    begin = 0
    for stream in range(streams):
        count = units // streams + (1 if stream < units % streams else 0)
        if count == 0:
            continue
        shift = stream % len(middle)
        order = middle[shift:] + middle[:shift]
        segs.append(reduce_replicated(part[begin : begin + count * unit], order))
        orders.append(order)
        begin += count * unit
    seg_rows = [seg.shape[0] for seg in segs]
    part = reduce_replicated(jnp.concatenate(segs), last)
    part = gather_replicated((part * scale).astype(jnp.bfloat16), last)
    outs = []
    begin = 0
    for order, rows in zip(orders, seg_rows):
        outs.append(gather_replicated(part[begin : begin + rows], order))
        begin += rows
    return gather_replicated(jnp.concatenate(outs), first)[:total], hold


def on_device(obs_rows, cell_ids, counts, w_embed, w_density, kernels, cotangent):
    lon_count = lax.axis_size("lon")
    lat_count = lax.axis_size("lat")
    devices = lon_count * lat_count
    height, tile_width, channels = cotangent.shape
    cell_count = height * tile_width
    slot_rows = obs_rows.shape[0] // devices
    feat_count = obs_rows.shape[1]
    layer_count = kernels.shape[0]
    margin = 2 * layer_count

    cot_wide = widen(cotangent, layer_count)

    live_mask = jnp.arange(slot_rows, dtype=jnp.int32)[None, :] < counts[0][:, None]
    slot_ids = cell_ids.reshape(devices, slot_rows)
    id_high = jnp.where(live_mask, slot_ids // ID_BASE, -1)
    id_low = jnp.where(live_mask, slot_ids % ID_BASE, -1)
    code = jnp.concatenate([id_high, id_low], axis=1).astype(jnp.bfloat16)
    code_rows = -(-2 * slot_rows // feat_count)
    code_pad = -(-code_rows // 16) * 16
    code = jnp.pad(code, ((0, 0), (0, code_rows * feat_count - 2 * slot_rows)))
    code = code.reshape(devices, code_rows, feat_count)
    code = jnp.pad(code, ((0, 0), (0, code_pad - code_rows), (0, 0)))
    packed = jnp.concatenate([obs_rows.reshape(devices, slot_rows, feat_count), code], axis=1)
    got = lax.all_to_all(packed, ("lon", "lat"), split_axis=0, concat_axis=0, tiled=True)
    got_rows = got[:, :slot_rows].reshape(devices * slot_rows, feat_count)
    got_code = got[:, slot_rows : slot_rows + code_rows].reshape(devices, code_rows * feat_count)
    got_code = got_code.astype(jnp.int32)
    got_ids = (got_code[:, :slot_rows] * ID_BASE + got_code[:, slot_rows : 2 * slot_rows]).reshape(-1)

    cell_iota = jnp.arange(cell_count, dtype=jnp.int32)
    onehot = (got_ids[:, None] == cell_iota[None, :]).astype(jnp.bfloat16)
    cell_sums = lax.dot_general(
        onehot, got_rows, (((0,), (0,)), ((), ())), preferred_element_type=jnp.float32
    )
    density = jnp.sum(onehot.astype(jnp.float32), axis=0)
    inv_root = lax.rsqrt(density + 1.0)
    features = (cell_sums * inv_root[:, None]).astype(jnp.bfloat16)
    start_act = (
        jnp.dot(features, w_embed, preferred_element_type=jnp.float32)
        + jnp.log1p(density)[:, None] * w_density.astype(jnp.float32)[None, :]
    )
    activation = start_act.astype(jnp.bfloat16).reshape(height, tile_width, channels)

    act = widen(activation, margin)
    stored_acts = [act]
    stored_pre = []
    for layer_index in range(layer_count):
        out_margin = margin - layer_index - 1
        preact = conv_valid(act, kernels[layer_index])
        act = (crop(act, 1).astype(jnp.float32) + jax.nn.silu(preact)).astype(jnp.bfloat16)
        act = jnp.where(lat_mask(act.shape[0], out_margin, height), act, jnp.zeros_like(act))
        stored_pre.append(preact)
        stored_acts.append(act)
    encoded = crop(act, margin - layer_count)

    grad_scale = 1.0 / math.sqrt(cell_count * devices)
    back = cot_wide
    grads = [None] * layer_count
    for layer_index in reversed(range(layer_count)):
        back_margin = layer_index + 1
        preact = crop(stored_pre[layer_index], margin - layer_index - 1 - back_margin)
        sigmoid_v = jax.nn.sigmoid(preact)
        slope = (
            back.astype(jnp.float32) * (sigmoid_v * (1.0 + preact * (1.0 - sigmoid_v)))
        ).astype(jnp.bfloat16)
        slope = jnp.where(lat_mask(slope.shape[0], back_margin, height), slope, jnp.zeros_like(slope))
        slope_flat = crop(slope, back_margin).reshape(cell_count, channels)
        act_in = crop(stored_acts[layer_index], margin - layer_index - 1)
        patches = jnp.concatenate(
            [
                act_in[row_off : row_off + height, col_off : col_off + tile_width]
                for row_off in range(3)
                for col_off in range(3)
            ],
            axis=-1,
        ).reshape(cell_count, 9 * channels)
        tap_grad = lax.dot_general(
            patches, slope_flat, (((0,), (0,)), ((), ())), preferred_element_type=jnp.float32
        )
        flipped = jnp.transpose(kernels[layer_index][::-1, ::-1], (0, 1, 3, 2))
        spread = conv_valid(slope, flipped)
        back = lax.optimization_barrier(
            (crop(back, 1).astype(jnp.float32) + spread).astype(jnp.bfloat16)
        )
        grads[layer_index] = tap_grad
    back_flat = back.reshape(cell_count, channels)
    embed_grad = lax.dot_general(
        features, back_flat, (((0,), (0,)), ((), ())), preferred_element_type=jnp.float32
    )
    cell_grad = (
        lax.dot_general(
            back_flat, w_embed, (((1,), (1,)), ((), ())), preferred_element_type=jnp.float32
        )
        * inv_root[:, None]
    ).astype(jnp.bfloat16)
    picked = jnp.dot(onehot, cell_grad, preferred_element_type=jnp.float32).astype(jnp.bfloat16)

    summed, picked = all_sum(grads + [embed_grad], grad_scale, picked)
    grad_obs = lax.all_to_all(picked, ("lon", "lat"), split_axis=0, concat_axis=0, tiled=True)
    tap_rows_n = kernels.size // channels
    kernel_out = summed[:tap_rows_n].reshape(kernels.shape)
    embed_out = summed[tap_rows_n:]
    return (encoded, kernel_out, embed_out, grad_obs)


def solution(mesh):
    placed = (
        P(("lon", "lat"), None),
        P(("lon", "lat")),
        P(("lon", "lat"), None),
        P(),
        P(),
        P(),
        P("lat", "lon", None),
    )
    return jax.shard_map(
        on_device,
        mesh=mesh,
        in_specs=placed,
        out_specs=(P("lat", "lon", None), P(), P(), P(("lon", "lat"), None)),
        check_vma=False,
    )
```

```python
import math

import jax
import jax.numpy as jnp
from jax import lax
from jax.sharding import PartitionSpec as P

ID_BASE = 128


def shift_pairs(count, step, periodic):
    pairs = []
    for source in range(count):
        target = source + step
        if 0 <= target < count:
            pairs.append((source, target))
        elif periodic:
            pairs.append((source, target % count))
    return pairs


def widen(block, depth):
    lon_count = lax.axis_size("lon")
    lat_count = lax.axis_size("lat")
    west = lax.ppermute(block[:, -depth:], "lon", shift_pairs(lon_count, 1, True))
    east = lax.ppermute(block[:, :depth], "lon", shift_pairs(lon_count, -1, True))
    block = jnp.concatenate([west, block, east], axis=1)
    north = lax.ppermute(block[-depth:], "lat", shift_pairs(lat_count, 1, False))
    south = lax.ppermute(block[:depth], "lat", shift_pairs(lat_count, -1, False))
    return jnp.concatenate([north, block, south], axis=0)


def lat_mask(rows, margin, height):
    lat_index = lax.axis_index("lat")
    lat_count = lax.axis_size("lat")
    global_row = lat_index * height - margin + jnp.arange(rows, dtype=jnp.int32)
    return ((global_row >= 0) & (global_row < lat_count * height))[:, None, None]


def crop(field, margin):
    if margin == 0:
        return field
    return field[margin:-margin, margin:-margin]


def conv_valid(padded, kernel):
    return lax.conv_general_dilated(
        padded[None],
        kernel,
        (1, 1),
        "VALID",
        dimension_numbers=("NHWC", "HWIO", "NHWC"),
        preferred_element_type=jnp.float32,
    )[0]


def cube_steps():
    steps = []
    for axis in ("lon", "lat"):
        count = lax.axis_size(axis)
        bit = 1
        while bit < count:
            steps.append((axis, bit, [(i, i ^ bit) for i in range(count)]))
            bit *= 2
    return steps


def reduce_replicated(part, steps):
    for axis, bit, pairs in steps:
        half = part.shape[0] // 2
        mine = (lax.axis_index(axis) // bit) % 2
        keep = lax.dynamic_slice_in_dim(part, mine * half, half)
        give = lax.dynamic_slice_in_dim(part, (1 - mine) * half, half)
        got = lax.ppermute(give.astype(jnp.bfloat16), axis, pairs)
        part = keep + got.astype(jnp.float32)
    return part


def gather_replicated(part, steps):
    for axis, bit, pairs in reversed(steps):
        mine = (lax.axis_index(axis) // bit) % 2
        got = lax.ppermute(part, axis, pairs)
        first = jnp.where(mine == 0, part, got)
        second = jnp.where(mine == 0, got, part)
        part = jnp.concatenate([first, second])
    return part


def all_sum(pieces, scale, hold, streams=2):
    lanes = pieces[0].shape[-1]
    flat = jnp.concatenate([piece.reshape(-1, lanes) for piece in pieces])
    steps = cube_steps()
    devices = 2 ** len(steps)
    unit = devices * 16
    total = flat.shape[0]
    units = -(-total // unit)
    flat = jnp.pad(flat, ((0, units * unit - total), (0, 0)))
    middle = steps[1:-1] if len(steps) > 2 else []
    orders = []
    parts = []
    begin = 0
    for stream in range(streams):
        count = units // streams + (1 if stream < units % streams else 0)
        if count == 0:
            continue
        shift = stream % len(middle) if middle else 0
        order = steps[:1] + middle[shift:] + middle[:shift] + steps[len(middle) + 1 :]
        if len(steps) <= 2:
            order = steps
        parts.append(reduce_replicated(flat[begin : begin + count * unit], order[:1]))
        orders.append(order)
        begin += count * unit
    hold, parts = lax.optimization_barrier((hold, parts))
    outs = []
    for part, order in zip(parts, orders):
        part = reduce_replicated(part, order[1:])
        outs.append(gather_replicated((part * scale).astype(jnp.bfloat16), order))
    return jnp.concatenate(outs)[:total], hold


def on_device(obs_rows, cell_ids, counts, w_embed, w_density, kernels, cotangent):
    lon_count = lax.axis_size("lon")
    lat_count = lax.axis_size("lat")
    devices = lon_count * lat_count
    height, tile_width, channels = cotangent.shape
    cell_count = height * tile_width
    slot_rows = obs_rows.shape[0] // devices
    feat_count = obs_rows.shape[1]
    layer_count = kernels.shape[0]
    margin = 2 * layer_count

    cot_wide = widen(cotangent, layer_count)

    live_mask = jnp.arange(slot_rows, dtype=jnp.int32)[None, :] < counts[0][:, None]
    slot_ids = cell_ids.reshape(devices, slot_rows)
    id_high = jnp.where(live_mask, slot_ids // ID_BASE, -1)
    id_low = jnp.where(live_mask, slot_ids % ID_BASE, -1)
    code = jnp.concatenate([id_high, id_low], axis=1).astype(jnp.bfloat16)
    code_rows = -(-2 * slot_rows // feat_count)
    code_pad = -(-code_rows // 16) * 16
    code = jnp.pad(code, ((0, 0), (0, code_rows * feat_count - 2 * slot_rows)))
    code = code.reshape(devices, code_rows, feat_count)
    code = jnp.pad(code, ((0, 0), (0, code_pad - code_rows), (0, 0)))
    packed = jnp.concatenate([obs_rows.reshape(devices, slot_rows, feat_count), code], axis=1)
    got = lax.all_to_all(packed, ("lon", "lat"), split_axis=0, concat_axis=0, tiled=True)
    got_rows = got[:, :slot_rows].reshape(devices * slot_rows, feat_count)
    got_code = got[:, slot_rows : slot_rows + code_rows].reshape(devices, code_rows * feat_count)
    got_code = got_code.astype(jnp.int32)
    got_ids = (got_code[:, :slot_rows] * ID_BASE + got_code[:, slot_rows : 2 * slot_rows]).reshape(-1)

    cell_iota = jnp.arange(cell_count, dtype=jnp.int32)
    onehot = (got_ids[:, None] == cell_iota[None, :]).astype(jnp.bfloat16)
    cell_sums = lax.dot_general(
        onehot, got_rows, (((0,), (0,)), ((), ())), preferred_element_type=jnp.float32
    )
    density = jnp.sum(onehot.astype(jnp.float32), axis=0)
    inv_root = lax.rsqrt(density + 1.0)
    features = (cell_sums * inv_root[:, None]).astype(jnp.bfloat16)
    start_act = (
        jnp.dot(features, w_embed, preferred_element_type=jnp.float32)
        + jnp.log1p(density)[:, None] * w_density.astype(jnp.float32)[None, :]
    )
    activation = start_act.astype(jnp.bfloat16).reshape(height, tile_width, channels)

    act = widen(activation, margin)
    stored_acts = [act]
    stored_pre = []
    for layer_index in range(layer_count):
        out_margin = margin - layer_index - 1
        preact = conv_valid(act, kernels[layer_index])
        act = (crop(act, 1).astype(jnp.float32) + jax.nn.silu(preact)).astype(jnp.bfloat16)
        act = jnp.where(lat_mask(act.shape[0], out_margin, height), act, jnp.zeros_like(act))
        stored_pre.append(preact)
        stored_acts.append(act)
    encoded = crop(act, margin - layer_count)

    grad_scale = 1.0 / math.sqrt(cell_count * devices)
    back = cot_wide
    grads = [None] * layer_count
    for layer_index in reversed(range(layer_count)):
        back_margin = layer_index + 1
        preact = crop(stored_pre[layer_index], margin - layer_index - 1 - back_margin)
        sigmoid_v = jax.nn.sigmoid(preact)
        slope = (
            back.astype(jnp.float32) * (sigmoid_v * (1.0 + preact * (1.0 - sigmoid_v)))
        ).astype(jnp.bfloat16)
        slope = jnp.where(lat_mask(slope.shape[0], back_margin, height), slope, jnp.zeros_like(slope))
        slope_flat = crop(slope, back_margin).reshape(cell_count, channels)
        act_in = crop(stored_acts[layer_index], margin - layer_index - 1)
        patches = jnp.concatenate(
            [
                act_in[row_off : row_off + height, col_off : col_off + tile_width]
                for row_off in range(3)
                for col_off in range(3)
            ],
            axis=-1,
        ).reshape(cell_count, 9 * channels)
        tap_grad = lax.dot_general(
            patches, slope_flat, (((0,), (0,)), ((), ())), preferred_element_type=jnp.float32
        )
        flipped = jnp.transpose(kernels[layer_index][::-1, ::-1], (0, 1, 3, 2))
        spread = conv_valid(slope, flipped)
        back = lax.optimization_barrier(
            (crop(back, 1).astype(jnp.float32) + spread).astype(jnp.bfloat16)
        )
        grads[layer_index] = tap_grad
    back_flat = back.reshape(cell_count, channels)
    embed_grad = lax.dot_general(
        features, back_flat, (((0,), (0,)), ((), ())), preferred_element_type=jnp.float32
    )
    cell_grad = (
        lax.dot_general(
            back_flat, w_embed, (((1,), (1,)), ((), ())), preferred_element_type=jnp.float32
        )
        * inv_root[:, None]
    ).astype(jnp.bfloat16)
    picked = jnp.dot(onehot, cell_grad, preferred_element_type=jnp.float32).astype(jnp.bfloat16)

    summed, picked = all_sum(grads + [embed_grad], grad_scale, picked)
    grad_obs = lax.all_to_all(picked, ("lon", "lat"), split_axis=0, concat_axis=0, tiled=True)
    tap_rows_n = kernels.size // channels
    kernel_out = summed[:tap_rows_n].reshape(kernels.shape)
    embed_out = summed[tap_rows_n:]
    return (encoded, kernel_out, embed_out, grad_obs)


def solution(mesh):
    placed = (
        P(("lon", "lat"), None),
        P(("lon", "lat")),
        P(("lon", "lat"), None),
        P(),
        P(),
        P(),
        P("lat", "lon", None),
    )
    return jax.shard_map(
        on_device,
        mesh=mesh,
        in_specs=placed,
        out_specs=(P("lat", "lon", None), P(), P(), P(("lon", "lat"), None)),
        check_vma=False,
    )
```

```python
import math

import jax
import jax.numpy as jnp
from jax import lax
from jax.sharding import PartitionSpec as P

ID_BASE = 128


def shift_pairs(count, step, periodic):
    pairs = []
    for source in range(count):
        target = source + step
        if 0 <= target < count:
            pairs.append((source, target))
        elif periodic:
            pairs.append((source, target % count))
    return pairs


def widen(block, depth):
    lon_count = lax.axis_size("lon")
    lat_count = lax.axis_size("lat")
    west = lax.ppermute(block[:, -depth:], "lon", shift_pairs(lon_count, 1, True))
    east = lax.ppermute(block[:, :depth], "lon", shift_pairs(lon_count, -1, True))
    block = jnp.concatenate([west, block, east], axis=1)
    north = lax.ppermute(block[-depth:], "lat", shift_pairs(lat_count, 1, False))
    south = lax.ppermute(block[:depth], "lat", shift_pairs(lat_count, -1, False))
    return jnp.concatenate([north, block, south], axis=0)


def lat_mask(rows, margin, height):
    lat_index = lax.axis_index("lat")
    lat_count = lax.axis_size("lat")
    global_row = lat_index * height - margin + jnp.arange(rows, dtype=jnp.int32)
    return ((global_row >= 0) & (global_row < lat_count * height))[:, None, None]


def crop(field, margin):
    if margin == 0:
        return field
    return field[margin:-margin, margin:-margin]


def conv_valid(padded, kernel):
    return lax.conv_general_dilated(
        padded[None],
        kernel,
        (1, 1),
        "VALID",
        dimension_numbers=("NHWC", "HWIO", "NHWC"),
        preferred_element_type=jnp.float32,
    )[0]


def cube_steps():
    steps = []
    for axis in ("lon", "lat"):
        count = lax.axis_size(axis)
        bit = 1
        while bit < count:
            steps.append((axis, bit, [(i, i ^ bit) for i in range(count)]))
            bit *= 2
    return steps


def reduce_replicated(part, steps):
    for axis, bit, pairs in steps:
        half = part.shape[0] // 2
        mine = (lax.axis_index(axis) // bit) % 2
        keep = lax.dynamic_slice_in_dim(part, mine * half, half)
        give = lax.dynamic_slice_in_dim(part, (1 - mine) * half, half)
        got = lax.ppermute(give.astype(jnp.bfloat16), axis, pairs)
        part = keep + got.astype(jnp.float32)
    return part


def gather_replicated(part, steps):
    for axis, bit, pairs in reversed(steps):
        mine = (lax.axis_index(axis) // bit) % 2
        got = lax.ppermute(part, axis, pairs)
        first = jnp.where(mine == 0, part, got)
        second = jnp.where(mine == 0, got, part)
        part = jnp.concatenate([first, second])
    return part


def all_sum(pieces, scale, hold, streams=2):
    lanes = pieces[0].shape[-1]
    flat = jnp.concatenate([piece.reshape(-1, lanes) for piece in pieces])
    steps = cube_steps()
    devices = 2 ** len(steps)
    unit = devices * 16
    total = flat.shape[0]
    units = -(-total // unit)
    flat = jnp.pad(flat, ((0, units * unit - total), (0, 0)))
    middle = steps[1:-1] if len(steps) > 2 else []
    orders = []
    parts = []
    begin = 0
    for stream in range(streams):
        count = units // streams + (1 if stream < units % streams else 0)
        if count == 0:
            continue
        shift = stream % len(middle) if middle else 0
        order = steps[:1] + middle[shift:] + middle[:shift] + steps[len(middle) + 1 :]
        if len(steps) <= 2:
            order = steps
        parts.append(reduce_replicated(flat[begin : begin + count * unit], order[:1]))
        orders.append(order)
        begin += count * unit
    hold, parts = lax.optimization_barrier((hold, parts))
    outs = []
    for part, order in zip(parts, orders):
        part = reduce_replicated(part, order[1:])
        outs.append(gather_replicated((part * scale).astype(jnp.bfloat16), order))
    return jnp.concatenate(outs)[:total], hold


def on_device(obs_rows, cell_ids, counts, w_embed, w_density, kernels, cotangent):
    lon_count = lax.axis_size("lon")
    lat_count = lax.axis_size("lat")
    devices = lon_count * lat_count
    height, tile_width, channels = cotangent.shape
    cell_count = height * tile_width
    slot_rows = obs_rows.shape[0] // devices
    feat_count = obs_rows.shape[1]
    layer_count = kernels.shape[0]
    margin = 2 * layer_count

    live_mask = jnp.arange(slot_rows, dtype=jnp.int32)[None, :] < counts[0][:, None]
    slot_ids = cell_ids.reshape(devices, slot_rows)
    id_high = jnp.where(live_mask, slot_ids // ID_BASE, -1)
    id_low = jnp.where(live_mask, slot_ids % ID_BASE, -1)
    code = jnp.concatenate([id_high, id_low], axis=1).astype(jnp.bfloat16)
    code_rows = -(-2 * slot_rows // feat_count)
    code_pad = -(-code_rows // 16) * 16
    code = jnp.pad(code, ((0, 0), (0, code_rows * feat_count - 2 * slot_rows)))
    code = code.reshape(devices, code_rows, feat_count)
    code = jnp.pad(code, ((0, 0), (0, code_pad - code_rows), (0, 0)))
    packed = jnp.concatenate([obs_rows.reshape(devices, slot_rows, feat_count), code], axis=1)
    got = lax.all_to_all(packed, ("lon", "lat"), split_axis=0, concat_axis=0, tiled=True)
    got_rows = got[:, :slot_rows].reshape(devices * slot_rows, feat_count)
    got_code = got[:, slot_rows : slot_rows + code_rows].reshape(devices, code_rows * feat_count)
    got_code = got_code.astype(jnp.int32)
    got_ids = (got_code[:, :slot_rows] * ID_BASE + got_code[:, slot_rows : 2 * slot_rows]).reshape(-1)

    cell_iota = jnp.arange(cell_count, dtype=jnp.int32)
    onehot = (got_ids[:, None] == cell_iota[None, :]).astype(jnp.bfloat16)
    cell_sums = lax.dot_general(
        onehot, got_rows, (((0,), (0,)), ((), ())), preferred_element_type=jnp.float32
    )
    density = jnp.sum(onehot.astype(jnp.float32), axis=0)
    inv_root = lax.rsqrt(density + 1.0)
    features = (cell_sums * inv_root[:, None]).astype(jnp.bfloat16)
    start_act = (
        jnp.dot(features, w_embed, preferred_element_type=jnp.float32)
        + jnp.log1p(density)[:, None] * w_density.astype(jnp.float32)[None, :]
    )
    activation = start_act.astype(jnp.bfloat16).reshape(height, tile_width, channels)

    wide = widen(jnp.concatenate([activation, cotangent], axis=-1), margin)
    act = wide[..., :channels]
    cot_wide = crop(wide[..., channels:], margin - layer_count)
    stored_acts = [act]
    stored_pre = []
    for layer_index in range(layer_count):
        out_margin = margin - layer_index - 1
        preact = conv_valid(act, kernels[layer_index])
        act = (crop(act, 1).astype(jnp.float32) + jax.nn.silu(preact)).astype(jnp.bfloat16)
        act = jnp.where(lat_mask(act.shape[0], out_margin, height), act, jnp.zeros_like(act))
        stored_pre.append(preact)
        stored_acts.append(act)
    encoded = crop(act, margin - layer_count)

    grad_scale = 1.0 / math.sqrt(cell_count * devices)
    back = cot_wide
    grads = [None] * layer_count
    for layer_index in reversed(range(layer_count)):
        back_margin = layer_index + 1
        preact = crop(stored_pre[layer_index], margin - layer_index - 1 - back_margin)
        sigmoid_v = jax.nn.sigmoid(preact)
        slope = (
            back.astype(jnp.float32) * (sigmoid_v * (1.0 + preact * (1.0 - sigmoid_v)))
        ).astype(jnp.bfloat16)
        slope = jnp.where(lat_mask(slope.shape[0], back_margin, height), slope, jnp.zeros_like(slope))
        slope_flat = crop(slope, back_margin).reshape(cell_count, channels)
        act_in = crop(stored_acts[layer_index], margin - layer_index - 1)
        patches = jnp.concatenate(
            [
                act_in[row_off : row_off + height, col_off : col_off + tile_width]
                for row_off in range(3)
                for col_off in range(3)
            ],
            axis=-1,
        ).reshape(cell_count, 9 * channels)
        tap_grad = lax.dot_general(
            patches, slope_flat, (((0,), (0,)), ((), ())), preferred_element_type=jnp.float32
        )
        flipped = jnp.transpose(kernels[layer_index][::-1, ::-1], (0, 1, 3, 2))
        spread = conv_valid(slope, flipped)
        back = lax.optimization_barrier(
            (crop(back, 1).astype(jnp.float32) + spread).astype(jnp.bfloat16)
        )
        grads[layer_index] = tap_grad
    back_flat = back.reshape(cell_count, channels)
    embed_grad = lax.dot_general(
        features, back_flat, (((0,), (0,)), ((), ())), preferred_element_type=jnp.float32
    )
    cell_grad = (
        lax.dot_general(
            back_flat, w_embed, (((1,), (1,)), ((), ())), preferred_element_type=jnp.float32
        )
        * inv_root[:, None]
    ).astype(jnp.bfloat16)
    picked = jnp.dot(onehot, cell_grad, preferred_element_type=jnp.float32).astype(jnp.bfloat16)

    summed, picked = all_sum(grads + [embed_grad], grad_scale, picked)
    grad_obs = lax.all_to_all(picked, ("lon", "lat"), split_axis=0, concat_axis=0, tiled=True)
    tap_rows_n = kernels.size // channels
    kernel_out = summed[:tap_rows_n].reshape(kernels.shape)
    embed_out = summed[tap_rows_n:]
    return (encoded, kernel_out, embed_out, grad_obs)


def solution(mesh):
    placed = (
        P(("lon", "lat"), None),
        P(("lon", "lat")),
        P(("lon", "lat"), None),
        P(),
        P(),
        P(),
        P("lat", "lon", None),
    )
    return jax.shard_map(
        on_device,
        mesh=mesh,
        in_specs=placed,
        out_specs=(P("lat", "lon", None), P(), P(), P(("lon", "lat"), None)),
        check_vma=False,
    )
```

```python
import math

import jax
import jax.numpy as jnp
from jax import lax
from jax.sharding import PartitionSpec as P

ID_BASE = 128


def shift_pairs(count, step, periodic):
    pairs = []
    for source in range(count):
        target = source + step
        if 0 <= target < count:
            pairs.append((source, target))
        elif periodic:
            pairs.append((source, target % count))
    return pairs


def widen(block, depth):
    lon_count = lax.axis_size("lon")
    lat_count = lax.axis_size("lat")
    west = lax.ppermute(block[:, -depth:], "lon", shift_pairs(lon_count, 1, True))
    east = lax.ppermute(block[:, :depth], "lon", shift_pairs(lon_count, -1, True))
    block = jnp.concatenate([west, block, east], axis=1)
    north = lax.ppermute(block[-depth:], "lat", shift_pairs(lat_count, 1, False))
    south = lax.ppermute(block[:depth], "lat", shift_pairs(lat_count, -1, False))
    return jnp.concatenate([north, block, south], axis=0)


def lat_mask(rows, margin, height):
    lat_index = lax.axis_index("lat")
    lat_count = lax.axis_size("lat")
    global_row = lat_index * height - margin + jnp.arange(rows, dtype=jnp.int32)
    return ((global_row >= 0) & (global_row < lat_count * height))[:, None, None]


def crop(field, margin):
    if margin == 0:
        return field
    return field[margin:-margin, margin:-margin]


def conv_valid(padded, kernel):
    return lax.conv_general_dilated(
        padded[None],
        kernel,
        (1, 1),
        "VALID",
        dimension_numbers=("NHWC", "HWIO", "NHWC"),
        preferred_element_type=jnp.float32,
    )[0]


def cube_steps():
    steps = []
    for axis in ("lon", "lat"):
        count = lax.axis_size(axis)
        bit = 1
        while bit < count:
            steps.append((axis, bit, [(i, i ^ bit) for i in range(count)]))
            bit *= 2
    return steps


def reduce_replicated(part, steps):
    for axis, bit, pairs in steps:
        half = part.shape[0] // 2
        mine = (lax.axis_index(axis) // bit) % 2
        keep = lax.dynamic_slice_in_dim(part, mine * half, half)
        give = lax.dynamic_slice_in_dim(part, (1 - mine) * half, half)
        got = lax.ppermute(give.astype(jnp.bfloat16), axis, pairs)
        part = keep + got.astype(jnp.float32)
    return part


def gather_replicated(part, steps):
    for axis, bit, pairs in reversed(steps):
        mine = (lax.axis_index(axis) // bit) % 2
        got = lax.ppermute(part, axis, pairs)
        first = jnp.where(mine == 0, part, got)
        second = jnp.where(mine == 0, got, part)
        part = jnp.concatenate([first, second])
    return part


def all_sum(pieces, scale, hold, streams=2):
    lanes = pieces[0].shape[-1]
    flat = jnp.concatenate([piece.reshape(-1, lanes) for piece in pieces])
    steps = cube_steps()
    devices = 2 ** len(steps)
    unit = devices * 16
    total = flat.shape[0]
    units = -(-total // unit)
    flat = jnp.pad(flat, ((0, units * unit - total), (0, 0)))
    middle = steps[1:-1] if len(steps) > 2 else []
    orders = []
    parts = []
    begin = 0
    for stream in range(streams):
        count = units // streams + (1 if stream < units % streams else 0)
        if count == 0:
            continue
        shift = stream % len(middle) if middle else 0
        order = steps[:1] + middle[shift:] + middle[:shift] + steps[len(middle) + 1 :]
        if len(steps) <= 2:
            order = steps
        parts.append(reduce_replicated(flat[begin : begin + count * unit], order[:1]))
        orders.append(order)
        begin += count * unit
    hold, parts = lax.optimization_barrier((hold, parts))
    outs = []
    for part, order in zip(parts, orders):
        part = reduce_replicated(part, order[1:])
        outs.append(gather_replicated((part * scale).astype(jnp.bfloat16), order))
    return jnp.concatenate(outs)[:total], hold


def on_device(obs_rows, cell_ids, counts, w_embed, w_density, kernels, cotangent):
    lon_count = lax.axis_size("lon")
    lat_count = lax.axis_size("lat")
    devices = lon_count * lat_count
    height, tile_width, channels = cotangent.shape
    cell_count = height * tile_width
    slot_rows = obs_rows.shape[0] // devices
    feat_count = obs_rows.shape[1]
    layer_count = kernels.shape[0]
    margin = 2 * layer_count

    cot_wide = widen(cotangent, layer_count)

    live_mask = jnp.arange(slot_rows, dtype=jnp.int32)[None, :] < counts[0][:, None]
    slot_ids = cell_ids.reshape(devices, slot_rows)
    id_high = jnp.where(live_mask, slot_ids // ID_BASE, -1)
    id_low = jnp.where(live_mask, slot_ids % ID_BASE, -1)
    code = jnp.concatenate([id_high, id_low], axis=1).astype(jnp.bfloat16)
    code_rows = -(-2 * slot_rows // feat_count)
    code_pad = -(-code_rows // 16) * 16
    code = jnp.pad(code, ((0, 0), (0, code_rows * feat_count - 2 * slot_rows)))
    code = code.reshape(devices, code_rows, feat_count)
    code = jnp.pad(code, ((0, 0), (0, code_pad - code_rows), (0, 0)))
    packed = jnp.concatenate([obs_rows.reshape(devices, slot_rows, feat_count), code], axis=1)
    got = lax.all_to_all(packed, ("lon", "lat"), split_axis=0, concat_axis=0, tiled=True)
    got_rows = got[:, :slot_rows].reshape(devices * slot_rows, feat_count)
    got_code = got[:, slot_rows : slot_rows + code_rows].reshape(devices, code_rows * feat_count)
    got_code = got_code.astype(jnp.int32)
    got_ids = (got_code[:, :slot_rows] * ID_BASE + got_code[:, slot_rows : 2 * slot_rows]).reshape(-1)

    cell_iota = jnp.arange(cell_count, dtype=jnp.int32)
    onehot = (got_ids[:, None] == cell_iota[None, :]).astype(jnp.bfloat16)
    cell_sums = lax.dot_general(
        onehot, got_rows, (((0,), (0,)), ((), ())), preferred_element_type=jnp.float32
    )
    density = jnp.sum(onehot.astype(jnp.float32), axis=0)
    inv_root = lax.rsqrt(density + 1.0)
    features = (cell_sums * inv_root[:, None]).astype(jnp.bfloat16)
    start_act = (
        jnp.dot(features, w_embed, preferred_element_type=jnp.float32)
        + jnp.log1p(density)[:, None] * w_density.astype(jnp.float32)[None, :]
    )
    activation = start_act.astype(jnp.bfloat16).reshape(height, tile_width, channels)

    act = widen(activation, margin)
    stored_acts = [act]
    stored_pre = []
    for layer_index in range(layer_count):
        out_margin = margin - layer_index - 1
        preact = conv_valid(act, kernels[layer_index])
        act = (crop(act, 1).astype(jnp.float32) + jax.nn.silu(preact)).astype(jnp.bfloat16)
        act = jnp.where(lat_mask(act.shape[0], out_margin, height), act, jnp.zeros_like(act))
        stored_pre.append(preact)
        stored_acts.append(act)
    encoded = crop(act, margin - layer_count)

    grad_scale = 1.0 / math.sqrt(cell_count * devices)
    back = cot_wide
    grads = [None] * layer_count
    for layer_index in reversed(range(layer_count)):
        back_margin = layer_index + 1
        preact = crop(stored_pre[layer_index], margin - layer_index - 1 - back_margin)
        sigmoid_v = jax.nn.sigmoid(preact)
        slope = (
            back.astype(jnp.float32) * (sigmoid_v * (1.0 + preact * (1.0 - sigmoid_v)))
        ).astype(jnp.bfloat16)
        slope = jnp.where(lat_mask(slope.shape[0], back_margin, height), slope, jnp.zeros_like(slope))
        slope_flat = crop(slope, back_margin).reshape(cell_count, channels)
        act_in = crop(stored_acts[layer_index], margin - layer_index - 1)
        patches = jnp.concatenate(
            [
                act_in[row_off : row_off + height, col_off : col_off + tile_width]
                for row_off in range(3)
                for col_off in range(3)
            ],
            axis=-1,
        ).reshape(cell_count, 9 * channels)
        tap_grad = lax.dot_general(
            patches, slope_flat, (((0,), (0,)), ((), ())), preferred_element_type=jnp.float32
        )
        flipped = jnp.transpose(kernels[layer_index][::-1, ::-1], (0, 1, 3, 2))
        spread = conv_valid(slope, flipped)
        back = (crop(back, 1).astype(jnp.float32) + spread).astype(jnp.bfloat16)
        grads[layer_index] = tap_grad
    back_flat = back.reshape(cell_count, channels)
    embed_grad = lax.dot_general(
        features, back_flat, (((0,), (0,)), ((), ())), preferred_element_type=jnp.float32
    )
    cell_grad = (
        lax.dot_general(
            back_flat, w_embed, (((1,), (1,)), ((), ())), preferred_element_type=jnp.float32
        )
        * inv_root[:, None]
    ).astype(jnp.bfloat16)
    picked = jnp.dot(onehot, cell_grad, preferred_element_type=jnp.float32).astype(jnp.bfloat16)

    summed, picked = all_sum(grads + [embed_grad], grad_scale, picked)
    grad_obs = lax.all_to_all(picked, ("lon", "lat"), split_axis=0, concat_axis=0, tiled=True)
    tap_rows_n = kernels.size // channels
    kernel_out = summed[:tap_rows_n].reshape(kernels.shape)
    embed_out = summed[tap_rows_n:]
    return (encoded, kernel_out, embed_out, grad_obs)


def solution(mesh):
    placed = (
        P(("lon", "lat"), None),
        P(("lon", "lat")),
        P(("lon", "lat"), None),
        P(),
        P(),
        P(),
        P("lat", "lon", None),
    )
    return jax.shard_map(
        on_device,
        mesh=mesh,
        in_specs=placed,
        out_specs=(P("lat", "lon", None), P(), P(), P(("lon", "lat"), None)),
        check_vma=False,
    )
```

```python
import math

import jax
import jax.numpy as jnp
from jax import lax
from jax.sharding import PartitionSpec as P

ID_BASE = 128


def shift_pairs(count, step, periodic):
    pairs = []
    for source in range(count):
        target = source + step
        if 0 <= target < count:
            pairs.append((source, target))
        elif periodic:
            pairs.append((source, target % count))
    return pairs


def widen(block, depth):
    lon_count = lax.axis_size("lon")
    lat_count = lax.axis_size("lat")
    west = lax.ppermute(block[:, -depth:], "lon", shift_pairs(lon_count, 1, True))
    east = lax.ppermute(block[:, :depth], "lon", shift_pairs(lon_count, -1, True))
    block = jnp.concatenate([west, block, east], axis=1)
    north = lax.ppermute(block[-depth:], "lat", shift_pairs(lat_count, 1, False))
    south = lax.ppermute(block[:depth], "lat", shift_pairs(lat_count, -1, False))
    return jnp.concatenate([north, block, south], axis=0)


def lat_mask(rows, margin, height):
    lat_index = lax.axis_index("lat")
    lat_count = lax.axis_size("lat")
    global_row = lat_index * height - margin + jnp.arange(rows, dtype=jnp.int32)
    return ((global_row >= 0) & (global_row < lat_count * height))[:, None, None]


def crop(field, margin):
    if margin == 0:
        return field
    return field[margin:-margin, margin:-margin]


def conv_valid(padded, kernel):
    return lax.conv_general_dilated(
        padded[None],
        kernel,
        (1, 1),
        "VALID",
        dimension_numbers=("NHWC", "HWIO", "NHWC"),
        preferred_element_type=jnp.float32,
    )[0]


def cube_steps():
    steps = []
    for axis in ("lon", "lat"):
        count = lax.axis_size(axis)
        bit = 1
        while bit < count:
            steps.append((axis, bit, [(i, i ^ bit) for i in range(count)]))
            bit *= 2
    return steps


def reduce_replicated(part, steps):
    for axis, bit, pairs in steps:
        half = part.shape[0] // 2
        mine = (lax.axis_index(axis) // bit) % 2
        keep = lax.dynamic_slice_in_dim(part, mine * half, half)
        give = lax.dynamic_slice_in_dim(part, (1 - mine) * half, half)
        got = lax.ppermute(give.astype(jnp.bfloat16), axis, pairs)
        part = keep + got.astype(jnp.float32)
    return part


def gather_replicated(part, steps):
    for axis, bit, pairs in reversed(steps):
        mine = (lax.axis_index(axis) // bit) % 2
        got = lax.ppermute(part, axis, pairs)
        size = part.shape[0]
        joined = jnp.zeros((2 * size,) + part.shape[1:], part.dtype)
        joined = lax.dynamic_update_slice_in_dim(joined, part, mine * size, 0)
        part = lax.dynamic_update_slice_in_dim(joined, got, (1 - mine) * size, 0)
    return part


def all_sum(pieces, scale, hold, streams=2):
    lanes = pieces[0].shape[-1]
    flat = jnp.concatenate([piece.reshape(-1, lanes) for piece in pieces])
    steps = cube_steps()
    devices = 2 ** len(steps)
    unit = devices * 16
    total = flat.shape[0]
    units = -(-total // unit)
    flat = jnp.pad(flat, ((0, units * unit - total), (0, 0)))
    middle = steps[1:-1] if len(steps) > 2 else []
    orders = []
    parts = []
    begin = 0
    for stream in range(streams):
        count = units // streams + (1 if stream < units % streams else 0)
        if count == 0:
            continue
        shift = stream % len(middle) if middle else 0
        order = steps[:1] + middle[shift:] + middle[:shift] + steps[len(middle) + 1 :]
        if len(steps) <= 2:
            order = steps
        parts.append(reduce_replicated(flat[begin : begin + count * unit], order[:1]))
        orders.append(order)
        begin += count * unit
    hold, parts = lax.optimization_barrier((hold, parts))
    outs = []
    for part, order in zip(parts, orders):
        part = reduce_replicated(part, order[1:])
        outs.append(gather_replicated((part * scale).astype(jnp.bfloat16), order))
    return jnp.concatenate(outs)[:total], hold


def on_device(obs_rows, cell_ids, counts, w_embed, w_density, kernels, cotangent):
    lon_count = lax.axis_size("lon")
    lat_count = lax.axis_size("lat")
    devices = lon_count * lat_count
    height, tile_width, channels = cotangent.shape
    cell_count = height * tile_width
    slot_rows = obs_rows.shape[0] // devices
    feat_count = obs_rows.shape[1]
    layer_count = kernels.shape[0]
    margin = 2 * layer_count

    cot_wide = widen(cotangent, layer_count)

    live_mask = jnp.arange(slot_rows, dtype=jnp.int32)[None, :] < counts[0][:, None]
    slot_ids = cell_ids.reshape(devices, slot_rows)
    id_high = jnp.where(live_mask, slot_ids // ID_BASE, -1)
    id_low = jnp.where(live_mask, slot_ids % ID_BASE, -1)
    code = jnp.concatenate([id_high, id_low], axis=1).astype(jnp.bfloat16)
    code_rows = -(-2 * slot_rows // feat_count)
    code_pad = -(-code_rows // 16) * 16
    code = jnp.pad(code, ((0, 0), (0, code_rows * feat_count - 2 * slot_rows)))
    code = code.reshape(devices, code_rows, feat_count)
    code = jnp.pad(code, ((0, 0), (0, code_pad - code_rows), (0, 0)))
    packed = jnp.concatenate([obs_rows.reshape(devices, slot_rows, feat_count), code], axis=1)
    got = lax.all_to_all(packed, ("lon", "lat"), split_axis=0, concat_axis=0, tiled=True)
    got_rows = got[:, :slot_rows].reshape(devices * slot_rows, feat_count)
    got_code = got[:, slot_rows : slot_rows + code_rows].reshape(devices, code_rows * feat_count)
    got_code = got_code.astype(jnp.int32)
    got_ids = (got_code[:, :slot_rows] * ID_BASE + got_code[:, slot_rows : 2 * slot_rows]).reshape(-1)

    cell_iota = jnp.arange(cell_count, dtype=jnp.int32)
    onehot = (got_ids[:, None] == cell_iota[None, :]).astype(jnp.bfloat16)
    cell_sums = lax.dot_general(
        onehot, got_rows, (((0,), (0,)), ((), ())), preferred_element_type=jnp.float32
    )
    density = jnp.sum(onehot.astype(jnp.float32), axis=0)
    inv_root = lax.rsqrt(density + 1.0)
    features = (cell_sums * inv_root[:, None]).astype(jnp.bfloat16)
    start_act = (
        jnp.dot(features, w_embed, preferred_element_type=jnp.float32)
        + jnp.log1p(density)[:, None] * w_density.astype(jnp.float32)[None, :]
    )
    activation = start_act.astype(jnp.bfloat16).reshape(height, tile_width, channels)

    act = widen(activation, margin)
    stored_acts = [act]
    stored_pre = []
    for layer_index in range(layer_count):
        out_margin = margin - layer_index - 1
        preact = conv_valid(act, kernels[layer_index])
        act = (crop(act, 1).astype(jnp.float32) + jax.nn.silu(preact)).astype(jnp.bfloat16)
        act = jnp.where(lat_mask(act.shape[0], out_margin, height), act, jnp.zeros_like(act))
        stored_pre.append(preact)
        stored_acts.append(act)
    encoded = crop(act, margin - layer_count)

    grad_scale = 1.0 / math.sqrt(cell_count * devices)
    back = cot_wide
    grads = [None] * layer_count
    for layer_index in reversed(range(layer_count)):
        back_margin = layer_index + 1
        preact = crop(stored_pre[layer_index], margin - layer_index - 1 - back_margin)
        sigmoid_v = jax.nn.sigmoid(preact)
        slope = (
            back.astype(jnp.float32) * (sigmoid_v * (1.0 + preact * (1.0 - sigmoid_v)))
        ).astype(jnp.bfloat16)
        slope = jnp.where(lat_mask(slope.shape[0], back_margin, height), slope, jnp.zeros_like(slope))
        slope_flat = crop(slope, back_margin).reshape(cell_count, channels)
        act_in = crop(stored_acts[layer_index], margin - layer_index - 1)
        patches = jnp.concatenate(
            [
                act_in[row_off : row_off + height, col_off : col_off + tile_width]
                for row_off in range(3)
                for col_off in range(3)
            ],
            axis=-1,
        ).reshape(cell_count, 9 * channels)
        tap_grad = lax.dot_general(
            patches, slope_flat, (((0,), (0,)), ((), ())), preferred_element_type=jnp.float32
        )
        flipped = jnp.transpose(kernels[layer_index][::-1, ::-1], (0, 1, 3, 2))
        spread = conv_valid(slope, flipped)
        back = lax.optimization_barrier(
            (crop(back, 1).astype(jnp.float32) + spread).astype(jnp.bfloat16)
        )
        grads[layer_index] = tap_grad
    back_flat = back.reshape(cell_count, channels)
    embed_grad = lax.dot_general(
        features, back_flat, (((0,), (0,)), ((), ())), preferred_element_type=jnp.float32
    )
    cell_grad = (
        lax.dot_general(
            back_flat, w_embed, (((1,), (1,)), ((), ())), preferred_element_type=jnp.float32
        )
        * inv_root[:, None]
    ).astype(jnp.bfloat16)
    picked = jnp.dot(onehot, cell_grad, preferred_element_type=jnp.float32).astype(jnp.bfloat16)

    summed, picked = all_sum(grads + [embed_grad], grad_scale, picked)
    grad_obs = lax.all_to_all(picked, ("lon", "lat"), split_axis=0, concat_axis=0, tiled=True)
    tap_rows_n = kernels.size // channels
    kernel_out = summed[:tap_rows_n].reshape(kernels.shape)
    embed_out = summed[tap_rows_n:]
    return (encoded, kernel_out, embed_out, grad_obs)


def solution(mesh):
    placed = (
        P(("lon", "lat"), None),
        P(("lon", "lat")),
        P(("lon", "lat"), None),
        P(),
        P(),
        P(),
        P("lat", "lon", None),
    )
    return jax.shard_map(
        on_device,
        mesh=mesh,
        in_specs=placed,
        out_specs=(P("lat", "lon", None), P(), P(), P(("lon", "lat"), None)),
        check_vma=False,
    )
```

```python
import math

import jax
import jax.numpy as jnp
from jax import lax
from jax.sharding import PartitionSpec as P

ID_BASE = 128


def shift_pairs(count, step, periodic):
    pairs = []
    for source in range(count):
        target = source + step
        if 0 <= target < count:
            pairs.append((source, target))
        elif periodic:
            pairs.append((source, target % count))
    return pairs


def widen(block, depth):
    lon_count = lax.axis_size("lon")
    lat_count = lax.axis_size("lat")
    west = lax.ppermute(block[:, -depth:], "lon", shift_pairs(lon_count, 1, True))
    east = lax.ppermute(block[:, :depth], "lon", shift_pairs(lon_count, -1, True))
    block = jnp.concatenate([west, block, east], axis=1)
    north = lax.ppermute(block[-depth:], "lat", shift_pairs(lat_count, 1, False))
    south = lax.ppermute(block[:depth], "lat", shift_pairs(lat_count, -1, False))
    return jnp.concatenate([north, block, south], axis=0)


def lat_mask(rows, margin, height):
    lat_index = lax.axis_index("lat")
    lat_count = lax.axis_size("lat")
    global_row = lat_index * height - margin + jnp.arange(rows, dtype=jnp.int32)
    return ((global_row >= 0) & (global_row < lat_count * height))[:, None, None]


def crop(field, margin):
    if margin == 0:
        return field
    return field[margin:-margin, margin:-margin]


def conv_valid(padded, kernel):
    return lax.conv_general_dilated(
        padded[None],
        kernel,
        (1, 1),
        "VALID",
        dimension_numbers=("NHWC", "HWIO", "NHWC"),
        preferred_element_type=jnp.float32,
    )[0]


def cube_steps():
    steps = []
    for axis in ("lon", "lat"):
        count = lax.axis_size(axis)
        bit = 1
        while bit < count:
            steps.append((axis, bit, [(i, i ^ bit) for i in range(count)]))
            bit *= 2
    return steps


def reduce_replicated(part, steps):
    for axis, bit, pairs in steps:
        half = part.shape[0] // 2
        mine = (lax.axis_index(axis) // bit) % 2
        keep = lax.dynamic_slice_in_dim(part, mine * half, half)
        give = lax.dynamic_slice_in_dim(part, (1 - mine) * half, half)
        got = lax.ppermute(give.astype(jnp.bfloat16), axis, pairs)
        part = keep + got.astype(jnp.float32)
    return part


def gather_replicated(part, steps):
    for axis, bit, pairs in reversed(steps):
        mine = (lax.axis_index(axis) // bit) % 2
        got = lax.ppermute(part, axis, pairs)
        first = jnp.where(mine == 0, part, got)
        second = jnp.where(mine == 0, got, part)
        part = jnp.concatenate([first, second])
    return part


def all_sum(pieces, scale, hold, streams=2):
    lanes = pieces[0].shape[-1]
    flat = jnp.concatenate([piece.reshape(-1, lanes) for piece in pieces])
    steps = cube_steps()
    devices = 2 ** len(steps)
    unit = devices * 16
    total = flat.shape[0]
    units = -(-total // unit)
    flat = jnp.pad(flat, ((0, units * unit - total), (0, 0)))
    middle = steps[1:-1] if len(steps) > 2 else []
    orders = []
    parts = []
    begin = 0
    for stream in range(streams):
        count = units // streams + (1 if stream < units % streams else 0)
        if count == 0:
            continue
        shift = (2 * stream) % len(middle) if middle else 0
        order = steps[:1] + middle[shift:] + middle[:shift] + steps[len(middle) + 1 :]
        if len(steps) <= 2:
            order = steps
        parts.append(reduce_replicated(flat[begin : begin + count * unit], order[:1]))
        orders.append(order)
        begin += count * unit
    hold, parts = lax.optimization_barrier((hold, parts))
    outs = []
    for part, order in zip(parts, orders):
        part = reduce_replicated(part, order[1:])
        outs.append(gather_replicated((part * scale).astype(jnp.bfloat16), order))
    return jnp.concatenate(outs)[:total], hold


def on_device(obs_rows, cell_ids, counts, w_embed, w_density, kernels, cotangent):
    lon_count = lax.axis_size("lon")
    lat_count = lax.axis_size("lat")
    devices = lon_count * lat_count
    height, tile_width, channels = cotangent.shape
    cell_count = height * tile_width
    slot_rows = obs_rows.shape[0] // devices
    feat_count = obs_rows.shape[1]
    layer_count = kernels.shape[0]
    margin = 2 * layer_count

    cot_wide = widen(cotangent, layer_count)

    live_mask = jnp.arange(slot_rows, dtype=jnp.int32)[None, :] < counts[0][:, None]
    slot_ids = cell_ids.reshape(devices, slot_rows)
    id_high = jnp.where(live_mask, slot_ids // ID_BASE, -1)
    id_low = jnp.where(live_mask, slot_ids % ID_BASE, -1)
    code = jnp.concatenate([id_high, id_low], axis=1).astype(jnp.bfloat16)
    code_rows = -(-2 * slot_rows // feat_count)
    code_pad = -(-code_rows // 16) * 16
    code = jnp.pad(code, ((0, 0), (0, code_rows * feat_count - 2 * slot_rows)))
    code = code.reshape(devices, code_rows, feat_count)
    code = jnp.pad(code, ((0, 0), (0, code_pad - code_rows), (0, 0)))
    packed = jnp.concatenate([obs_rows.reshape(devices, slot_rows, feat_count), code], axis=1)
    got = lax.all_to_all(packed, ("lon", "lat"), split_axis=0, concat_axis=0, tiled=True)
    got_rows = got[:, :slot_rows].reshape(devices * slot_rows, feat_count)
    got_code = got[:, slot_rows : slot_rows + code_rows].reshape(devices, code_rows * feat_count)
    got_code = got_code.astype(jnp.int32)
    got_ids = (got_code[:, :slot_rows] * ID_BASE + got_code[:, slot_rows : 2 * slot_rows]).reshape(-1)

    cell_iota = jnp.arange(cell_count, dtype=jnp.int32)
    onehot = (got_ids[:, None] == cell_iota[None, :]).astype(jnp.bfloat16)
    cell_sums = lax.dot_general(
        onehot, got_rows, (((0,), (0,)), ((), ())), preferred_element_type=jnp.float32
    )
    density = jnp.sum(onehot.astype(jnp.float32), axis=0)
    inv_root = lax.rsqrt(density + 1.0)
    features = (cell_sums * inv_root[:, None]).astype(jnp.bfloat16)
    start_act = (
        jnp.dot(features, w_embed, preferred_element_type=jnp.float32)
        + jnp.log1p(density)[:, None] * w_density.astype(jnp.float32)[None, :]
    )
    activation = start_act.astype(jnp.bfloat16).reshape(height, tile_width, channels)

    act = widen(activation, margin)
    stored_acts = [act]
    stored_pre = []
    for layer_index in range(layer_count):
        out_margin = margin - layer_index - 1
        preact = conv_valid(act, kernels[layer_index])
        act = (crop(act, 1).astype(jnp.float32) + jax.nn.silu(preact)).astype(jnp.bfloat16)
        act = jnp.where(lat_mask(act.shape[0], out_margin, height), act, jnp.zeros_like(act))
        stored_pre.append(preact)
        stored_acts.append(act)
    encoded = crop(act, margin - layer_count)

    grad_scale = 1.0 / math.sqrt(cell_count * devices)
    back = cot_wide
    grads = [None] * layer_count
    for layer_index in reversed(range(layer_count)):
        back_margin = layer_index + 1
        preact = crop(stored_pre[layer_index], margin - layer_index - 1 - back_margin)
        sigmoid_v = jax.nn.sigmoid(preact)
        slope = (
            back.astype(jnp.float32) * (sigmoid_v * (1.0 + preact * (1.0 - sigmoid_v)))
        ).astype(jnp.bfloat16)
        slope = jnp.where(lat_mask(slope.shape[0], back_margin, height), slope, jnp.zeros_like(slope))
        slope_flat = crop(slope, back_margin).reshape(cell_count, channels)
        act_in = crop(stored_acts[layer_index], margin - layer_index - 1)
        patches = jnp.concatenate(
            [
                act_in[row_off : row_off + height, col_off : col_off + tile_width]
                for row_off in range(3)
                for col_off in range(3)
            ],
            axis=-1,
        ).reshape(cell_count, 9 * channels)
        tap_grad = lax.dot_general(
            patches, slope_flat, (((0,), (0,)), ((), ())), preferred_element_type=jnp.float32
        )
        flipped = jnp.transpose(kernels[layer_index][::-1, ::-1], (0, 1, 3, 2))
        spread = conv_valid(slope, flipped)
        back = lax.optimization_barrier(
            (crop(back, 1).astype(jnp.float32) + spread).astype(jnp.bfloat16)
        )
        grads[layer_index] = tap_grad
    back_flat = back.reshape(cell_count, channels)
    embed_grad = lax.dot_general(
        features, back_flat, (((0,), (0,)), ((), ())), preferred_element_type=jnp.float32
    )
    cell_grad = (
        lax.dot_general(
            back_flat, w_embed, (((1,), (1,)), ((), ())), preferred_element_type=jnp.float32
        )
        * inv_root[:, None]
    ).astype(jnp.bfloat16)
    picked = jnp.dot(onehot, cell_grad, preferred_element_type=jnp.float32).astype(jnp.bfloat16)

    summed, picked = all_sum(grads + [embed_grad], grad_scale, picked)
    grad_obs = lax.all_to_all(picked, ("lon", "lat"), split_axis=0, concat_axis=0, tiled=True)
    tap_rows_n = kernels.size // channels
    kernel_out = summed[:tap_rows_n].reshape(kernels.shape)
    embed_out = summed[tap_rows_n:]
    return (encoded, kernel_out, embed_out, grad_obs)


def solution(mesh):
    placed = (
        P(("lon", "lat"), None),
        P(("lon", "lat")),
        P(("lon", "lat"), None),
        P(),
        P(),
        P(),
        P("lat", "lon", None),
    )
    return jax.shard_map(
        on_device,
        mesh=mesh,
        in_specs=placed,
        out_specs=(P("lat", "lon", None), P(), P(), P(("lon", "lat"), None)),
        check_vma=False,
    )
```

```python
import math

import jax
import jax.numpy as jnp
from jax import lax
from jax.sharding import PartitionSpec as P

ID_BASE = 128


def shift_pairs(count, step, periodic):
    pairs = []
    for source in range(count):
        target = source + step
        if 0 <= target < count:
            pairs.append((source, target))
        elif periodic:
            pairs.append((source, target % count))
    return pairs


def widen(block, depth):
    lon_count = lax.axis_size("lon")
    lat_count = lax.axis_size("lat")
    west = lax.ppermute(block[:, -depth:], "lon", shift_pairs(lon_count, 1, True))
    east = lax.ppermute(block[:, :depth], "lon", shift_pairs(lon_count, -1, True))
    block = jnp.concatenate([west, block, east], axis=1)
    north = lax.ppermute(block[-depth:], "lat", shift_pairs(lat_count, 1, False))
    south = lax.ppermute(block[:depth], "lat", shift_pairs(lat_count, -1, False))
    return jnp.concatenate([north, block, south], axis=0)


def lat_mask(rows, margin, height):
    lat_index = lax.axis_index("lat")
    lat_count = lax.axis_size("lat")
    global_row = lat_index * height - margin + jnp.arange(rows, dtype=jnp.int32)
    return ((global_row >= 0) & (global_row < lat_count * height))[:, None, None]


def crop(field, margin):
    if margin == 0:
        return field
    return field[margin:-margin, margin:-margin]


def conv_valid(padded, kernel):
    return lax.conv_general_dilated(
        padded[None],
        kernel,
        (1, 1),
        "VALID",
        dimension_numbers=("NHWC", "HWIO", "NHWC"),
        preferred_element_type=jnp.float32,
    )[0]


def cube_steps():
    steps = []
    for axis in ("lon", "lat"):
        count = lax.axis_size(axis)
        bit = 1
        while bit < count:
            steps.append((axis, bit, [(i, i ^ bit) for i in range(count)]))
            bit *= 2
    return steps


def reduce_replicated(part, steps):
    for axis, bit, pairs in steps:
        half = part.shape[0] // 2
        mine = (lax.axis_index(axis) // bit) % 2
        keep = lax.dynamic_slice_in_dim(part, mine * half, half)
        give = lax.dynamic_slice_in_dim(part, (1 - mine) * half, half)
        got = lax.ppermute(give.astype(jnp.bfloat16), axis, pairs)
        part = keep + got.astype(jnp.float32)
    return part


def gather_replicated(part, steps):
    for axis, bit, pairs in reversed(steps):
        mine = (lax.axis_index(axis) // bit) % 2
        got = lax.ppermute(part, axis, pairs)
        first = jnp.where(mine == 0, part, got)
        second = jnp.where(mine == 0, got, part)
        part = jnp.concatenate([first, second])
    return part


def all_sum(pieces, scale, hold, streams=2):
    lanes = pieces[0].shape[-1]
    flat = jnp.concatenate([piece.reshape(-1, lanes) for piece in pieces])
    steps = cube_steps()
    devices = 2 ** len(steps)
    unit = devices * 16
    total = flat.shape[0]
    units = -(-total // unit)
    flat = jnp.pad(flat, ((0, units * unit - total), (0, 0)))
    middle = steps[1:-1] if len(steps) > 2 else []
    orders = []
    parts = []
    begin = 0
    for stream in range(streams):
        count = units // streams + (1 if stream < units % streams else 0)
        if count == 0:
            continue
        shift = (stream + 1) % len(middle) if middle else 0
        order = steps[:1] + middle[shift:] + middle[:shift] + steps[len(middle) + 1 :]
        if len(steps) <= 2:
            order = steps
        parts.append(reduce_replicated(flat[begin : begin + count * unit], order[:1]))
        orders.append(order)
        begin += count * unit
    hold, parts = lax.optimization_barrier((hold, parts))
    outs = []
    for part, order in zip(parts, orders):
        part = reduce_replicated(part, order[1:])
        outs.append(gather_replicated((part * scale).astype(jnp.bfloat16), order))
    return jnp.concatenate(outs)[:total], hold


def on_device(obs_rows, cell_ids, counts, w_embed, w_density, kernels, cotangent):
    lon_count = lax.axis_size("lon")
    lat_count = lax.axis_size("lat")
    devices = lon_count * lat_count
    height, tile_width, channels = cotangent.shape
    cell_count = height * tile_width
    slot_rows = obs_rows.shape[0] // devices
    feat_count = obs_rows.shape[1]
    layer_count = kernels.shape[0]
    margin = 2 * layer_count

    cot_wide = widen(cotangent, layer_count)

    live_mask = jnp.arange(slot_rows, dtype=jnp.int32)[None, :] < counts[0][:, None]
    slot_ids = cell_ids.reshape(devices, slot_rows)
    id_high = jnp.where(live_mask, slot_ids // ID_BASE, -1)
    id_low = jnp.where(live_mask, slot_ids % ID_BASE, -1)
    code = jnp.concatenate([id_high, id_low], axis=1).astype(jnp.bfloat16)
    code_rows = -(-2 * slot_rows // feat_count)
    code_pad = -(-code_rows // 16) * 16
    code = jnp.pad(code, ((0, 0), (0, code_rows * feat_count - 2 * slot_rows)))
    code = code.reshape(devices, code_rows, feat_count)
    code = jnp.pad(code, ((0, 0), (0, code_pad - code_rows), (0, 0)))
    packed = jnp.concatenate([obs_rows.reshape(devices, slot_rows, feat_count), code], axis=1)
    got = lax.all_to_all(packed, ("lon", "lat"), split_axis=0, concat_axis=0, tiled=True)
    got_rows = got[:, :slot_rows].reshape(devices * slot_rows, feat_count)
    got_code = got[:, slot_rows : slot_rows + code_rows].reshape(devices, code_rows * feat_count)
    got_code = got_code.astype(jnp.int32)
    got_ids = (got_code[:, :slot_rows] * ID_BASE + got_code[:, slot_rows : 2 * slot_rows]).reshape(-1)

    cell_iota = jnp.arange(cell_count, dtype=jnp.int32)
    onehot = (got_ids[:, None] == cell_iota[None, :]).astype(jnp.bfloat16)
    cell_sums = lax.dot_general(
        onehot, got_rows, (((0,), (0,)), ((), ())), preferred_element_type=jnp.float32
    )
    density = jnp.sum(onehot.astype(jnp.float32), axis=0)
    inv_root = lax.rsqrt(density + 1.0)
    features = (cell_sums * inv_root[:, None]).astype(jnp.bfloat16)
    start_act = (
        jnp.dot(features, w_embed, preferred_element_type=jnp.float32)
        + jnp.log1p(density)[:, None] * w_density.astype(jnp.float32)[None, :]
    )
    activation = start_act.astype(jnp.bfloat16).reshape(height, tile_width, channels)

    act = widen(activation, margin)
    stored_acts = [act]
    stored_pre = []
    for layer_index in range(layer_count):
        out_margin = margin - layer_index - 1
        preact = conv_valid(act, kernels[layer_index])
        act = (crop(act, 1).astype(jnp.float32) + jax.nn.silu(preact)).astype(jnp.bfloat16)
        act = jnp.where(lat_mask(act.shape[0], out_margin, height), act, jnp.zeros_like(act))
        stored_pre.append(preact)
        stored_acts.append(act)
    encoded = crop(act, margin - layer_count)

    grad_scale = 1.0 / math.sqrt(cell_count * devices)
    back = cot_wide
    grads = [None] * layer_count
    for layer_index in reversed(range(layer_count)):
        back_margin = layer_index + 1
        preact = crop(stored_pre[layer_index], margin - layer_index - 1 - back_margin)
        sigmoid_v = jax.nn.sigmoid(preact)
        slope = (
            back.astype(jnp.float32) * (sigmoid_v * (1.0 + preact * (1.0 - sigmoid_v)))
        ).astype(jnp.bfloat16)
        slope = jnp.where(lat_mask(slope.shape[0], back_margin, height), slope, jnp.zeros_like(slope))
        slope_flat = crop(slope, back_margin).reshape(cell_count, channels)
        act_in = crop(stored_acts[layer_index], margin - layer_index - 1)
        patches = jnp.concatenate(
            [
                act_in[row_off : row_off + height, col_off : col_off + tile_width]
                for row_off in range(3)
                for col_off in range(3)
            ],
            axis=-1,
        ).reshape(cell_count, 9 * channels)
        tap_grad = lax.dot_general(
            patches, slope_flat, (((0,), (0,)), ((), ())), preferred_element_type=jnp.float32
        )
        flipped = jnp.transpose(kernels[layer_index][::-1, ::-1], (0, 1, 3, 2))
        spread = conv_valid(slope, flipped)
        back = lax.optimization_barrier(
            (crop(back, 1).astype(jnp.float32) + spread).astype(jnp.bfloat16)
        )
        grads[layer_index] = tap_grad
    back_flat = back.reshape(cell_count, channels)
    embed_grad = lax.dot_general(
        features, back_flat, (((0,), (0,)), ((), ())), preferred_element_type=jnp.float32
    )
    cell_grad = (
        lax.dot_general(
            back_flat, w_embed, (((1,), (1,)), ((), ())), preferred_element_type=jnp.float32
        )
        * inv_root[:, None]
    ).astype(jnp.bfloat16)
    picked = jnp.dot(onehot, cell_grad, preferred_element_type=jnp.float32).astype(jnp.bfloat16)

    summed, picked = all_sum(grads + [embed_grad], grad_scale, picked)
    grad_obs = lax.all_to_all(picked, ("lon", "lat"), split_axis=0, concat_axis=0, tiled=True)
    tap_rows_n = kernels.size // channels
    kernel_out = summed[:tap_rows_n].reshape(kernels.shape)
    embed_out = summed[tap_rows_n:]
    return (encoded, kernel_out, embed_out, grad_obs)


def solution(mesh):
    placed = (
        P(("lon", "lat"), None),
        P(("lon", "lat")),
        P(("lon", "lat"), None),
        P(),
        P(),
        P(),
        P("lat", "lon", None),
    )
    return jax.shard_map(
        on_device,
        mesh=mesh,
        in_specs=placed,
        out_specs=(P("lat", "lon", None), P(), P(), P(("lon", "lat"), None)),
        check_vma=False,
    )
```
